256 devices in a mesh: row: 16 (over z, y_hi), col: 16 (over x, y_lo, core).
Axes of the slice: x: 4, y: 4 (y_hi: 2, y_lo: 2; y = y_hi * 2 + y_lo), z: 8, core: 2. Of those that a mesh axis runs over, the one named last changes fastest.
Arguments:
- features: bfloat16 [512, 512, 256], P('row', 'col'), may hold values from -6 to 6
- dw_kernel: bfloat16 [7, 7, 256], replicated, may hold values from -0.875 to 0.875
- dw_bias: float32 [256], replicated, may hold values from -4 to 4
- norm_gain: float32 [256], replicated, may hold values from 0.5 to 2
- norm_bias: float32 [256], replicated, may hold values from -3 to 3
- w_expand: bfloat16 [256, 1024], replicated, may hold values from -0.375 to 0.375
- b_expand: float32 [1024], replicated, may hold values from -3 to 3
- w_reduce: bfloat16 [1024, 256], replicated, may hold values from -0.1875 to 0.1875
- b_reduce: float32 [256], replicated, may hold values from -3 to 3
- layer_scale: float32 [256], replicated, may hold values from 0.5 to 2
- w_query: bfloat16 [256, 256], replicated, may hold values from -2 to 2
- w_keyval: bfloat16 [256, 512], replicated, may hold values from -0.375 to 0.375
- rel_bias: float32 [8, 7, 127], replicated, may hold values from -8 to 250, as said below
- w_out: bfloat16 [256, 256], replicated, may hold values from -0.75 to 0.75
Outputs:
- result: bfloat16 [512, 512, 256], P('row', 'col')
The draws below stay inside these ranges and needn't reach their ends.
Inputs may be any that keep to these rules, and one draw needn't show every extreme that they name: `rel_bias`: relative position bias of moderate size, with possibly a few much larger entries.
All inputs are finite; a program needn't handle non-finite values.
Results may differ from the reference program's by a relative error of at most 0.014.
Values may be sent and summed in bfloat16 or wider, within the bound.
No kernel may reach another device: no remote copies, remote signals or barrier semaphores. Data moves between devices by JAX's collectives and lax.ppermute only.
A program may use at most 64 MiB of HBM per device.

```python
import math
import jax
import jax.numpy as jnp
from jax import lax

C = 256
FF = 1024
HEADS = 8
TILE = 32
HEIGHT = 512
WIDTH = 512
OFFSET_ROWS = 7
OFFSET_COLS = 127
N_ROW = 16


def draw_rel_bias(key, part):
    shape = (HEADS, OFFSET_ROWS, OFFSET_COLS)
    return jnp.clip(2.0 * jax.random.normal(key, shape, jnp.float32), -8.0, 8.0)


def levels(stream_key, shape, shards, low, top_value):
    def one(axis_at, shards_of):
        heights = jax.random.uniform(jax.random.fold_in(jax.random.fold_in(stream_key, 6), axis_at), (shards_of,), jnp.float32, low / len(shards), top_value / len(shards))
        return jnp.repeat(jnp.exp(heights), shape[axis_at] // shards_of).reshape((-1,) + (1,) * (len(shape) - axis_at - 1))

    level = one(*shards[0])
    for cut in shards[1:]:
        level = level * one(*cut)
    return level


def noise(stream_key, extent, width, most, split=(), held_as=jnp.bfloat16):
    result = jax.random.normal(stream_key, extent, jnp.float32) * width
    if len(split) > 0:
        result = levels(stream_key, extent, split, -0.22, 0.18) * result
    return jnp.clip(result, min=-most, max=most).astype(held_as)


def setup_inputs(seed: int = 0) -> dict:
    keys = jax.random.split(jax.random.key(seed), 15)
    features = noise(keys[0], (HEIGHT, WIDTH, C), 1.0, 6.0, ((0, 16), (1, 16)))
    dw_kernel = noise(keys[1], (7, 7, C), 49 ** -0.5, 0.875)
    dw_bias = noise(keys[2], (C,), 1.0, 4.0, (), jnp.float32)
    norm_gain = jnp.clip(jnp.exp(jax.random.uniform(keys[3], (C,), jnp.float32, math.log(0.5), math.log(2.0))), 0.5, 2.0)
    norm_bias = noise(keys[4], (C,), 0.5, 3.0, (), jnp.float32)
    w_expand = noise(keys[5], (C, FF), C ** -0.5, 0.375)
    b_expand = noise(keys[6], (FF,), 0.5, 3.0, (), jnp.float32)
    w_reduce = noise(keys[7], (FF, C), FF ** -0.5, 0.1875)
    b_reduce = noise(keys[8], (C,), 0.5, 3.0, (), jnp.float32)
    layer_scale = jnp.clip(jnp.exp(jax.random.uniform(keys[9], (C,), jnp.float32, math.log(0.5), math.log(2.0))), 0.5, 2.0)
    w_query = noise(keys[10], (C, C), (max(C // 32, 1)) ** -0.5, 2.0)
    w_keyval = noise(keys[11], (C, 2 * C), C ** -0.5, 0.375)
    rel_bias = draw_rel_bias(jax.random.fold_in(keys[14], 71), 0)
    w_out = noise(keys[13], (C, C), (C // 4) ** -0.5, 0.75)
    return dict(features=features, dw_kernel=dw_kernel, dw_bias=dw_bias, norm_gain=norm_gain, norm_bias=norm_bias, w_expand=w_expand, b_expand=b_expand, w_reduce=w_reduce, b_reduce=b_reduce, layer_scale=layer_scale, w_query=w_query, w_keyval=w_keyval, rel_bias=rel_bias, w_out=w_out)


def block_pass(padded, features, dw_kernel, dw_bias, norm_gain, norm_bias, w_expand, b_expand, w_reduce, b_reduce, layer_scale):
    tile_rows, tile_cols, channels = features.shape
    convolved = jnp.zeros((tile_rows, tile_cols, channels), jnp.float32)
    for tap_row in range(7):
        for tap_col in range(7):
            convolved = convolved + padded[tap_row:tap_row + tile_rows, tap_col:tap_col + tile_cols].astype(jnp.float32) * dw_kernel[tap_row, tap_col].astype(jnp.float32)
    convolved = convolved + dw_bias
    average = lax.optimization_barrier(jnp.mean(convolved, axis=-1, keepdims=True))
    centred = convolved - average
    variance = lax.optimization_barrier(jnp.mean(centred * centred, axis=-1, keepdims=True))
    normed = (centred * lax.rsqrt(variance + 1e-06) * norm_gain + norm_bias).astype(jnp.bfloat16).reshape(-1, channels)
    hidden = jax.nn.gelu(jnp.dot(normed, w_expand, preferred_element_type=jnp.float32) + b_expand, approximate=False).astype(jnp.bfloat16)
    reduced = jnp.dot(hidden, w_reduce, preferred_element_type=jnp.float32) + b_reduce
    summed = features.astype(jnp.float32).reshape(-1, channels) + layer_scale * reduced
    return summed.astype(jnp.bfloat16).reshape(tile_rows, tile_cols, channels)

def reference(features, dw_kernel, dw_bias, norm_gain, norm_bias, w_expand, b_expand, w_reduce, b_reduce, layer_scale, w_query, w_keyval, rel_bias, w_out):
    map_width = features.shape[1]
    channels = features.shape[2]
    region_rows = TILE // 8
    region_cols = map_width // 8
    token_count = region_rows * region_cols
    head_dim = channels // HEADS
    padded = jnp.pad(features, ((3, 3), (3, 3), (0, 0)))
    token_index = jnp.arange(token_count, dtype=jnp.int32)
    token_row = token_index // region_cols
    token_col = token_index % region_cols
    offset_rows = token_row[None, :] - token_row[:, None] + region_rows - 1
    offset_cols = token_col[None, :] - token_col[:, None] + region_cols - 1
    bias_full = rel_bias[:, offset_rows, offset_cols]

    def strip_pass(strip_index):
        band = lax.dynamic_slice_in_dim(padded, strip_index * TILE, TILE + 6, 0)
        centre = band[3:3 + TILE, 3:3 + map_width]
        block_out = block_pass(band, centre, dw_kernel, dw_bias, norm_gain, norm_bias, w_expand, b_expand, w_reduce, b_reduce, layer_scale)
        pooled = block_out.astype(jnp.float32).reshape(region_rows, 8, region_cols, 8, channels).mean(axis=(1, 3))
        pooled = pooled.astype(jnp.bfloat16).reshape(token_count, channels)
        queries = jnp.dot(pooled, w_query, preferred_element_type=jnp.float32).astype(jnp.bfloat16)
        keyval = jnp.dot(pooled, w_keyval, preferred_element_type=jnp.float32).astype(jnp.bfloat16)
        query_heads = queries.astype(jnp.float32).reshape(token_count, HEADS, head_dim)
        key_heads = keyval[:, :channels].astype(jnp.float32).reshape(token_count, HEADS, head_dim)
        value_heads = keyval[:, channels:].astype(jnp.float32).reshape(token_count, HEADS, head_dim)
        scores = jnp.einsum('qhd,khd->hqk', query_heads, key_heads) / jnp.sqrt(jnp.float32(head_dim)) + bias_full
        attn = jax.nn.softmax(scores, axis=-1).astype(jnp.bfloat16)
        context = jnp.einsum('hqk,khd->qhd', attn.astype(jnp.float32), value_heads).reshape(token_count, channels).astype(jnp.bfloat16)
        lifted = jnp.dot(context, w_out, preferred_element_type=jnp.float32).reshape(region_rows, 1, region_cols, 1, channels)
        spread = jnp.broadcast_to(lifted, (region_rows, 8, region_cols, 8, channels)).reshape(TILE, map_width, channels)
        return (block_out.astype(jnp.float32) + spread).astype(jnp.bfloat16)
    bands = lax.map(strip_pass, jnp.arange(N_ROW, dtype=jnp.int32))
    return bands.reshape(N_ROW * TILE, map_width, channels)
```

```python
import jax
import jax.numpy as jnp
from jax import lax
from jax.sharding import PartitionSpec as P

HEADS = 8


def padded_2(array, sides, width):
    for axis, dim in sides:
        devices, length = (lax.axis_size(axis), array.shape[dim])
        up = [(i, (i + 1) % devices) for i in range(devices - 1)]
        down = [(j, i) for i, j in up]
        last = lax.slice_in_dim(array, length - width, length, axis=dim)
        leading = lax.slice_in_dim(array, 0, width, axis=dim)
        before = lax.ppermute(last, axis, up)
        after = lax.ppermute(leading, axis, down)
        array = jnp.concatenate([before, array, after], axis=dim)
    return array


def block_pass(
    padded,
    features,
    dw_kernel,
    dw_bias,
    norm_gain,
    norm_bias,
    w_expand,
    b_expand,
    w_reduce,
    b_reduce,
    layer_scale,
):
    tile_rows, tile_cols, channels = features.shape
    convolved = jnp.zeros((tile_rows, tile_cols, channels), jnp.float32)
    for tap_row in range(7):
        for tap_col in range(7):
            convolved = convolved + padded[
                tap_row : tap_row + tile_rows, tap_col : tap_col + tile_cols
            ].astype(jnp.float32) * dw_kernel[tap_row, tap_col].astype(jnp.float32)
    convolved = convolved + dw_bias
    average = jnp.mean(convolved, axis=-1, keepdims=True)
    centred = convolved - average
    variance = jnp.mean(centred * centred, axis=-1, keepdims=True)
    normed = (
        (centred * lax.rsqrt(variance + 1e-06) * norm_gain + norm_bias)
        .astype(jnp.bfloat16)
        .reshape(-1, channels)
    )
    hidden = jax.nn.gelu(
        jnp.dot(normed, w_expand, preferred_element_type=jnp.float32) + b_expand, approximate=False
    ).astype(jnp.bfloat16)
    reduced = jnp.dot(hidden, w_reduce, preferred_element_type=jnp.float32) + b_reduce
    summed = features.astype(jnp.float32).reshape(-1, channels) + layer_scale * reduced
    return summed.astype(jnp.bfloat16).reshape(tile_rows, tile_cols, channels)


def shards(
    features,
    dw_kernel,
    dw_bias,
    norm_gain,
    norm_bias,
    w_expand,
    b_expand,
    w_reduce,
    b_reduce,
    layer_scale,
    w_query,
    w_keyval,
    rel_bias,
    w_out,
):
    tile_rows, tile_cols, channels = features.shape
    head_dim = channels // HEADS
    extended = padded_2(features, (("row", 0),), 3)
    padded = padded_2(extended, (("col", 1),), 3)
    block_out = block_pass(
        padded,
        features,
        dw_kernel,
        dw_bias,
        norm_gain,
        norm_bias,
        w_expand,
        b_expand,
        w_reduce,
        b_reduce,
        layer_scale,
    )
    region_side = tile_rows // 8
    local_count = region_side * region_side
    pooled = (
        block_out.astype(jnp.float32)
        .reshape(region_side, 8, region_side, 8, channels)
        .mean(axis=(1, 3))
    )
    pooled = pooled.astype(jnp.bfloat16).reshape(local_count, channels)
    queries = jnp.dot(pooled, w_query, preferred_element_type=jnp.float32).astype(jnp.bfloat16)
    columns = lax.axis_size("col")
    position = lax.axis_index("col")
    span_cols = region_side * columns
    key_count = local_count * columns
    sent = jnp.broadcast_to(pooled[None], (columns, local_count, channels)).reshape(
        columns * local_count, channels
    )
    band_pooled = lax.all_to_all(sent, "col", 0, 0, tiled=True)
    band_pooled = (
        band_pooled.reshape(columns, region_side, region_side, channels)
        .transpose(1, 0, 2, 3)
        .reshape(key_count, channels)
    )
    band_keyval = jnp.dot(band_pooled, w_keyval, preferred_element_type=jnp.float32).astype(
        jnp.bfloat16
    )
    windows = []
    for query_col in range(region_side):
        first = span_cols - 1 - (position * region_side + query_col)
        windows.append(lax.dynamic_slice_in_dim(rel_bias, first, span_cols, axis=2))
    rows_of = []
    for query_row in range(region_side):
        per_col = [
            w[:, region_side - 1 - query_row : 2 * region_side - 1 - query_row, :] for w in windows
        ]
        rows_of.append(jnp.stack(per_col, axis=1))
    bias_block = jnp.stack(rows_of, axis=1).reshape(HEADS, local_count, key_count)
    query_heads = queries.reshape(local_count, HEADS, head_dim)
    key_heads = band_keyval[:, :channels].reshape(key_count, HEADS, head_dim)
    value_heads = band_keyval[:, channels:].reshape(key_count, HEADS, head_dim)
    scores = (
        jnp.einsum("qhd,khd->hqk", query_heads, key_heads, preferred_element_type=jnp.float32)
        / jnp.sqrt(jnp.float32(head_dim))
        + bias_block
    )
    attn = jax.nn.softmax(scores, axis=-1).astype(jnp.bfloat16)
    context = (
        jnp.einsum("hqk,khd->qhd", attn, value_heads, preferred_element_type=jnp.float32)
        .reshape(local_count, channels)
        .astype(jnp.bfloat16)
    )
    lifted = jnp.dot(context, w_out, preferred_element_type=jnp.float32).reshape(
        region_side, 1, region_side, 1, channels
    )
    spread = jnp.broadcast_to(lifted, (region_side, 8, region_side, 8, channels)).reshape(
        tile_rows, tile_cols, channels
    )
    return (block_out.astype(jnp.float32) + spread).astype(jnp.bfloat16)


def solution(mesh):
    return jax.shard_map(
        shards,
        mesh=mesh,
        in_specs=(
            P("row", "col", None),
            P(),
            P(),
            P(),
            P(),
            P(),
            P(),
            P(),
            P(),
            P(),
            P(),
            P(),
            P(),
            P(),
        ),
        out_specs=P("row", "col", None),
        check_vma=False,
    )
```

```python
import jax
import jax.numpy as jnp
from jax import lax
from jax.sharding import PartitionSpec as P
from jax.experimental import pallas as pl
from jax.experimental.pallas import tpu as pltpu

HEADS = 8


def padded_2(array, sides, width):
    for axis, dim in sides:
        devices, length = (lax.axis_size(axis), array.shape[dim])
        up = [(i, (i + 1) % devices) for i in range(devices - 1)]
        down = [(j, i) for i, j in up]
        last = lax.slice_in_dim(array, length - width, length, axis=dim)
        leading = lax.slice_in_dim(array, 0, width, axis=dim)
        before = lax.ppermute(last, axis, up)
        after = lax.ppermute(leading, axis, down)
        array = jnp.concatenate([before, array, after], axis=dim)
    return array


TAPS = 7
ROW_BLOCK = 2


def conv_norm_kernel(x_ref, k_ref, db_ref, g_ref, nb_ref, o_ref, xf_ref, sh_ref):
    rows_p = x_ref.shape[0]
    tile_rows, tile_cols, channels = o_ref.shape

    def widen(r, carry):
        xf_ref[r] = x_ref[r].astype(jnp.float32)
        for b in range(TAPS):
            sh_ref[b, r] = xf_ref[r, pl.ds(b, tile_cols), :]
        return carry

    lax.fori_loop(0, rows_p, widen, 0)
    db = db_ref[...]
    g = g_ref[...]
    nb = nb_ref[...]

    def body(i, carry):
        r0 = pl.multiple_of(i * ROW_BLOCK, ROW_BLOCK)
        acc = jnp.zeros((ROW_BLOCK, tile_cols, channels), jnp.float32)
        for a in range(TAPS):
            for b in range(TAPS):
                acc = acc + sh_ref[b, pl.ds(r0 + a, ROW_BLOCK)] * k_ref[pl.ds(a * TAPS + b, 1), :]
        acc = acc + db
        mean = jnp.mean(acc, axis=-1, keepdims=True)
        cen = acc - mean
        var = jnp.mean(cen * cen, axis=-1, keepdims=True)
        o_ref[pl.ds(r0, ROW_BLOCK)] = (cen * lax.rsqrt(var + 1e-06) * g + nb).astype(o_ref.dtype)
        return carry

    lax.fori_loop(0, tile_rows // ROW_BLOCK, body, 0)


def conv_norm(padded, dw_kernel, dw_bias, norm_gain, norm_bias, tile_rows, tile_cols):
    rows_p, cols_p, channels = padded.shape
    vmem = pl.BlockSpec(memory_space=pltpu.VMEM)
    return pl.pallas_call(
        conv_norm_kernel,
        out_shape=jax.ShapeDtypeStruct((tile_rows, tile_cols, channels), jnp.bfloat16),
        in_specs=[vmem] * 5,
        out_specs=vmem,
        scratch_shapes=[
            pltpu.VMEM((rows_p, cols_p, channels), jnp.float32),
            pltpu.VMEM((TAPS, rows_p, tile_cols, channels), jnp.float32),
        ],
        cost_estimate=pl.CostEstimate(
            flops=2 * TAPS * TAPS * tile_rows * tile_cols * channels,
            bytes_accessed=2 * (rows_p * cols_p + tile_rows * tile_cols) * channels,
            transcendentals=tile_rows * tile_cols,
        ),
    )(
        padded,
        dw_kernel.astype(jnp.float32).reshape(TAPS * TAPS, channels),
        dw_bias.reshape(1, channels),
        norm_gain.reshape(1, channels),
        norm_bias.reshape(1, channels),
    )


def block_pass(
    padded,
    features,
    dw_kernel,
    dw_bias,
    norm_gain,
    norm_bias,
    w_expand,
    b_expand,
    w_reduce,
    b_reduce,
    layer_scale,
):
    tile_rows, tile_cols, channels = features.shape
    padded = jnp.pad(padded, ((0, 0), (0, 8 - padded.shape[1] % 8), (0, 0)))
    normed = conv_norm(
        padded, dw_kernel, dw_bias, norm_gain, norm_bias, tile_rows, tile_cols
    ).reshape(-1, channels)
    hidden = jax.nn.gelu(
        jnp.dot(normed, w_expand, preferred_element_type=jnp.float32) + b_expand, approximate=False
    ).astype(jnp.bfloat16)
    reduced = jnp.dot(hidden, w_reduce, preferred_element_type=jnp.float32) + b_reduce
    summed = features.astype(jnp.float32).reshape(-1, channels) + layer_scale * reduced
    return summed.astype(jnp.bfloat16).reshape(tile_rows, tile_cols, channels)


def shards(
    features,
    dw_kernel,
    dw_bias,
    norm_gain,
    norm_bias,
    w_expand,
    b_expand,
    w_reduce,
    b_reduce,
    layer_scale,
    w_query,
    w_keyval,
    rel_bias,
    w_out,
):
    tile_rows, tile_cols, channels = features.shape
    head_dim = channels // HEADS
    extended = padded_2(features, (("row", 0),), 3)
    padded = padded_2(extended, (("col", 1),), 3)
    block_out = block_pass(
        padded,
        features,
        dw_kernel,
        dw_bias,
        norm_gain,
        norm_bias,
        w_expand,
        b_expand,
        w_reduce,
        b_reduce,
        layer_scale,
    )
    region_side = tile_rows // 8
    local_count = region_side * region_side
    pooled = (
        block_out.astype(jnp.float32)
        .reshape(region_side, 8, region_side, 8, channels)
        .mean(axis=(1, 3))
    )
    pooled = pooled.astype(jnp.bfloat16).reshape(local_count, channels)
    queries = jnp.dot(pooled, w_query, preferred_element_type=jnp.float32).astype(jnp.bfloat16)
    columns = lax.axis_size("col")
    position = lax.axis_index("col")
    span_cols = region_side * columns
    key_count = local_count * columns
    sent = jnp.broadcast_to(pooled[None], (columns, local_count, channels)).reshape(
        columns * local_count, channels
    )
    band_pooled = lax.all_to_all(sent, "col", 0, 0, tiled=True)
    band_pooled = (
        band_pooled.reshape(columns, region_side, region_side, channels)
        .transpose(1, 0, 2, 3)
        .reshape(key_count, channels)
    )
    band_keyval = jnp.dot(band_pooled, w_keyval, preferred_element_type=jnp.float32).astype(
        jnp.bfloat16
    )
    windows = []
    for query_col in range(region_side):
        first = span_cols - 1 - (position * region_side + query_col)
        windows.append(lax.dynamic_slice_in_dim(rel_bias, first, span_cols, axis=2))
    rows_of = []
    for query_row in range(region_side):
        per_col = [
            w[:, region_side - 1 - query_row : 2 * region_side - 1 - query_row, :] for w in windows
        ]
        rows_of.append(jnp.stack(per_col, axis=1))
    bias_block = jnp.stack(rows_of, axis=1).reshape(HEADS, local_count, key_count)
    query_heads = queries.reshape(local_count, HEADS, head_dim)
    key_heads = band_keyval[:, :channels].reshape(key_count, HEADS, head_dim)
    value_heads = band_keyval[:, channels:].reshape(key_count, HEADS, head_dim)
    scores = (
        jnp.einsum("qhd,khd->hqk", query_heads, key_heads, preferred_element_type=jnp.float32)
        / jnp.sqrt(jnp.float32(head_dim))
        + bias_block
    )
    attn = jax.nn.softmax(scores, axis=-1).astype(jnp.bfloat16)
    context = (
        jnp.einsum("hqk,khd->qhd", attn, value_heads, preferred_element_type=jnp.float32)
        .reshape(local_count, channels)
        .astype(jnp.bfloat16)
    )
    lifted = jnp.dot(context, w_out, preferred_element_type=jnp.float32).reshape(
        region_side, 1, region_side, 1, channels
    )
    spread = jnp.broadcast_to(lifted, (region_side, 8, region_side, 8, channels)).reshape(
        tile_rows, tile_cols, channels
    )
    return (block_out.astype(jnp.float32) + spread).astype(jnp.bfloat16)


def solution(mesh):
    return jax.shard_map(
        shards,
        mesh=mesh,
        in_specs=(
            P("row", "col", None),
            P(),
            P(),
            P(),
            P(),
            P(),
            P(),
            P(),
            P(),
            P(),
            P(),
            P(),
            P(),
            P(),
        ),
        out_specs=P("row", "col", None),
        check_vma=False,
    )
```

```python
import jax
import jax.numpy as jnp
from jax import lax
from jax.sharding import PartitionSpec as P
from jax.experimental import pallas as pl
from jax.experimental.pallas import tpu as pltpu

HEADS = 8


def padded_2(array, sides, width):
    for axis, dim in sides:
        devices, length = (lax.axis_size(axis), array.shape[dim])
        up = [(i, (i + 1) % devices) for i in range(devices - 1)]
        down = [(j, i) for i, j in up]
        last = lax.slice_in_dim(array, length - width, length, axis=dim)
        leading = lax.slice_in_dim(array, 0, width, axis=dim)
        before = lax.ppermute(last, axis, up)
        after = lax.ppermute(leading, axis, down)
        array = jnp.concatenate([before, array, after], axis=dim)
    return array


TAPS = 7
ROW_BLOCK = 2


def conv_norm_kernel(x_ref, k_ref, db_ref, g_ref, nb_ref, o_ref, xf_ref, sh_ref):
    rows_p = x_ref.shape[0]
    tile_rows, tile_cols, channels = o_ref.shape

    def widen(r, carry):
        xf_ref[r] = x_ref[r].astype(jnp.float32)
        for b in range(TAPS):
            sh_ref[b, r] = xf_ref[r, pl.ds(b, tile_cols), :]
        return carry

    lax.fori_loop(0, rows_p, widen, 0)
    db = db_ref[...]
    g = g_ref[...]
    nb = nb_ref[...]

    def body(i, carry):
        r0 = pl.multiple_of(i * ROW_BLOCK, ROW_BLOCK)
        acc = jnp.zeros((ROW_BLOCK, tile_cols, channels), jnp.float32)
        for a in range(TAPS):
            for b in range(TAPS):
                acc = acc + sh_ref[b, pl.ds(r0 + a, ROW_BLOCK)] * k_ref[pl.ds(a * TAPS + b, 1), :]
        acc = acc + db
        mean = jnp.mean(acc, axis=-1, keepdims=True)
        cen = acc - mean
        var = jnp.mean(cen * cen, axis=-1, keepdims=True)
        o_ref[pl.ds(r0, ROW_BLOCK)] = (cen * lax.rsqrt(var + 1e-06) * g + nb).astype(o_ref.dtype)
        return carry

    lax.fori_loop(0, tile_rows // ROW_BLOCK, body, 0)


def conv_norm(padded, dw_kernel, dw_bias, norm_gain, norm_bias, tile_rows, tile_cols):
    rows_p, cols_p, channels = padded.shape
    vmem = pl.BlockSpec(memory_space=pltpu.VMEM)
    return pl.pallas_call(
        conv_norm_kernel,
        out_shape=jax.ShapeDtypeStruct((tile_rows, tile_cols, channels), jnp.bfloat16),
        in_specs=[vmem] * 5,
        out_specs=vmem,
        scratch_shapes=[
            pltpu.VMEM((rows_p, cols_p, channels), jnp.float32),
            pltpu.VMEM((TAPS, rows_p, tile_cols, channels), jnp.float32),
        ],
        cost_estimate=pl.CostEstimate(
            flops=2 * TAPS * TAPS * tile_rows * tile_cols * channels,
            bytes_accessed=2 * (rows_p * cols_p + tile_rows * tile_cols) * channels,
            transcendentals=tile_rows * tile_cols,
        ),
    )(
        padded,
        dw_kernel.astype(jnp.float32).reshape(TAPS * TAPS, channels),
        dw_bias.reshape(1, channels),
        norm_gain.reshape(1, channels),
        norm_bias.reshape(1, channels),
    )


def block_pass(
    padded,
    features,
    dw_kernel,
    dw_bias,
    norm_gain,
    norm_bias,
    w_expand,
    b_expand,
    w_reduce,
    b_reduce,
    layer_scale,
):
    tile_rows, tile_cols, channels = features.shape
    padded = jnp.pad(padded, ((0, 0), (0, 8 - padded.shape[1] % 8), (0, 0)))
    normed = conv_norm(
        padded, dw_kernel, dw_bias, norm_gain, norm_bias, tile_rows, tile_cols
    ).reshape(-1, channels)
    hidden = jax.nn.gelu(
        jnp.dot(normed, w_expand, preferred_element_type=jnp.float32) + b_expand, approximate=False
    ).astype(jnp.bfloat16)
    reduced = jnp.dot(hidden, w_reduce, preferred_element_type=jnp.float32) + b_reduce
    summed = features.astype(jnp.float32).reshape(-1, channels) + layer_scale * reduced
    return summed.astype(jnp.bfloat16).reshape(tile_rows, tile_cols, channels)


def shards(
    features,
    dw_kernel,
    dw_bias,
    norm_gain,
    norm_bias,
    w_expand,
    b_expand,
    w_reduce,
    b_reduce,
    layer_scale,
    w_query,
    w_keyval,
    rel_bias,
    w_out,
):
    tile_rows, tile_cols, channels = features.shape
    head_dim = channels // HEADS
    extended = padded_2(features, (("row", 0),), 3)
    padded = padded_2(extended, (("col", 1),), 3)
    block_out = block_pass(
        padded,
        features,
        dw_kernel,
        dw_bias,
        norm_gain,
        norm_bias,
        w_expand,
        b_expand,
        w_reduce,
        b_reduce,
        layer_scale,
    )
    region_side = tile_rows // 8
    local_count = region_side * region_side
    pooled = (
        block_out.astype(jnp.float32)
        .reshape(region_side, 8, region_side, 8, channels)
        .mean(axis=(1, 3))
    )
    pooled = pooled.astype(jnp.bfloat16).reshape(local_count, channels)
    queries = jnp.dot(pooled, w_query, preferred_element_type=jnp.float32).astype(jnp.bfloat16)
    columns = lax.axis_size("col")
    position = lax.axis_index("col")
    span_cols = region_side * columns
    key_count = local_count * columns
    block = pooled[None]
    bits = []
    distance = columns // 2
    while distance >= 1:
        pairs = [(i, i ^ distance) for i in range(columns)]
        theirs = lax.ppermute(block, "col", pairs)
        upper = (position & distance) != 0
        block = jnp.where(
            upper,
            jnp.concatenate([theirs, block], axis=0),
            jnp.concatenate([block, theirs], axis=0),
        )
        bits.append(distance)
        distance //= 2
    steps = len(bits)
    band_pooled = block.reshape((2,) * steps + (region_side, region_side, channels))
    order = (steps,) + tuple(range(steps - 1, -1, -1)) + (steps + 1, steps + 2)
    band_pooled = band_pooled.transpose(order).reshape(key_count, channels)
    band_keyval = jnp.dot(band_pooled, w_keyval, preferred_element_type=jnp.float32).astype(
        jnp.bfloat16
    )
    window_all = lax.dynamic_slice_in_dim(
        rel_bias, span_cols - region_side - position * region_side, span_cols + region_side - 1, axis=2
    )
    windows = [
        window_all[:, :, region_side - 1 - query_col : region_side - 1 - query_col + span_cols]
        for query_col in range(region_side)
    ]
    rows_of = []
    for query_row in range(region_side):
        per_col = [
            w[:, region_side - 1 - query_row : 2 * region_side - 1 - query_row, :] for w in windows
        ]
        rows_of.append(jnp.stack(per_col, axis=1))
    bias_block = jnp.stack(rows_of, axis=1).reshape(HEADS, local_count, key_count)
    query_heads = queries.reshape(local_count, HEADS, head_dim)
    key_heads = band_keyval[:, :channels].reshape(key_count, HEADS, head_dim)
    value_heads = band_keyval[:, channels:].reshape(key_count, HEADS, head_dim)
    scores = (
        jnp.einsum("qhd,khd->hqk", query_heads, key_heads, preferred_element_type=jnp.float32)
        / jnp.sqrt(jnp.float32(head_dim))
        + bias_block
    )
    attn = jax.nn.softmax(scores, axis=-1).astype(jnp.bfloat16)
    context = (
        jnp.einsum("hqk,khd->qhd", attn, value_heads, preferred_element_type=jnp.float32)
        .reshape(local_count, channels)
        .astype(jnp.bfloat16)
    )
    lifted = jnp.dot(context, w_out, preferred_element_type=jnp.float32).reshape(
        region_side, 1, region_side, 1, channels
    )
    spread = jnp.broadcast_to(lifted, (region_side, 8, region_side, 8, channels)).reshape(
        tile_rows, tile_cols, channels
    )
    return (block_out.astype(jnp.float32) + spread).astype(jnp.bfloat16)


def solution(mesh):
    return jax.shard_map(
        shards,
        mesh=mesh,
        in_specs=(
            P("row", "col", None),
            P(),
            P(),
            P(),
            P(),
            P(),
            P(),
            P(),
            P(),
            P(),
            P(),
            P(),
            P(),
            P(),
        ),
        out_specs=P("row", "col", None),
        check_vma=False,
    )
```

```python
import jax
import jax.numpy as jnp
from jax import lax
from jax.sharding import PartitionSpec as P
from jax.experimental import pallas as pl
from jax.experimental.pallas import tpu as pltpu

HEADS = 8


def padded_2(array, sides, width):
    for axis, dim in sides:
        devices, length = (lax.axis_size(axis), array.shape[dim])
        up = [(i, (i + 1) % devices) for i in range(devices - 1)]
        down = [(j, i) for i, j in up]
        last = lax.slice_in_dim(array, length - width, length, axis=dim)
        leading = lax.slice_in_dim(array, 0, width, axis=dim)
        before = lax.ppermute(last, axis, up)
        after = lax.ppermute(leading, axis, down)
        array = jnp.concatenate([before, array, after], axis=dim)
    return array


TAPS = 7
ROW_BLOCK = 2


def conv_norm_kernel(x_ref, k_ref, db_ref, g_ref, nb_ref, o_ref, xf_ref, sh_ref):
    rows_p = x_ref.shape[0]
    tile_rows, tile_cols, channels = o_ref.shape

    def widen(r, carry):
        xf_ref[r] = x_ref[r].astype(jnp.float32)
        for b in range(TAPS):
            sh_ref[b, r] = xf_ref[r, pl.ds(b, tile_cols), :]
        return carry

    lax.fori_loop(0, rows_p, widen, 0)
    db = db_ref[...]
    g = g_ref[...]
    nb = nb_ref[...]

    def body(i, carry):
        r0 = pl.multiple_of(i * ROW_BLOCK, ROW_BLOCK)
        acc = jnp.zeros((ROW_BLOCK, tile_cols, channels), jnp.float32)
        for a in range(TAPS):
            for b in range(TAPS):
                acc = acc + sh_ref[b, pl.ds(r0 + a, ROW_BLOCK)] * k_ref[pl.ds(a * TAPS + b, 1), :]
        acc = acc + db
        mean = jnp.mean(acc, axis=-1, keepdims=True)
        cen = acc - mean
        var = jnp.mean(cen * cen, axis=-1, keepdims=True)
        o_ref[pl.ds(r0, ROW_BLOCK)] = (cen * lax.rsqrt(var + 1e-06) * g + nb).astype(o_ref.dtype)
        return carry

    lax.fori_loop(0, tile_rows // ROW_BLOCK, body, 0)


def conv_norm(padded, dw_kernel, dw_bias, norm_gain, norm_bias, tile_rows, tile_cols):
    rows_p, cols_p, channels = padded.shape
    vmem = pl.BlockSpec(memory_space=pltpu.VMEM)
    return pl.pallas_call(
        conv_norm_kernel,
        out_shape=jax.ShapeDtypeStruct((tile_rows, tile_cols, channels), jnp.bfloat16),
        in_specs=[vmem] * 5,
        out_specs=vmem,
        scratch_shapes=[
            pltpu.VMEM((rows_p, cols_p, channels), jnp.float32),
            pltpu.VMEM((TAPS, rows_p, tile_cols, channels), jnp.float32),
        ],
        cost_estimate=pl.CostEstimate(
            flops=2 * TAPS * TAPS * tile_rows * tile_cols * channels,
            bytes_accessed=2 * (rows_p * cols_p + tile_rows * tile_cols) * channels,
            transcendentals=tile_rows * tile_cols,
        ),
    )(
        padded,
        dw_kernel.astype(jnp.float32).reshape(TAPS * TAPS, channels),
        dw_bias.reshape(1, channels),
        norm_gain.reshape(1, channels),
        norm_bias.reshape(1, channels),
    )


ERFC_COEFFS = (
    -1.26551223,
    1.00002368,
    0.37409196,
    0.09678418,
    -0.18628806,
    0.27886807,
    -1.13520398,
    1.48851587,
    -0.82215223,
    0.17087277,
)
PIXEL_BLOCK = 256
HIDDEN_BLOCK = 256


def gelu_exact(pre):
    z = jnp.abs(pre) * jnp.float32(0.7071067811865476)
    t = 1.0 / (1.0 + 0.5 * z)
    poly = jnp.float32(ERFC_COEFFS[-1])
    for coeff in ERFC_COEFFS[-2::-1]:
        poly = poly * t + jnp.float32(coeff)
    tail = t * jnp.exp(poly - z * z)
    one_plus_erf = jnp.where(pre >= 0, 2.0 - tail, tail)
    return 0.5 * pre * one_plus_erf


def mlp_kernel(n_ref, f_ref, we_ref, be_ref, wr_ref, br_ref, ls_ref, o_ref):
    normed = n_ref[...]
    hidden_total = we_ref.shape[1]
    acc = jnp.zeros(o_ref.shape, jnp.float32)
    for h0 in range(0, hidden_total, HIDDEN_BLOCK):
        pre = (
            jnp.dot(normed, we_ref[:, h0 : h0 + HIDDEN_BLOCK], preferred_element_type=jnp.float32)
            + be_ref[:, h0 : h0 + HIDDEN_BLOCK]
        )
        hidden = gelu_exact(pre).astype(jnp.bfloat16)
        acc = acc + jnp.dot(hidden, wr_ref[h0 : h0 + HIDDEN_BLOCK, :], preferred_element_type=jnp.float32)
    reduced = acc + br_ref[...]
    o_ref[...] = (f_ref[...].astype(jnp.float32) + ls_ref[...] * reduced).astype(o_ref.dtype)


def mlp(normed, features, w_expand, b_expand, w_reduce, b_reduce, layer_scale):
    pixels, channels = normed.shape
    hidden_total = w_expand.shape[1]
    rows = pl.BlockSpec((PIXEL_BLOCK, channels), lambda i: (i, 0))
    whole = lambda shape: pl.BlockSpec(shape, lambda i: (0, 0))
    return pl.pallas_call(
        mlp_kernel,
        out_shape=jax.ShapeDtypeStruct((pixels, channels), jnp.bfloat16),
        grid=(pixels // PIXEL_BLOCK,),
        in_specs=[
            rows,
            rows,
            whole((channels, hidden_total)),
            whole((1, hidden_total)),
            whole((hidden_total, channels)),
            whole((1, channels)),
            whole((1, channels)),
        ],
        out_specs=rows,
        cost_estimate=pl.CostEstimate(
            flops=4 * pixels * channels * hidden_total,
            bytes_accessed=2 * (3 * pixels * channels + 2 * channels * hidden_total),
            transcendentals=2 * pixels * hidden_total,
        ),
    )(
        normed,
        features,
        w_expand,
        b_expand.reshape(1, hidden_total),
        w_reduce,
        b_reduce.reshape(1, channels),
        layer_scale.reshape(1, channels),
    )


def block_pass(
    padded,
    features,
    dw_kernel,
    dw_bias,
    norm_gain,
    norm_bias,
    w_expand,
    b_expand,
    w_reduce,
    b_reduce,
    layer_scale,
):
    tile_rows, tile_cols, channels = features.shape
    padded = jnp.pad(padded, ((0, 0), (0, 8 - padded.shape[1] % 8), (0, 0)))
    normed = conv_norm(
        padded, dw_kernel, dw_bias, norm_gain, norm_bias, tile_rows, tile_cols
    ).reshape(-1, channels)
    summed = mlp(
        normed,
        features.reshape(-1, channels),
        w_expand,
        b_expand,
        w_reduce,
        b_reduce,
        layer_scale,
    )
    return summed.reshape(tile_rows, tile_cols, channels)


def shards(
    features,
    dw_kernel,
    dw_bias,
    norm_gain,
    norm_bias,
    w_expand,
    b_expand,
    w_reduce,
    b_reduce,
    layer_scale,
    w_query,
    w_keyval,
    rel_bias,
    w_out,
):
    tile_rows, tile_cols, channels = features.shape
    head_dim = channels // HEADS
    extended = padded_2(features, (("row", 0),), 3)
    padded = padded_2(extended, (("col", 1),), 3)
    block_out = block_pass(
        padded,
        features,
        dw_kernel,
        dw_bias,
        norm_gain,
        norm_bias,
        w_expand,
        b_expand,
        w_reduce,
        b_reduce,
        layer_scale,
    )
    region_side = tile_rows // 8
    local_count = region_side * region_side
    pooled = (
        block_out.astype(jnp.float32)
        .reshape(region_side, 8, region_side, 8, channels)
        .mean(axis=(1, 3))
    )
    pooled = pooled.astype(jnp.bfloat16).reshape(local_count, channels)
    queries = jnp.dot(pooled, w_query, preferred_element_type=jnp.float32).astype(jnp.bfloat16)
    columns = lax.axis_size("col")
    position = lax.axis_index("col")
    span_cols = region_side * columns
    key_count = local_count * columns
    sent = jnp.broadcast_to(pooled[None], (columns, local_count, channels)).reshape(
        columns * local_count, channels
    )
    band_pooled = lax.all_to_all(sent, "col", 0, 0, tiled=True)
    band_pooled = (
        band_pooled.reshape(columns, region_side, region_side, channels)
        .transpose(1, 0, 2, 3)
        .reshape(key_count, channels)
    )
    band_keyval = jnp.dot(band_pooled, w_keyval, preferred_element_type=jnp.float32).astype(
        jnp.bfloat16
    )
    windows = []
    for query_col in range(region_side):
        first = span_cols - 1 - (position * region_side + query_col)
        windows.append(lax.dynamic_slice_in_dim(rel_bias, first, span_cols, axis=2))
    rows_of = []
    for query_row in range(region_side):
        per_col = [
            w[:, region_side - 1 - query_row : 2 * region_side - 1 - query_row, :] for w in windows
        ]
        rows_of.append(jnp.stack(per_col, axis=1))
    bias_block = jnp.stack(rows_of, axis=1).reshape(HEADS, local_count, key_count)
    query_heads = queries.reshape(local_count, HEADS, head_dim)
    key_heads = band_keyval[:, :channels].reshape(key_count, HEADS, head_dim)
    value_heads = band_keyval[:, channels:].reshape(key_count, HEADS, head_dim)
    scores = (
        jnp.einsum("qhd,khd->hqk", query_heads, key_heads, preferred_element_type=jnp.float32)
        / jnp.sqrt(jnp.float32(head_dim))
        + bias_block
    )
    attn = jax.nn.softmax(scores, axis=-1).astype(jnp.bfloat16)
    context = (
        jnp.einsum("hqk,khd->qhd", attn, value_heads, preferred_element_type=jnp.float32)
        .reshape(local_count, channels)
        .astype(jnp.bfloat16)
    )
    lifted = jnp.dot(context, w_out, preferred_element_type=jnp.float32).reshape(
        region_side, 1, region_side, 1, channels
    )
    spread = jnp.broadcast_to(lifted, (region_side, 8, region_side, 8, channels)).reshape(
        tile_rows, tile_cols, channels
    )
    return (block_out.astype(jnp.float32) + spread).astype(jnp.bfloat16)


def solution(mesh):
    return jax.shard_map(
        shards,
        mesh=mesh,
        in_specs=(
            P("row", "col", None),
            P(),
            P(),
            P(),
            P(),
            P(),
            P(),
            P(),
            P(),
            P(),
            P(),
            P(),
            P(),
            P(),
        ),
        out_specs=P("row", "col", None),
        check_vma=False,
    )
```

```python
import jax
import jax.numpy as jnp
from jax import lax
from jax.sharding import PartitionSpec as P
from jax.experimental import pallas as pl
from jax.experimental.pallas import tpu as pltpu

HEADS = 8


def shifted(piece, axis):
    devices = lax.axis_size(axis)
    up = [(i, i + 1) for i in range(devices - 1)]
    down = [(i + 1, i) for i in range(devices - 1)]
    return lax.ppermute(piece, axis, up), lax.ppermute(piece, axis, down)


def halo_pieces(features, width):
    rows, cols = features.shape[:2]
    top, _ = shifted(features[rows - width :], "row")
    _, bottom = shifted(features[:width], "row")
    last_cols = jnp.concatenate(
        [top[:, cols - width :], features[:, cols - width :], bottom[:, cols - width :]], axis=0
    )
    first_cols = jnp.concatenate([top[:, :width], features[:, :width], bottom[:, :width]], axis=0)
    left, _ = shifted(last_cols, "col")
    _, right = shifted(first_cols, "col")
    return top, bottom, left, right

TAPS = 7
ROW_BLOCK = 2


def conv_norm_kernel(
    c_ref, t_ref, b_ref, l_ref, r_ref, k_ref, db_ref, g_ref, nb_ref, o_ref, xf_ref, kf_ref, sh_ref
):
    tile_rows, tile_cols, channels = o_ref.shape
    halo = t_ref.shape[0]
    rows_p = tile_rows + 2 * halo
    for a in range(TAPS):
        kf_ref[a, pl.ds(0, TAPS), :] = k_ref[a].astype(jnp.float32)

    def put(r, mid):
        xf_ref[r, pl.ds(0, halo), :] = l_ref[r].astype(jnp.float32)
        xf_ref[r, pl.ds(halo, tile_cols), :] = mid.astype(jnp.float32)
        xf_ref[r, pl.ds(halo + tile_cols, halo), :] = r_ref[r].astype(jnp.float32)
        for b in range(TAPS):
            sh_ref[b, r] = xf_ref[r, pl.ds(b, tile_cols), :]

    for r in range(halo):
        put(r, t_ref[r])
        put(rows_p - halo + r, b_ref[r])

    def widen(r, carry):
        put(r, c_ref[r - halo])
        return carry

    lax.fori_loop(halo, rows_p - halo, widen, 0)
    db = db_ref[...]
    g = g_ref[...]
    nb = nb_ref[...]

    def body(i, carry):
        r0 = pl.multiple_of(i * ROW_BLOCK, ROW_BLOCK)
        acc = jnp.zeros((ROW_BLOCK, tile_cols, channels), jnp.float32)
        for a in range(TAPS):
            for b in range(TAPS):
                acc = acc + sh_ref[b, pl.ds(r0 + a, ROW_BLOCK)] * kf_ref[a, pl.ds(b, 1), :]
        acc = acc + db
        mean = jnp.mean(acc, axis=-1, keepdims=True)
        cen = acc - mean
        var = jnp.mean(cen * cen, axis=-1, keepdims=True)
        o_ref[pl.ds(r0, ROW_BLOCK)] = (cen * lax.rsqrt(var + 1e-06) * g + nb).astype(o_ref.dtype)
        return carry

    lax.fori_loop(0, tile_rows // ROW_BLOCK, body, 0)


def conv_norm(centre, top, bottom, left, right, dw_kernel, dw_bias, norm_gain, norm_bias):
    tile_rows, tile_cols, channels = centre.shape
    halo = top.shape[0]
    rows_p = tile_rows + 2 * halo
    cols_p = tile_cols + 2 * halo
    cols_p += -cols_p % 8
    vmem = pl.BlockSpec(memory_space=pltpu.VMEM)
    return pl.pallas_call(
        conv_norm_kernel,
        out_shape=jax.ShapeDtypeStruct((tile_rows, tile_cols, channels), jnp.bfloat16),
        in_specs=[vmem] * 9,
        out_specs=vmem,
        scratch_shapes=[
            pltpu.VMEM((rows_p, cols_p, channels), jnp.float32),
            pltpu.VMEM((TAPS, 8, channels), jnp.float32),
            pltpu.VMEM((TAPS, rows_p, tile_cols, channels), jnp.float32),
        ],
        cost_estimate=pl.CostEstimate(
            flops=2 * TAPS * TAPS * tile_rows * tile_cols * channels,
            bytes_accessed=2 * (rows_p * cols_p + tile_rows * tile_cols) * channels,
            transcendentals=tile_rows * tile_cols,
        ),
    )(
        centre,
        top,
        bottom,
        left,
        right,
        dw_kernel,
        dw_bias.reshape(1, channels),
        norm_gain.reshape(1, channels),
        norm_bias.reshape(1, channels),
    )


ERFC_COEFFS = (
    -1.26551223,
    1.00002368,
    0.37409196,
    0.09678418,
    -0.18628806,
    0.27886807,
    -1.13520398,
    1.48851587,
    -0.82215223,
    0.17087277,
)
PIXEL_BLOCK = 256
HIDDEN_BLOCK = 256


def gelu_exact(pre):
    z = jnp.abs(pre) * jnp.float32(0.7071067811865476)
    t = 1.0 / (1.0 + 0.5 * z)
    poly = jnp.float32(ERFC_COEFFS[-1])
    for coeff in ERFC_COEFFS[-2::-1]:
        poly = poly * t + jnp.float32(coeff)
    tail = t * jnp.exp(poly - z * z)
    one_plus_erf = jnp.where(pre >= 0, 2.0 - tail, tail)
    return 0.5 * pre * one_plus_erf


def mlp_kernel(n_ref, f_ref, we_ref, be_ref, wr_ref, br_ref, ls_ref, o_ref, p_ref):
    normed = n_ref[...]
    hidden_total = we_ref.shape[1]
    acc = jnp.zeros(o_ref.shape, jnp.float32)
    for h0 in range(0, hidden_total, HIDDEN_BLOCK):
        pre = (
            jnp.dot(normed, we_ref[:, h0 : h0 + HIDDEN_BLOCK], preferred_element_type=jnp.float32)
            + be_ref[:, h0 : h0 + HIDDEN_BLOCK]
        )
        hidden = gelu_exact(pre).astype(jnp.bfloat16)
        acc = acc + jnp.dot(hidden, wr_ref[h0 : h0 + HIDDEN_BLOCK, :], preferred_element_type=jnp.float32)
    reduced = acc + br_ref[...]
    out = (f_ref[...].astype(jnp.float32) + ls_ref[...] * reduced).astype(o_ref.dtype)
    o_ref[...] = out
    pixels, channels = o_ref.shape
    tile_cols = pixels // 8
    column_sums = out.astype(jnp.float32).reshape(8, tile_cols, channels).sum(axis=0)
    region_sums = column_sums.reshape(tile_cols // 8, 8, channels).sum(axis=1)
    p_ref[0] = (region_sums * jnp.float32(1.0 / 64.0)).astype(p_ref.dtype)


def mlp(normed, features, w_expand, b_expand, w_reduce, b_reduce, layer_scale, tile_cols):
    pixels, channels = normed.shape
    hidden_total = w_expand.shape[1]
    block = 8 * tile_cols
    steps = pixels // block
    rows = pl.BlockSpec((block, channels), lambda i: (i, 0))
    whole = lambda shape: pl.BlockSpec(shape, lambda i: (0, 0))
    return pl.pallas_call(
        mlp_kernel,
        out_shape=(
            jax.ShapeDtypeStruct((pixels, channels), jnp.bfloat16),
            jax.ShapeDtypeStruct((steps, tile_cols // 8, channels), jnp.bfloat16),
        ),
        grid=(steps,),
        in_specs=[
            rows,
            rows,
            whole((channels, hidden_total)),
            whole((1, hidden_total)),
            whole((hidden_total, channels)),
            whole((1, channels)),
            whole((1, channels)),
        ],
        out_specs=(rows, pl.BlockSpec((1, tile_cols // 8, channels), lambda i: (i, 0, 0))),
        cost_estimate=pl.CostEstimate(
            flops=4 * pixels * channels * hidden_total,
            bytes_accessed=2 * (3 * pixels * channels + 2 * channels * hidden_total),
            transcendentals=2 * pixels * hidden_total,
        ),
    )(
        normed,
        features,
        w_expand,
        b_expand.reshape(1, hidden_total),
        w_reduce,
        b_reduce.reshape(1, channels),
        layer_scale.reshape(1, channels),
    )

def block_pass(
    pieces,
    features,
    dw_kernel,
    dw_bias,
    norm_gain,
    norm_bias,
    w_expand,
    b_expand,
    w_reduce,
    b_reduce,
    layer_scale,
):
    tile_rows, tile_cols, channels = features.shape
    normed = conv_norm(features, *pieces, dw_kernel, dw_bias, norm_gain, norm_bias).reshape(
        -1, channels
    )
    summed, pooled = mlp(
        normed,
        features.reshape(-1, channels),
        w_expand,
        b_expand,
        w_reduce,
        b_reduce,
        layer_scale,
        tile_cols,
    )
    return summed.reshape(tile_rows, tile_cols, channels), pooled


def shards(
    features,
    dw_kernel,
    dw_bias,
    norm_gain,
    norm_bias,
    w_expand,
    b_expand,
    w_reduce,
    b_reduce,
    layer_scale,
    w_query,
    w_keyval,
    rel_bias,
    w_out,
):
    tile_rows, tile_cols, channels = features.shape
    head_dim = channels // HEADS
    pieces = halo_pieces(features, 3)
    block_out, pooled = block_pass(
        pieces,
        features,
        dw_kernel,
        dw_bias,
        norm_gain,
        norm_bias,
        w_expand,
        b_expand,
        w_reduce,
        b_reduce,
        layer_scale,
    )
    region_side = tile_rows // 8
    local_count = region_side * region_side
    pooled = pooled.reshape(local_count, channels)
    queries = jnp.dot(pooled, w_query, preferred_element_type=jnp.float32).astype(jnp.bfloat16)
    columns = lax.axis_size("col")
    position = lax.axis_index("col")
    span_cols = region_side * columns
    key_count = local_count * columns
    sent = jnp.broadcast_to(pooled[None], (columns, local_count, channels)).reshape(
        columns * local_count, channels
    )
    band_pooled = lax.all_to_all(sent, "col", 0, 0, tiled=True)
    band_pooled = (
        band_pooled.reshape(columns, region_side, region_side, channels)
        .transpose(1, 0, 2, 3)
        .reshape(key_count, channels)
    )
    band_keyval = jnp.dot(band_pooled, w_keyval, preferred_element_type=jnp.float32).astype(
        jnp.bfloat16
    )
    windows = []
    for query_col in range(region_side):
        first = span_cols - 1 - (position * region_side + query_col)
        windows.append(lax.dynamic_slice_in_dim(rel_bias, first, span_cols, axis=2))
    rows_of = []
    for query_row in range(region_side):
        per_col = [
            w[:, region_side - 1 - query_row : 2 * region_side - 1 - query_row, :] for w in windows
        ]
        rows_of.append(jnp.stack(per_col, axis=1))
    bias_block = jnp.stack(rows_of, axis=1).reshape(HEADS, local_count, key_count)
    query_heads = queries.reshape(local_count, HEADS, head_dim)
    key_heads = band_keyval[:, :channels].reshape(key_count, HEADS, head_dim)
    value_heads = band_keyval[:, channels:].reshape(key_count, HEADS, head_dim)
    scores = (
        jnp.einsum("qhd,khd->hqk", query_heads, key_heads, preferred_element_type=jnp.float32)
        / jnp.sqrt(jnp.float32(head_dim))
        + bias_block
    )
    attn = jax.nn.softmax(scores, axis=-1).astype(jnp.bfloat16)
    context = (
        jnp.einsum("hqk,khd->qhd", attn, value_heads, preferred_element_type=jnp.float32)
        .reshape(local_count, channels)
        .astype(jnp.bfloat16)
    )
    lifted = jnp.dot(context, w_out, preferred_element_type=jnp.float32).reshape(
        region_side, 1, region_side, 1, channels
    )
    spread = jnp.broadcast_to(lifted, (region_side, 8, region_side, 8, channels)).reshape(
        tile_rows, tile_cols, channels
    )
    return (block_out.astype(jnp.float32) + spread).astype(jnp.bfloat16)


def solution(mesh):
    return jax.shard_map(
        shards,
        mesh=mesh,
        in_specs=(
            P("row", "col", None),
            P(),
            P(),
            P(),
            P(),
            P(),
            P(),
            P(),
            P(),
            P(),
            P(),
            P(),
            P(),
            P(),
        ),
        out_specs=P("row", "col", None),
        check_vma=False,
    )
```

```python
import jax
import jax.numpy as jnp
from jax import lax
from jax.sharding import PartitionSpec as P
from jax.experimental import pallas as pl
from jax.experimental.pallas import tpu as pltpu

HEADS = 8


def shifted(piece, axis):
    devices = lax.axis_size(axis)
    up = [(i, i + 1) for i in range(devices - 1)]
    down = [(i + 1, i) for i in range(devices - 1)]
    return lax.ppermute(piece, axis, up), lax.ppermute(piece, axis, down)


def halo_pieces(features, width):
    rows, cols = features.shape[:2]
    top, _ = shifted(features[rows - width :], "row")
    _, bottom = shifted(features[:width], "row")
    last_cols = jnp.concatenate(
        [top[:, cols - width :], features[:, cols - width :], bottom[:, cols - width :]], axis=0
    )
    first_cols = jnp.concatenate([top[:, :width], features[:, :width], bottom[:, :width]], axis=0)
    left, _ = shifted(last_cols, "col")
    _, right = shifted(first_cols, "col")
    return top, bottom, left, right

TAPS = 7
ROW_BLOCK = 8


def conv_norm_kernel(x_ref, k_ref, db_ref, g_ref, nb_ref, o_ref, kf_ref, sh_ref):
    rows_p = x_ref.shape[0]
    tile_rows, tile_cols, channels = o_ref.shape
    for a in range(TAPS):
        kf_ref[a, pl.ds(0, TAPS), :] = k_ref[a].astype(jnp.float32)

    def widen(r, carry):
        row = x_ref[r].astype(jnp.float32)
        for b in range(TAPS):
            sh_ref[b, r] = row[b : b + tile_cols]
        return carry

    lax.fori_loop(0, rows_p, widen, 0)
    db = db_ref[...]
    g = g_ref[...]
    nb = nb_ref[...]
    lanes = 128
    halves = channels // lanes

    def body(i, carry):
        r0 = pl.multiple_of(i * ROW_BLOCK, ROW_BLOCK)
        for s0 in range(0, tile_cols, 8):
            parts = []
            for h in range(halves):
                lane = pl.ds(h * lanes, lanes)
                acc = jnp.zeros((ROW_BLOCK, 8, lanes), jnp.float32)
                for b in range(TAPS):
                    x = sh_ref[b, pl.ds(r0, ROW_BLOCK + TAPS - 1), pl.ds(s0, 8), lane]
                    for a in range(TAPS):
                        acc = acc + x[a : a + ROW_BLOCK] * kf_ref[a, pl.ds(b, 1), lane]
                parts.append(acc)
            acc = jnp.concatenate(parts, axis=-1) + db
            mean = jnp.mean(acc, axis=-1, keepdims=True)
            cen = acc - mean
            var = jnp.mean(cen * cen, axis=-1, keepdims=True)
            normed = cen * lax.rsqrt(var + 1e-06) * g + nb
            o_ref[pl.ds(r0, ROW_BLOCK), pl.ds(s0, 8), :] = normed.astype(o_ref.dtype)
        return carry

    lax.fori_loop(0, tile_rows // ROW_BLOCK, body, 0)


def conv_norm(padded, dw_kernel, dw_bias, norm_gain, norm_bias, tile_rows, tile_cols):
    rows_p, cols_p, channels = padded.shape
    vmem = pl.BlockSpec(memory_space=pltpu.VMEM)
    return pl.pallas_call(
        conv_norm_kernel,
        out_shape=jax.ShapeDtypeStruct((tile_rows, tile_cols, channels), jnp.bfloat16),
        in_specs=[vmem] * 5,
        out_specs=vmem,
        scratch_shapes=[
            pltpu.VMEM((TAPS, 8, channels), jnp.float32),
            pltpu.VMEM((TAPS, rows_p, tile_cols, channels), jnp.float32),
        ],
        cost_estimate=pl.CostEstimate(
            flops=2 * TAPS * TAPS * tile_rows * tile_cols * channels,
            bytes_accessed=2 * (rows_p * cols_p + tile_rows * tile_cols) * channels,
            transcendentals=tile_rows * tile_cols,
        ),
    )(
        padded,
        dw_kernel,
        dw_bias.reshape(1, channels),
        norm_gain.reshape(1, channels),
        norm_bias.reshape(1, channels),
    )


ERFC_COEFFS = (
    -1.26551223,
    1.00002368,
    0.37409196,
    0.09678418,
    -0.18628806,
    0.27886807,
    -1.13520398,
    1.48851587,
    -0.82215223,
    0.17087277,
)
PIXEL_BLOCK = 256
HIDDEN_BLOCK = 256


def gelu_exact(pre):
    z = jnp.abs(pre) * jnp.float32(0.7071067811865476)
    t = 1.0 / (1.0 + 0.5 * z)
    poly = jnp.float32(ERFC_COEFFS[-1])
    for coeff in ERFC_COEFFS[-2::-1]:
        poly = poly * t + jnp.float32(coeff)
    tail = t * jnp.exp(poly - z * z)
    one_plus_erf = jnp.where(pre >= 0, 2.0 - tail, tail)
    return 0.5 * pre * one_plus_erf


def mlp_kernel(n_ref, f_ref, we_ref, be_ref, wr_ref, br_ref, ls_ref, o_ref, p_ref):
    normed = n_ref[...]
    hidden_total = we_ref.shape[1]
    acc = jnp.zeros(o_ref.shape, jnp.float32)
    for h0 in range(0, hidden_total, HIDDEN_BLOCK):
        pre = (
            jnp.dot(normed, we_ref[:, h0 : h0 + HIDDEN_BLOCK], preferred_element_type=jnp.float32)
            + be_ref[:, h0 : h0 + HIDDEN_BLOCK]
        )
        hidden = gelu_exact(pre).astype(jnp.bfloat16)
        acc = acc + jnp.dot(hidden, wr_ref[h0 : h0 + HIDDEN_BLOCK, :], preferred_element_type=jnp.float32)
    reduced = acc + br_ref[...]
    out = (f_ref[...].astype(jnp.float32) + ls_ref[...] * reduced).astype(o_ref.dtype)
    o_ref[...] = out
    pixels, channels = o_ref.shape
    tile_cols = pixels // 8
    column_sums = out.astype(jnp.float32).reshape(8, tile_cols, channels).sum(axis=0)
    region_sums = column_sums.reshape(tile_cols // 8, 8, channels).sum(axis=1)
    p_ref[0] = (region_sums * jnp.float32(1.0 / 64.0)).astype(p_ref.dtype)


def mlp(normed, features, w_expand, b_expand, w_reduce, b_reduce, layer_scale, tile_cols):
    pixels, channels = normed.shape
    hidden_total = w_expand.shape[1]
    block = 8 * tile_cols
    steps = pixels // block
    rows = pl.BlockSpec((block, channels), lambda i: (i, 0))
    whole = lambda shape: pl.BlockSpec(shape, lambda i: (0, 0))
    return pl.pallas_call(
        mlp_kernel,
        out_shape=(
            jax.ShapeDtypeStruct((pixels, channels), jnp.bfloat16),
            jax.ShapeDtypeStruct((steps, tile_cols // 8, channels), jnp.bfloat16),
        ),
        grid=(steps,),
        in_specs=[
            rows,
            rows,
            whole((channels, hidden_total)),
            whole((1, hidden_total)),
            whole((hidden_total, channels)),
            whole((1, channels)),
            whole((1, channels)),
        ],
        out_specs=(rows, pl.BlockSpec((1, tile_cols // 8, channels), lambda i: (i, 0, 0))),
        cost_estimate=pl.CostEstimate(
            flops=4 * pixels * channels * hidden_total,
            bytes_accessed=2 * (3 * pixels * channels + 2 * channels * hidden_total),
            transcendentals=2 * pixels * hidden_total,
        ),
    )(
        normed,
        features,
        w_expand,
        b_expand.reshape(1, hidden_total),
        w_reduce,
        b_reduce.reshape(1, channels),
        layer_scale.reshape(1, channels),
    )

def block_pass(
    pieces,
    features,
    dw_kernel,
    dw_bias,
    norm_gain,
    norm_bias,
    w_expand,
    b_expand,
    w_reduce,
    b_reduce,
    layer_scale,
):
    tile_rows, tile_cols, channels = features.shape
    top, bottom, left, right = pieces
    extended = jnp.concatenate([top, features, bottom], axis=0)
    padded = jnp.concatenate(
        [left, extended, right, jnp.zeros_like(right)[:, : -(tile_cols + 3 * 3) % 8]], axis=1
    )
    normed = conv_norm(
        padded, dw_kernel, dw_bias, norm_gain, norm_bias, tile_rows, tile_cols
    ).reshape(-1, channels)
    summed, pooled = mlp(
        normed,
        features.reshape(-1, channels),
        w_expand,
        b_expand,
        w_reduce,
        b_reduce,
        layer_scale,
        tile_cols,
    )
    return summed.reshape(tile_rows, tile_cols, channels), pooled


def shards(
    features,
    dw_kernel,
    dw_bias,
    norm_gain,
    norm_bias,
    w_expand,
    b_expand,
    w_reduce,
    b_reduce,
    layer_scale,
    w_query,
    w_keyval,
    rel_bias,
    w_out,
):
    tile_rows, tile_cols, channels = features.shape
    head_dim = channels // HEADS
    pieces = halo_pieces(features, 3)
    block_out, pooled = block_pass(
        pieces,
        features,
        dw_kernel,
        dw_bias,
        norm_gain,
        norm_bias,
        w_expand,
        b_expand,
        w_reduce,
        b_reduce,
        layer_scale,
    )
    region_side = tile_rows // 8
    local_count = region_side * region_side
    queries = jnp.einsum("rcd,de->rce", pooled, w_query, preferred_element_type=jnp.float32)
    queries = queries.astype(jnp.bfloat16).reshape(local_count, channels)
    columns = lax.axis_size("col")
    position = lax.axis_index("col")
    span_cols = region_side * columns
    key_count = local_count * columns
    sent = jnp.broadcast_to(pooled[None], (columns,) + pooled.shape)
    band_pooled = lax.all_to_all(sent, "col", 0, 0)
    band_pooled = (
        band_pooled.reshape(columns, region_side, region_side, channels)
        .transpose(1, 0, 2, 3)
        .reshape(key_count, channels)
    )
    band_keyval = jnp.dot(band_pooled, w_keyval, preferred_element_type=jnp.float32).astype(
        jnp.bfloat16
    )
    windows = []
    for query_col in range(region_side):
        first = span_cols - 1 - (position * region_side + query_col)
        windows.append(lax.dynamic_slice_in_dim(rel_bias, first, span_cols, axis=2))
    rows_of = []
    for query_row in range(region_side):
        per_col = [
            w[:, region_side - 1 - query_row : 2 * region_side - 1 - query_row, :] for w in windows
        ]
        rows_of.append(jnp.stack(per_col, axis=1))
    bias_block = jnp.stack(rows_of, axis=1).reshape(HEADS, local_count, key_count)
    query_heads = queries.reshape(local_count, HEADS, head_dim)
    key_heads = band_keyval[:, :channels].reshape(key_count, HEADS, head_dim)
    value_heads = band_keyval[:, channels:].reshape(key_count, HEADS, head_dim)
    scores = (
        jnp.einsum("qhd,khd->hqk", query_heads, key_heads, preferred_element_type=jnp.float32)
        / jnp.sqrt(jnp.float32(head_dim))
        + bias_block
    )
    attn = jax.nn.softmax(scores, axis=-1).astype(jnp.bfloat16)
    context = (
        jnp.einsum("hqk,khd->qhd", attn, value_heads, preferred_element_type=jnp.float32)
        .reshape(local_count, channels)
        .astype(jnp.bfloat16)
    )
    lifted = jnp.dot(context, w_out, preferred_element_type=jnp.float32).reshape(
        region_side, 1, region_side, 1, channels
    )
    spread = jnp.broadcast_to(lifted, (region_side, 8, region_side, 8, channels)).reshape(
        tile_rows, tile_cols, channels
    )
    return (block_out.astype(jnp.float32) + spread).astype(jnp.bfloat16)


def solution(mesh):
    return jax.shard_map(
        shards,
        mesh=mesh,
        in_specs=(
            P("row", "col", None),
            P(),
            P(),
            P(),
            P(),
            P(),
            P(),
            P(),
            P(),
            P(),
            P(),
            P(),
            P(),
            P(),
        ),
        out_specs=P("row", "col", None),
        check_vma=False,
    )
```

```python
import jax
import jax.numpy as jnp
from jax import lax
from jax.sharding import PartitionSpec as P
from jax.experimental import pallas as pl
from jax.experimental.pallas import tpu as pltpu

HEADS = 8


def shifted(piece, axis):
    devices = lax.axis_size(axis)
    up = [(i, i + 1) for i in range(devices - 1)]
    down = [(i + 1, i) for i in range(devices - 1)]
    return lax.ppermute(piece, axis, up), lax.ppermute(piece, axis, down)


def halo_pieces(features, width):
    rows, cols = features.shape[:2]
    left, _ = shifted(features[:, cols - width :], "col")
    _, right = shifted(features[:, :width], "col")
    spare = -(cols + 2 * width) % 8
    extended = jnp.concatenate([left, features, right, jnp.zeros_like(left)[:, :spare]], axis=1)
    top, _ = shifted(extended[rows - width :], "row")
    _, bottom = shifted(extended[:width], "row")
    return extended, top, bottom

TAPS = 7
ROW_BLOCK = 8


def conv_norm_kernel(x_ref, k_ref, db_ref, g_ref, nb_ref, o_ref, kf_ref, sh_ref):
    slabs, rows_in = x_ref.shape[:2]
    n_out, tile_cols, channels = o_ref.shape[1:]
    for a in range(TAPS):
        kf_ref[a, pl.ds(0, TAPS), :] = k_ref[a].astype(jnp.float32)
    db = db_ref[...]
    g = g_ref[...]
    nb = nb_ref[...]
    lanes = 128
    halves = channels // lanes

    for slab in range(slabs):

        def widen(r, carry):
            row = x_ref[slab, r].astype(jnp.float32)
            for b in range(TAPS):
                sh_ref[b, r] = row[b : b + tile_cols]
            return carry

        lax.fori_loop(0, rows_in, widen, 0)

        def rows_block(r0, count):
            for s0 in range(0, tile_cols, 8):
                parts = []
                for h in range(halves):
                    lane = pl.ds(h * lanes, lanes)
                    acc = jnp.zeros((count, 8, lanes), jnp.float32)
                    for b in range(TAPS):
                        x = sh_ref[b, pl.ds(r0, count + TAPS - 1), pl.ds(s0, 8), lane]
                        for a in range(TAPS):
                            acc = acc + x[a : a + count] * kf_ref[a, pl.ds(b, 1), lane]
                    parts.append(acc)
                acc = jnp.concatenate(parts, axis=-1) + db
                mean = jnp.mean(acc, axis=-1, keepdims=True)
                cen = acc - mean
                var = jnp.mean(cen * cen, axis=-1, keepdims=True)
                normed = cen * lax.rsqrt(var + 1e-06) * g + nb
                o_ref[slab, pl.ds(r0, count), pl.ds(s0, 8), :] = normed.astype(o_ref.dtype)

        full = n_out // ROW_BLOCK

        def body(i, carry):
            rows_block(pl.multiple_of(i * ROW_BLOCK, ROW_BLOCK), ROW_BLOCK)
            return carry

        if full:
            lax.fori_loop(0, full, body, 0)
        if n_out % ROW_BLOCK:
            rows_block(full * ROW_BLOCK, n_out % ROW_BLOCK)


def conv_norm(slabs_in, dw_kernel, dw_bias, norm_gain, norm_bias, tile_cols):
    slabs, rows_in, cols_p, channels = slabs_in.shape
    n_out = rows_in - (TAPS - 1)
    vmem = pl.BlockSpec(memory_space=pltpu.VMEM)
    return pl.pallas_call(
        conv_norm_kernel,
        out_shape=jax.ShapeDtypeStruct((slabs, n_out, tile_cols, channels), jnp.bfloat16),
        in_specs=[vmem] * 5,
        out_specs=vmem,
        scratch_shapes=[
            pltpu.VMEM((TAPS, 8, channels), jnp.float32),
            pltpu.VMEM((TAPS, rows_in, tile_cols, channels), jnp.float32),
        ],
        cost_estimate=pl.CostEstimate(
            flops=2 * TAPS * TAPS * slabs * n_out * tile_cols * channels,
            bytes_accessed=2 * slabs * (rows_in * cols_p + n_out * tile_cols) * channels,
            transcendentals=slabs * n_out * tile_cols,
        ),
    )(
        slabs_in,
        dw_kernel,
        dw_bias.reshape(1, channels),
        norm_gain.reshape(1, channels),
        norm_bias.reshape(1, channels),
    )


ERFC_COEFFS = (
    -1.26551223,
    1.00002368,
    0.37409196,
    0.09678418,
    -0.18628806,
    0.27886807,
    -1.13520398,
    1.48851587,
    -0.82215223,
    0.17087277,
)
PIXEL_BLOCK = 256
HIDDEN_BLOCK = 256


def gelu_exact(pre):
    z = jnp.abs(pre) * jnp.float32(0.7071067811865476)
    t = 1.0 / (1.0 + 0.5 * z)
    poly = jnp.float32(ERFC_COEFFS[-1])
    for coeff in ERFC_COEFFS[-2::-1]:
        poly = poly * t + jnp.float32(coeff)
    tail = t * jnp.exp(poly - z * z)
    one_plus_erf = jnp.where(pre >= 0, 2.0 - tail, tail)
    return 0.5 * pre * one_plus_erf


def mlp_kernel(n_ref, f_ref, we_ref, be_ref, wr_ref, br_ref, ls_ref, o_ref, p_ref):
    normed = n_ref[...]
    hidden_total = we_ref.shape[1]
    acc = jnp.zeros(o_ref.shape, jnp.float32)
    for h0 in range(0, hidden_total, HIDDEN_BLOCK):
        pre = (
            jnp.dot(normed, we_ref[:, h0 : h0 + HIDDEN_BLOCK], preferred_element_type=jnp.float32)
            + be_ref[:, h0 : h0 + HIDDEN_BLOCK]
        )
        hidden = gelu_exact(pre).astype(jnp.bfloat16)
        acc = acc + jnp.dot(hidden, wr_ref[h0 : h0 + HIDDEN_BLOCK, :], preferred_element_type=jnp.float32)
    reduced = acc + br_ref[...]
    out = (f_ref[...].astype(jnp.float32) + ls_ref[...] * reduced).astype(o_ref.dtype)
    o_ref[...] = out
    pixels, channels = o_ref.shape
    tile_cols = pixels // 8
    column_sums = out.astype(jnp.float32).reshape(8, tile_cols, channels).sum(axis=0)
    region_sums = column_sums.reshape(tile_cols // 8, 8, channels).sum(axis=1)
    p_ref[0] = (region_sums * jnp.float32(1.0 / 64.0)).astype(p_ref.dtype)


def mlp(normed, features, w_expand, b_expand, w_reduce, b_reduce, layer_scale, tile_cols):
    pixels, channels = normed.shape
    hidden_total = w_expand.shape[1]
    block = 8 * tile_cols
    steps = pixels // block
    rows = pl.BlockSpec((block, channels), lambda i: (i, 0))
    whole = lambda shape: pl.BlockSpec(shape, lambda i: (0, 0))
    return pl.pallas_call(
        mlp_kernel,
        out_shape=(
            jax.ShapeDtypeStruct((pixels, channels), jnp.bfloat16),
            jax.ShapeDtypeStruct((steps, tile_cols // 8, channels), jnp.bfloat16),
        ),
        grid=(steps,),
        in_specs=[
            rows,
            rows,
            whole((channels, hidden_total)),
            whole((1, hidden_total)),
            whole((hidden_total, channels)),
            whole((1, channels)),
            whole((1, channels)),
        ],
        out_specs=(rows, pl.BlockSpec((1, tile_cols // 8, channels), lambda i: (i, 0, 0))),
        cost_estimate=pl.CostEstimate(
            flops=4 * pixels * channels * hidden_total,
            bytes_accessed=2 * (3 * pixels * channels + 2 * channels * hidden_total),
            transcendentals=2 * pixels * hidden_total,
        ),
    )(
        normed,
        features,
        w_expand,
        b_expand.reshape(1, hidden_total),
        w_reduce,
        b_reduce.reshape(1, channels),
        layer_scale.reshape(1, channels),
    )

def block_pass(
    pieces,
    features,
    dw_kernel,
    dw_bias,
    norm_gain,
    norm_bias,
    w_expand,
    b_expand,
    w_reduce,
    b_reduce,
    layer_scale,
):
    tile_rows, tile_cols, channels = features.shape
    extended, top, bottom = pieces
    reach = TAPS - 1
    inner = conv_norm(extended[None], dw_kernel, dw_bias, norm_gain, norm_bias, tile_cols)
    edge_in = jnp.stack(
        [
            jnp.concatenate([top, extended[:reach]], axis=0),
            jnp.concatenate([extended[tile_rows - reach :], bottom], axis=0),
        ]
    )
    edges = conv_norm(edge_in, dw_kernel, dw_bias, norm_gain, norm_bias, tile_cols)
    normed = jnp.concatenate([edges[0], inner[0], edges[1]], axis=0).reshape(-1, channels)
    summed, pooled = mlp(
        normed,
        features.reshape(-1, channels),
        w_expand,
        b_expand,
        w_reduce,
        b_reduce,
        layer_scale,
        tile_cols,
    )
    return summed.reshape(tile_rows, tile_cols, channels), pooled


def shards(
    features,
    dw_kernel,
    dw_bias,
    norm_gain,
    norm_bias,
    w_expand,
    b_expand,
    w_reduce,
    b_reduce,
    layer_scale,
    w_query,
    w_keyval,
    rel_bias,
    w_out,
):
    tile_rows, tile_cols, channels = features.shape
    head_dim = channels // HEADS
    pieces = halo_pieces(features, 3)
    block_out, pooled = block_pass(
        pieces,
        features,
        dw_kernel,
        dw_bias,
        norm_gain,
        norm_bias,
        w_expand,
        b_expand,
        w_reduce,
        b_reduce,
        layer_scale,
    )
    region_side = tile_rows // 8
    local_count = region_side * region_side
    queries = jnp.einsum("rcd,de->rce", pooled, w_query, preferred_element_type=jnp.float32)
    queries = queries.astype(jnp.bfloat16).reshape(local_count, channels)
    columns = lax.axis_size("col")
    position = lax.axis_index("col")
    span_cols = region_side * columns
    key_count = local_count * columns
    sent = jnp.broadcast_to(pooled[None], (columns,) + pooled.shape)
    band_pooled = lax.all_to_all(sent, "col", 0, 0)
    band_pooled = (
        band_pooled.reshape(columns, region_side, region_side, channels)
        .transpose(1, 0, 2, 3)
        .reshape(key_count, channels)
    )
    band_keyval = jnp.dot(band_pooled, w_keyval, preferred_element_type=jnp.float32).astype(
        jnp.bfloat16
    )
    windows = []
    for query_col in range(region_side):
        first = span_cols - 1 - (position * region_side + query_col)
        windows.append(lax.dynamic_slice_in_dim(rel_bias, first, span_cols, axis=2))
    rows_of = []
    for query_row in range(region_side):
        per_col = [
            w[:, region_side - 1 - query_row : 2 * region_side - 1 - query_row, :] for w in windows
        ]
        rows_of.append(jnp.stack(per_col, axis=1))
    bias_block = jnp.stack(rows_of, axis=1).reshape(HEADS, local_count, key_count)
    query_heads = queries.reshape(local_count, HEADS, head_dim)
    key_heads = band_keyval[:, :channels].reshape(key_count, HEADS, head_dim)
    value_heads = band_keyval[:, channels:].reshape(key_count, HEADS, head_dim)
    scores = (
        jnp.einsum("qhd,khd->hqk", query_heads, key_heads, preferred_element_type=jnp.float32)
        / jnp.sqrt(jnp.float32(head_dim))
        + bias_block
    )
    attn = jax.nn.softmax(scores, axis=-1).astype(jnp.bfloat16)
    context = (
        jnp.einsum("hqk,khd->qhd", attn, value_heads, preferred_element_type=jnp.float32)
        .reshape(local_count, channels)
        .astype(jnp.bfloat16)
    )
    lifted = jnp.dot(context, w_out, preferred_element_type=jnp.float32).reshape(
        region_side, 1, region_side, 1, channels
    )
    spread = jnp.broadcast_to(lifted, (region_side, 8, region_side, 8, channels)).reshape(
        tile_rows, tile_cols, channels
    )
    return (block_out.astype(jnp.float32) + spread).astype(jnp.bfloat16)


def solution(mesh):
    return jax.shard_map(
        shards,
        mesh=mesh,
        in_specs=(
            P("row", "col", None),
            P(),
            P(),
            P(),
            P(),
            P(),
            P(),
            P(),
            P(),
            P(),
            P(),
            P(),
            P(),
            P(),
        ),
        out_specs=P("row", "col", None),
        check_vma=False,
    )
```

```python
import jax
import jax.numpy as jnp
from jax import lax
from jax.sharding import PartitionSpec as P
from jax.experimental import pallas as pl
from jax.experimental.pallas import tpu as pltpu

HEADS = 8


def shifted(piece, axis):
    devices = lax.axis_size(axis)
    up = [(i, i + 1) for i in range(devices - 1)]
    down = [(i + 1, i) for i in range(devices - 1)]
    return lax.ppermute(piece, axis, up), lax.ppermute(piece, axis, down)


def halo_pieces(features, width):
    rows, cols = features.shape[:2]
    top, _ = shifted(features[rows - width :], "row")
    _, bottom = shifted(features[:width], "row")
    last_cols = jnp.concatenate(
        [top[:, cols - width :], features[:, cols - width :], bottom[:, cols - width :]], axis=0
    )
    first_cols = jnp.concatenate([top[:, :width], features[:, :width], bottom[:, :width]], axis=0)
    left, _ = shifted(last_cols, "col")
    _, right = shifted(first_cols, "col")
    return top, bottom, left, right

TAPS = 7
ROW_BLOCK = 8


def conv_norm_kernel(
    c_ref, t_ref, b_ref, l_ref, r_ref, k_ref, db_ref, g_ref, nb_ref, o_ref, kf_ref, sh_ref
):
    tile_rows, tile_cols, channels = o_ref.shape
    halo = t_ref.shape[0]
    rows_p = tile_rows + 2 * halo
    for a in range(TAPS):
        kf_ref[a, pl.ds(0, TAPS), :] = k_ref[a].astype(jnp.float32)

    def put(r, mid):
        row = jnp.concatenate([l_ref[r], mid, r_ref[r]], axis=0).astype(jnp.float32)
        for b in range(TAPS):
            sh_ref[b, r] = row[b : b + tile_cols]

    for r in range(halo):
        put(r, t_ref[r])
        put(rows_p - halo + r, b_ref[r])

    def widen(r, carry):
        put(r, c_ref[r - halo])
        return carry

    lax.fori_loop(halo, rows_p - halo, widen, 0)
    db = db_ref[...]
    g = g_ref[...]
    nb = nb_ref[...]
    lanes = 128
    halves = channels // lanes

    def body(i, carry):
        r0 = pl.multiple_of(i * ROW_BLOCK, ROW_BLOCK)
        for s0 in range(0, tile_cols, 8):
            parts = []
            for h in range(halves):
                lane = pl.ds(h * lanes, lanes)
                acc = jnp.zeros((ROW_BLOCK, 8, lanes), jnp.float32)
                for b in range(TAPS):
                    x = sh_ref[b, pl.ds(r0, ROW_BLOCK + TAPS - 1), pl.ds(s0, 8), lane]
                    for a in range(TAPS):
                        acc = acc + x[a : a + ROW_BLOCK] * kf_ref[a, pl.ds(b, 1), lane]
                parts.append(acc)
            acc = jnp.concatenate(parts, axis=-1) + db
            mean = jnp.mean(acc, axis=-1, keepdims=True)
            cen = acc - mean
            var = jnp.mean(cen * cen, axis=-1, keepdims=True)
            normed = cen * lax.rsqrt(var + 1e-06) * g + nb
            o_ref[pl.ds(r0, ROW_BLOCK), pl.ds(s0, 8), :] = normed.astype(o_ref.dtype)
        return carry

    lax.fori_loop(0, tile_rows // ROW_BLOCK, body, 0)


def conv_norm(centre, top, bottom, left, right, dw_kernel, dw_bias, norm_gain, norm_bias):
    tile_rows, tile_cols, channels = centre.shape
    rows_p = tile_rows + 2 * top.shape[0]
    vmem = pl.BlockSpec(memory_space=pltpu.VMEM)
    return pl.pallas_call(
        conv_norm_kernel,
        out_shape=jax.ShapeDtypeStruct((tile_rows, tile_cols, channels), jnp.bfloat16),
        in_specs=[vmem] * 9,
        out_specs=vmem,
        scratch_shapes=[
            pltpu.VMEM((TAPS, 8, channels), jnp.float32),
            pltpu.VMEM((TAPS, rows_p, tile_cols, channels), jnp.float32),
        ],
        cost_estimate=pl.CostEstimate(
            flops=2 * TAPS * TAPS * tile_rows * tile_cols * channels,
            bytes_accessed=2 * (rows_p * rows_p + tile_rows * tile_cols) * channels,
            transcendentals=tile_rows * tile_cols,
        ),
    )(
        centre,
        top,
        bottom,
        left,
        right,
        dw_kernel,
        dw_bias.reshape(1, channels),
        norm_gain.reshape(1, channels),
        norm_bias.reshape(1, channels),
    )

ERFC_COEFFS = (
    -1.26551223,
    1.00002368,
    0.37409196,
    0.09678418,
    -0.18628806,
    0.27886807,
    -1.13520398,
    1.48851587,
    -0.82215223,
    0.17087277,
)
PIXEL_BLOCK = 256
HIDDEN_BLOCK = 256


def gelu_exact(pre):
    z = jnp.abs(pre) * jnp.float32(0.7071067811865476)
    t = 1.0 / (1.0 + 0.5 * z)
    poly = jnp.float32(ERFC_COEFFS[-1])
    for coeff in ERFC_COEFFS[-2::-1]:
        poly = poly * t + jnp.float32(coeff)
    tail = t * jnp.exp(poly - z * z)
    one_plus_erf = jnp.where(pre >= 0, 2.0 - tail, tail)
    return 0.5 * pre * one_plus_erf


def mlp_kernel(n_ref, f_ref, we_ref, be_ref, wr_ref, br_ref, ls_ref, wq_ref, o_ref, q_ref, s_ref):
    normed = n_ref[...]
    hidden_total = we_ref.shape[1]
    acc = jnp.zeros(o_ref.shape, jnp.float32)
    for h0 in range(0, hidden_total, HIDDEN_BLOCK):
        pre = (
            jnp.dot(normed, we_ref[:, h0 : h0 + HIDDEN_BLOCK], preferred_element_type=jnp.float32)
            + be_ref[:, h0 : h0 + HIDDEN_BLOCK]
        )
        hidden = gelu_exact(pre).astype(jnp.bfloat16)
        acc = acc + jnp.dot(hidden, wr_ref[h0 : h0 + HIDDEN_BLOCK, :], preferred_element_type=jnp.float32)
    reduced = acc + br_ref[...]
    out = (f_ref[...].astype(jnp.float32) + ls_ref[...] * reduced).astype(o_ref.dtype)
    o_ref[...] = out
    pixels, channels = o_ref.shape
    tile_cols = pixels // 8
    per_row = tile_cols // 8
    column_sums = out.astype(jnp.float32).reshape(8, tile_cols, channels).sum(axis=0)
    region_sums = column_sums.reshape(per_row, 8, channels).sum(axis=1)
    pooled = (region_sums * jnp.float32(1.0 / 64.0)).astype(jnp.bfloat16)
    queries = jnp.dot(pooled, wq_ref[...], preferred_element_type=jnp.float32)
    queries = queries.astype(jnp.bfloat16).astype(jnp.float32)
    copies = jnp.broadcast_to(pooled.astype(jnp.float32)[None], (s_ref.shape[0], per_row, channels))
    step = pl.program_id(0)
    for k in range(s_ref.shape[1] // per_row):

        @pl.when(step == k)
        def _():
            q_ref[pl.ds(k * per_row, per_row), :] = queries
            s_ref[:, pl.ds(k * per_row, per_row), :] = copies


def mlp(normed, features, w_expand, b_expand, w_reduce, b_reduce, layer_scale, w_query, tile_cols, copies):
    pixels, channels = normed.shape
    hidden_total = w_expand.shape[1]
    block = 8 * tile_cols
    steps = pixels // block
    tokens = steps * (tile_cols // 8)
    rows = pl.BlockSpec((block, channels), lambda i: (i, 0))
    whole = lambda shape: pl.BlockSpec(shape, lambda i: (0,) * len(shape))
    return pl.pallas_call(
        mlp_kernel,
        out_shape=(
            jax.ShapeDtypeStruct((pixels, channels), jnp.bfloat16),
            jax.ShapeDtypeStruct((tokens, channels), jnp.float32),
            jax.ShapeDtypeStruct((copies, tokens, channels), jnp.float32),
        ),
        grid=(steps,),
        in_specs=[
            rows,
            rows,
            whole((channels, hidden_total)),
            whole((1, hidden_total)),
            whole((hidden_total, channels)),
            whole((1, channels)),
            whole((1, channels)),
            whole((channels, channels)),
        ],
        out_specs=(rows, whole((tokens, channels)), whole((copies, tokens, channels))),
        cost_estimate=pl.CostEstimate(
            flops=4 * pixels * channels * hidden_total,
            bytes_accessed=2 * (3 * pixels * channels + 2 * channels * hidden_total),
            transcendentals=2 * pixels * hidden_total,
        ),
    )(
        normed,
        features,
        w_expand,
        b_expand.reshape(1, hidden_total),
        w_reduce,
        b_reduce.reshape(1, channels),
        layer_scale.reshape(1, channels),
        w_query,
    )

def block_pass(
    pieces,
    features,
    dw_kernel,
    dw_bias,
    norm_gain,
    norm_bias,
    w_expand,
    b_expand,
    w_reduce,
    b_reduce,
    layer_scale,
    w_query,
    copies,
):
    tile_rows, tile_cols, channels = features.shape
    normed = conv_norm(features, *pieces, dw_kernel, dw_bias, norm_gain, norm_bias).reshape(
        -1, channels
    )
    summed, queries, sent = mlp(
        normed,
        features.reshape(-1, channels),
        w_expand,
        b_expand,
        w_reduce,
        b_reduce,
        layer_scale,
        w_query,
        tile_cols,
        copies,
    )
    return summed.reshape(tile_rows, tile_cols, channels), queries, sent


def shards(
    features,
    dw_kernel,
    dw_bias,
    norm_gain,
    norm_bias,
    w_expand,
    b_expand,
    w_reduce,
    b_reduce,
    layer_scale,
    w_query,
    w_keyval,
    rel_bias,
    w_out,
):
    tile_rows, tile_cols, channels = features.shape
    head_dim = channels // HEADS
    pieces = halo_pieces(features, 3)
    columns = lax.axis_size("col")
    position = lax.axis_index("col")
    block_out, queries, sent = block_pass(
        pieces,
        features,
        dw_kernel,
        dw_bias,
        norm_gain,
        norm_bias,
        w_expand,
        b_expand,
        w_reduce,
        b_reduce,
        layer_scale,
        w_query,
        columns,
    )
    region_side = tile_rows // 8
    local_count = region_side * region_side
    queries = queries.astype(jnp.bfloat16)
    span_cols = region_side * columns
    key_count = local_count * columns
    band_pooled = lax.all_to_all(sent, "col", 0, 0)
    band_pooled = (
        band_pooled.reshape(columns, region_side, region_side, channels)
        .transpose(1, 0, 2, 3)
        .reshape(key_count, channels)
        .astype(jnp.bfloat16)
    )
    band_keyval = jnp.dot(band_pooled, w_keyval, preferred_element_type=jnp.float32).astype(
        jnp.bfloat16
    )
    windows = []
    for query_col in range(region_side):
        first = span_cols - 1 - (position * region_side + query_col)
        windows.append(lax.dynamic_slice_in_dim(rel_bias, first, span_cols, axis=2))
    rows_of = []
    for query_row in range(region_side):
        per_col = [
            w[:, region_side - 1 - query_row : 2 * region_side - 1 - query_row, :] for w in windows
        ]
        rows_of.append(jnp.stack(per_col, axis=1))
    bias_block = jnp.stack(rows_of, axis=1).reshape(HEADS, local_count, key_count)
    query_heads = queries.reshape(local_count, HEADS, head_dim)
    key_heads = band_keyval[:, :channels].reshape(key_count, HEADS, head_dim)
    value_heads = band_keyval[:, channels:].reshape(key_count, HEADS, head_dim)
    scores = (
        jnp.einsum("qhd,khd->hqk", query_heads, key_heads, preferred_element_type=jnp.float32)
        / jnp.sqrt(jnp.float32(head_dim))
        + bias_block
    )
    attn = jax.nn.softmax(scores, axis=-1).astype(jnp.bfloat16)
    context = (
        jnp.einsum("hqk,khd->qhd", attn, value_heads, preferred_element_type=jnp.float32)
        .reshape(local_count, channels)
        .astype(jnp.bfloat16)
    )
    lifted = jnp.dot(context, w_out, preferred_element_type=jnp.float32).reshape(
        region_side, 1, region_side, 1, channels
    )
    spread = jnp.broadcast_to(lifted, (region_side, 8, region_side, 8, channels)).reshape(
        tile_rows, tile_cols, channels
    )
    return (block_out.astype(jnp.float32) + spread).astype(jnp.bfloat16)


def solution(mesh):
    return jax.shard_map(
        shards,
        mesh=mesh,
        in_specs=(
            P("row", "col", None),
            P(),
            P(),
            P(),
            P(),
            P(),
            P(),
            P(),
            P(),
            P(),
            P(),
            P(),
            P(),
            P(),
        ),
        out_specs=P("row", "col", None),
        check_vma=False,
    )
```

```python
import jax
import jax.numpy as jnp
from jax import lax
from jax.sharding import PartitionSpec as P
from jax.experimental import pallas as pl
from jax.experimental.pallas import tpu as pltpu

HEADS = 8


def shifted(piece, axis):
    devices = lax.axis_size(axis)
    up = [(i, i + 1) for i in range(devices - 1)]
    down = [(i + 1, i) for i in range(devices - 1)]
    return lax.ppermute(piece, axis, up), lax.ppermute(piece, axis, down)


def halo_pieces(features, width):
    rows, cols = features.shape[:2]
    top, _ = shifted(features[rows - width :], "row")
    _, bottom = shifted(features[:width], "row")
    last_cols = jnp.concatenate(
        [top[:, cols - width :], features[:, cols - width :], bottom[:, cols - width :]], axis=0
    )
    first_cols = jnp.concatenate([top[:, :width], features[:, :width], bottom[:, :width]], axis=0)
    left, _ = shifted(last_cols, "col")
    _, right = shifted(first_cols, "col")
    return top, bottom, left, right

TAPS = 7
ROW_BLOCK = 8


def conv_norm_kernel(
    c_ref, t_ref, b_ref, l_ref, r_ref, k_ref, db_ref, g_ref, nb_ref, o_ref, kf_ref, sh_ref
):
    tile_rows, tile_cols, channels = o_ref.shape
    halo = t_ref.shape[0]
    rows_p = tile_rows + 2 * halo
    for a in range(TAPS):
        kf_ref[a, pl.ds(0, TAPS), :] = k_ref[a].astype(jnp.float32)

    def put(r, mid):
        row = jnp.concatenate([l_ref[r], mid, r_ref[r]], axis=0).astype(jnp.float32)
        for b in range(TAPS):
            sh_ref[b, r] = row[b : b + tile_cols]

    for r in range(halo):
        put(r, t_ref[r])
        put(rows_p - halo + r, b_ref[r])

    def widen(r, carry):
        put(r, c_ref[r - halo])
        return carry

    lax.fori_loop(halo, rows_p - halo, widen, 0)
    db = db_ref[...]
    g = g_ref[...]
    nb = nb_ref[...]
    lanes = 128
    halves = channels // lanes

    def body(i, carry):
        r0 = pl.multiple_of(i * ROW_BLOCK, ROW_BLOCK)
        for s0 in range(0, tile_cols, 8):
            parts = []
            for h in range(halves):
                lane = pl.ds(h * lanes, lanes)
                acc = jnp.zeros((ROW_BLOCK, 8, lanes), jnp.float32)
                for b in range(TAPS):
                    x = sh_ref[b, pl.ds(r0, ROW_BLOCK + TAPS - 1), pl.ds(s0, 8), lane]
                    for a in range(TAPS):
                        acc = acc + x[a : a + ROW_BLOCK] * kf_ref[a, pl.ds(b, 1), lane]
                parts.append(acc)
            acc = jnp.concatenate(parts, axis=-1) + db
            mean = jnp.mean(acc, axis=-1, keepdims=True)
            cen = acc - mean
            var = jnp.mean(cen * cen, axis=-1, keepdims=True)
            normed = cen * lax.rsqrt(var + 1e-06) * g + nb
            o_ref[pl.ds(r0, ROW_BLOCK), pl.ds(s0, 8), :] = normed.astype(o_ref.dtype)
        return carry

    lax.fori_loop(0, tile_rows // ROW_BLOCK, body, 0)


def conv_norm(centre, top, bottom, left, right, dw_kernel, dw_bias, norm_gain, norm_bias):
    tile_rows, tile_cols, channels = centre.shape
    rows_p = tile_rows + 2 * top.shape[0]
    vmem = pl.BlockSpec(memory_space=pltpu.VMEM)
    return pl.pallas_call(
        conv_norm_kernel,
        out_shape=jax.ShapeDtypeStruct((tile_rows, tile_cols, channels), jnp.bfloat16),
        in_specs=[vmem] * 9,
        out_specs=vmem,
        scratch_shapes=[
            pltpu.VMEM((TAPS, 8, channels), jnp.float32),
            pltpu.VMEM((TAPS, rows_p, tile_cols, channels), jnp.float32),
        ],
        cost_estimate=pl.CostEstimate(
            flops=2 * TAPS * TAPS * tile_rows * tile_cols * channels,
            bytes_accessed=2 * (rows_p * rows_p + tile_rows * tile_cols) * channels,
            transcendentals=tile_rows * tile_cols,
        ),
    )(
        centre,
        top,
        bottom,
        left,
        right,
        dw_kernel,
        dw_bias.reshape(1, channels),
        norm_gain.reshape(1, channels),
        norm_bias.reshape(1, channels),
    )

ERFC_COEFFS = (
    -1.26551223,
    1.00002368,
    0.37409196,
    0.09678418,
    -0.18628806,
    0.27886807,
    -1.13520398,
    1.48851587,
    -0.82215223,
    0.17087277,
)
PIXEL_BLOCK = 256
HIDDEN_BLOCK = 256


def gelu_exact(pre):
    z = jnp.abs(pre) * jnp.float32(0.7071067811865476)
    t = 1.0 / (1.0 + 0.5 * z)
    poly = jnp.float32(ERFC_COEFFS[-1])
    for coeff in ERFC_COEFFS[-2::-1]:
        poly = poly * t + jnp.float32(coeff)
    tail = t * jnp.exp(poly - z * z)
    one_plus_erf = jnp.where(pre >= 0, 2.0 - tail, tail)
    return 0.5 * pre * one_plus_erf


def mlp_kernel(n_ref, f_ref, we_ref, be_ref, wr_ref, br_ref, ls_ref, wq_ref, o_ref, q_ref, s_ref):
    normed = n_ref[...]
    hidden_total = we_ref.shape[1]
    acc = jnp.zeros(o_ref.shape, jnp.float32)
    for h0 in range(0, hidden_total, HIDDEN_BLOCK):
        pre = (
            jnp.dot(normed, we_ref[:, h0 : h0 + HIDDEN_BLOCK], preferred_element_type=jnp.float32)
            + be_ref[:, h0 : h0 + HIDDEN_BLOCK]
        )
        hidden = gelu_exact(pre).astype(jnp.bfloat16)
        acc = acc + jnp.dot(hidden, wr_ref[h0 : h0 + HIDDEN_BLOCK, :], preferred_element_type=jnp.float32)
    reduced = acc + br_ref[...]
    out = (f_ref[...].astype(jnp.float32) + ls_ref[...] * reduced).astype(o_ref.dtype)
    o_ref[...] = out
    pixels, channels = o_ref.shape
    tile_cols = pixels // 8
    per_row = tile_cols // 8
    column_sums = out.astype(jnp.float32).reshape(8, tile_cols, channels).sum(axis=0)
    region_sums = column_sums.reshape(per_row, 8, channels).sum(axis=1)
    pooled = (region_sums * jnp.float32(1.0 / 64.0)).astype(jnp.bfloat16)
    queries = jnp.dot(pooled, wq_ref[...], preferred_element_type=jnp.float32)
    queries = queries.astype(jnp.bfloat16).astype(jnp.float32)
    copies = jnp.broadcast_to(pooled[None], (s_ref.shape[0], per_row, channels))
    step = pl.program_id(0)
    for k in range(s_ref.shape[1] // per_row):

        @pl.when(step == k)
        def _():
            q_ref[pl.ds(k * per_row, per_row), :] = queries
            s_ref[:, pl.ds(k * per_row, per_row), :] = copies


def mlp(normed, features, w_expand, b_expand, w_reduce, b_reduce, layer_scale, w_query, tile_cols, copies):
    pixels, channels = normed.shape
    hidden_total = w_expand.shape[1]
    block = 8 * tile_cols
    steps = pixels // block
    tokens = steps * (tile_cols // 8)
    rows = pl.BlockSpec((block, channels), lambda i: (i, 0))
    whole = lambda shape: pl.BlockSpec(shape, lambda i: (0,) * len(shape))
    return pl.pallas_call(
        mlp_kernel,
        out_shape=(
            jax.ShapeDtypeStruct((pixels, channels), jnp.bfloat16),
            jax.ShapeDtypeStruct((tokens, channels), jnp.float32),
            jax.ShapeDtypeStruct((copies, tokens, channels), jnp.bfloat16),
        ),
        grid=(steps,),
        in_specs=[
            rows,
            rows,
            whole((channels, hidden_total)),
            whole((1, hidden_total)),
            whole((hidden_total, channels)),
            whole((1, channels)),
            whole((1, channels)),
            whole((channels, channels)),
        ],
        out_specs=(rows, whole((tokens, channels)), whole((copies, tokens, channels))),
        cost_estimate=pl.CostEstimate(
            flops=4 * pixels * channels * hidden_total,
            bytes_accessed=2 * (3 * pixels * channels + 2 * channels * hidden_total),
            transcendentals=2 * pixels * hidden_total,
        ),
    )(
        normed,
        features,
        w_expand,
        b_expand.reshape(1, hidden_total),
        w_reduce,
        b_reduce.reshape(1, channels),
        layer_scale.reshape(1, channels),
        w_query,
    )

def block_pass(
    pieces,
    features,
    dw_kernel,
    dw_bias,
    norm_gain,
    norm_bias,
    w_expand,
    b_expand,
    w_reduce,
    b_reduce,
    layer_scale,
    w_query,
    copies,
):
    tile_rows, tile_cols, channels = features.shape
    normed = conv_norm(features, *pieces, dw_kernel, dw_bias, norm_gain, norm_bias).reshape(
        -1, channels
    )
    summed, queries, sent = mlp(
        normed,
        features.reshape(-1, channels),
        w_expand,
        b_expand,
        w_reduce,
        b_reduce,
        layer_scale,
        w_query,
        tile_cols,
        copies,
    )
    return summed.reshape(tile_rows, tile_cols, channels), queries, sent


def shards(
    features,
    dw_kernel,
    dw_bias,
    norm_gain,
    norm_bias,
    w_expand,
    b_expand,
    w_reduce,
    b_reduce,
    layer_scale,
    w_query,
    w_keyval,
    rel_bias,
    w_out,
):
    tile_rows, tile_cols, channels = features.shape
    head_dim = channels // HEADS
    pieces = halo_pieces(features, 3)
    columns = lax.axis_size("col")
    position = lax.axis_index("col")
    block_out, queries, sent = block_pass(
        pieces,
        features,
        dw_kernel,
        dw_bias,
        norm_gain,
        norm_bias,
        w_expand,
        b_expand,
        w_reduce,
        b_reduce,
        layer_scale,
        w_query,
        columns,
    )
    region_side = tile_rows // 8
    local_count = region_side * region_side
    queries = queries.astype(jnp.bfloat16)
    span_cols = region_side * columns
    key_count = local_count * columns
    band_pooled = lax.all_to_all(sent, "col", 0, 0)
    band_pooled = (
        band_pooled.reshape(columns, region_side, region_side, channels)
        .transpose(1, 0, 2, 3)
        .reshape(key_count, channels)
    )
    band_keyval = jnp.dot(band_pooled, w_keyval, preferred_element_type=jnp.float32).astype(
        jnp.bfloat16
    )
    windows = []
    for query_col in range(region_side):
        first = span_cols - 1 - (position * region_side + query_col)
        windows.append(lax.dynamic_slice_in_dim(rel_bias, first, span_cols, axis=2))
    rows_of = []
    for query_row in range(region_side):
        per_col = [
            w[:, region_side - 1 - query_row : 2 * region_side - 1 - query_row, :] for w in windows
        ]
        rows_of.append(jnp.stack(per_col, axis=1))
    bias_block = jnp.stack(rows_of, axis=1).reshape(HEADS, local_count, key_count)
    query_heads = queries.reshape(local_count, HEADS, head_dim)
    key_heads = band_keyval[:, :channels].reshape(key_count, HEADS, head_dim)
    value_heads = band_keyval[:, channels:].reshape(key_count, HEADS, head_dim)
    scores = (
        jnp.einsum("qhd,khd->hqk", query_heads, key_heads, preferred_element_type=jnp.float32)
        / jnp.sqrt(jnp.float32(head_dim))
        + bias_block
    )
    attn = jax.nn.softmax(scores, axis=-1).astype(jnp.bfloat16)
    context = (
        jnp.einsum("hqk,khd->qhd", attn, value_heads, preferred_element_type=jnp.float32)
        .reshape(local_count, channels)
        .astype(jnp.bfloat16)
    )
    lifted = jnp.dot(context, w_out, preferred_element_type=jnp.float32).reshape(
        region_side, 1, region_side, 1, channels
    )
    spread = jnp.broadcast_to(lifted, (region_side, 8, region_side, 8, channels)).reshape(
        tile_rows, tile_cols, channels
    )
    return (block_out.astype(jnp.float32) + spread).astype(jnp.bfloat16)


def solution(mesh):
    return jax.shard_map(
        shards,
        mesh=mesh,
        in_specs=(
            P("row", "col", None),
            P(),
            P(),
            P(),
            P(),
            P(),
            P(),
            P(),
            P(),
            P(),
            P(),
            P(),
            P(),
            P(),
        ),
        out_specs=P("row", "col", None),
        check_vma=False,
    )
```

```python
import jax
import jax.numpy as jnp
from jax import lax
from jax.sharding import PartitionSpec as P
from jax.experimental import pallas as pl
from jax.experimental.pallas import tpu as pltpu

HEADS = 8


def shifted(piece, axis):
    devices = lax.axis_size(axis)
    up = [(i, i + 1) for i in range(devices - 1)]
    down = [(i + 1, i) for i in range(devices - 1)]
    return lax.ppermute(piece, axis, up), lax.ppermute(piece, axis, down)


def halo_pieces(features, width):
    rows, cols = features.shape[:2]
    top, _ = shifted(features[rows - width :], "row")
    _, bottom = shifted(features[:width], "row")
    last_cols = jnp.concatenate(
        [top[:, cols - width :], features[:, cols - width :], bottom[:, cols - width :]], axis=0
    )
    first_cols = jnp.concatenate([top[:, :width], features[:, :width], bottom[:, :width]], axis=0)
    left, _ = shifted(last_cols, "col")
    _, right = shifted(first_cols, "col")
    return top, bottom, left, right

TAPS = 7
ROW_BLOCK = 8


def conv_norm_kernel(
    c_ref, t_ref, b_ref, l_ref, r_ref, k_ref, db_ref, g_ref, nb_ref, o_ref, kf_ref, sh_ref
):
    tile_rows, tile_cols, channels = o_ref.shape
    halo = t_ref.shape[0]
    rows_p = tile_rows + 2 * halo
    for a in range(TAPS):
        kf_ref[a, pl.ds(0, TAPS), :] = k_ref[a].astype(jnp.float32)

    def put(r, mid):
        row = jnp.concatenate([l_ref[r], mid, r_ref[r]], axis=0).astype(jnp.float32)
        for b in range(TAPS):
            sh_ref[b, r] = row[b : b + tile_cols]

    for r in range(halo):
        put(r, t_ref[r])
        put(rows_p - halo + r, b_ref[r])

    def widen(r, carry):
        put(r, c_ref[r - halo])
        return carry

    lax.fori_loop(halo, rows_p - halo, widen, 0)
    db = db_ref[...]
    g = g_ref[...]
    nb = nb_ref[...]
    lanes = 128
    halves = channels // lanes

    def body(i, carry):
        r0 = pl.multiple_of(i * ROW_BLOCK, ROW_BLOCK)
        for s0 in range(0, tile_cols, 8):
            parts = []
            for h in range(halves):
                lane = pl.ds(h * lanes, lanes)
                acc = jnp.zeros((ROW_BLOCK, 8, lanes), jnp.float32)
                for b in range(TAPS):
                    x = sh_ref[b, pl.ds(r0, ROW_BLOCK + TAPS - 1), pl.ds(s0, 8), lane]
                    for a in range(TAPS):
                        acc = acc + x[a : a + ROW_BLOCK] * kf_ref[a, pl.ds(b, 1), lane]
                parts.append(acc)
            acc = jnp.concatenate(parts, axis=-1) + db
            mean = jnp.mean(acc, axis=-1, keepdims=True)
            cen = acc - mean
            var = jnp.mean(cen * cen, axis=-1, keepdims=True)
            normed = cen * lax.rsqrt(var + 1e-06) * g + nb
            o_ref[pl.ds(r0, ROW_BLOCK), pl.ds(s0, 8), :] = normed.astype(o_ref.dtype)
        return carry

    lax.fori_loop(0, tile_rows // ROW_BLOCK, body, 0)


def conv_norm(centre, top, bottom, left, right, dw_kernel, dw_bias, norm_gain, norm_bias):
    tile_rows, tile_cols, channels = centre.shape
    rows_p = tile_rows + 2 * top.shape[0]
    vmem = pl.BlockSpec(memory_space=pltpu.VMEM)
    return pl.pallas_call(
        conv_norm_kernel,
        out_shape=jax.ShapeDtypeStruct((tile_rows, tile_cols, channels), jnp.bfloat16),
        in_specs=[vmem] * 9,
        out_specs=vmem,
        scratch_shapes=[
            pltpu.VMEM((TAPS, 8, channels), jnp.float32),
            pltpu.VMEM((TAPS, rows_p, tile_cols, channels), jnp.float32),
        ],
        cost_estimate=pl.CostEstimate(
            flops=2 * TAPS * TAPS * tile_rows * tile_cols * channels,
            bytes_accessed=2 * (rows_p * rows_p + tile_rows * tile_cols) * channels,
            transcendentals=tile_rows * tile_cols,
        ),
    )(
        centre,
        top,
        bottom,
        left,
        right,
        dw_kernel,
        dw_bias.reshape(1, channels),
        norm_gain.reshape(1, channels),
        norm_bias.reshape(1, channels),
    )

ERFC_COEFFS = (
    -1.26551223,
    1.00002368,
    0.37409196,
    0.09678418,
    -0.18628806,
    0.27886807,
    -1.13520398,
    1.48851587,
    -0.82215223,
    0.17087277,
)
PIXEL_BLOCK = 256
HIDDEN_BLOCK = 256


def gelu_exact(pre):
    z = jnp.abs(pre) * jnp.float32(0.7071067811865476)
    t = 1.0 / (1.0 + 0.5 * z)
    poly = jnp.float32(ERFC_COEFFS[-1])
    for coeff in ERFC_COEFFS[-2::-1]:
        poly = poly * t + jnp.float32(coeff)
    tail = t * jnp.exp(poly - z * z)
    one_plus_erf = jnp.where(pre >= 0, 2.0 - tail, tail)
    return 0.5 * pre * one_plus_erf


def mlp_kernel(n_ref, f_ref, we_ref, be_ref, wr_ref, br_ref, ls_ref, wq_ref, o_ref, q_ref, s_ref):
    normed = n_ref[...]
    hidden_total = we_ref.shape[1]
    acc = jnp.zeros(o_ref.shape, jnp.float32)
    for h0 in range(0, hidden_total, HIDDEN_BLOCK):
        pre = (
            jnp.dot(normed, we_ref[:, h0 : h0 + HIDDEN_BLOCK], preferred_element_type=jnp.float32)
            + be_ref[:, h0 : h0 + HIDDEN_BLOCK]
        )
        hidden = gelu_exact(pre).astype(jnp.bfloat16)
        acc = acc + jnp.dot(hidden, wr_ref[h0 : h0 + HIDDEN_BLOCK, :], preferred_element_type=jnp.float32)
    reduced = acc + br_ref[...]
    out = (f_ref[...].astype(jnp.float32) + ls_ref[...] * reduced).astype(o_ref.dtype)
    o_ref[...] = out
    pixels, channels = o_ref.shape
    tile_cols = pixels // 8
    per_row = tile_cols // 8
    column_sums = out.astype(jnp.float32).reshape(8, tile_cols, channels).sum(axis=0)
    region_sums = column_sums.reshape(per_row, 8, channels).sum(axis=1)
    pooled = (region_sums * jnp.float32(1.0 / 64.0)).astype(jnp.bfloat16)
    queries = jnp.dot(pooled, wq_ref[...], preferred_element_type=jnp.float32)
    queries = queries.astype(jnp.bfloat16).astype(jnp.float32)
    copies = jnp.broadcast_to(pooled[None], (s_ref.shape[0], per_row, channels))
    step = pl.program_id(0)
    for k in range(s_ref.shape[1] // per_row):

        @pl.when(step == k)
        def _():
            q_ref[pl.ds(k * per_row, per_row), :] = queries
            s_ref[:, pl.ds(k * per_row, per_row), :] = copies


def mlp(normed, features, w_expand, b_expand, w_reduce, b_reduce, layer_scale, w_query, tile_cols, copies):
    pixels, channels = normed.shape
    hidden_total = w_expand.shape[1]
    block = 8 * tile_cols
    steps = pixels // block
    tokens = steps * (tile_cols // 8)
    rows = pl.BlockSpec((block, channels), lambda i: (i, 0))
    whole = lambda shape: pl.BlockSpec(shape, lambda i: (0,) * len(shape))
    return pl.pallas_call(
        mlp_kernel,
        out_shape=(
            jax.ShapeDtypeStruct((pixels, channels), jnp.bfloat16),
            jax.ShapeDtypeStruct((tokens, channels), jnp.float32),
            jax.ShapeDtypeStruct((copies, tokens, channels), jnp.bfloat16),
        ),
        grid=(steps,),
        in_specs=[
            rows,
            rows,
            whole((channels, hidden_total)),
            whole((1, hidden_total)),
            whole((hidden_total, channels)),
            whole((1, channels)),
            whole((1, channels)),
            whole((channels, channels)),
        ],
        out_specs=(rows, whole((tokens, channels)), whole((copies, tokens, channels))),
        cost_estimate=pl.CostEstimate(
            flops=4 * pixels * channels * hidden_total,
            bytes_accessed=2 * (3 * pixels * channels + 2 * channels * hidden_total),
            transcendentals=2 * pixels * hidden_total,
        ),
    )(
        normed,
        features,
        w_expand,
        b_expand.reshape(1, hidden_total),
        w_reduce,
        b_reduce.reshape(1, channels),
        layer_scale.reshape(1, channels),
        w_query,
    )

def attention_kernel(band_ref, wkv_ref, q_ref, bias_ref, wo_ref, bo_ref, o_ref):
    tokens, channels = q_ref.shape
    heads = bias_ref.shape[0]
    head_dim = channels // heads
    keyval = jnp.dot(band_ref[...], wkv_ref[...], preferred_element_type=jnp.float32)
    keyval = keyval.astype(jnp.bfloat16)
    keys = keyval[:, :channels]
    values = keyval[:, channels:]
    queries = q_ref[...]
    head_of = lax.broadcasted_iota(jnp.int32, (1, channels), 1) // head_dim
    zero = jnp.zeros((), jnp.bfloat16)
    context = jnp.zeros((tokens, channels), jnp.float32)
    for h in range(heads):
        mine = head_of == h
        scores = lax.dot_general(
            jnp.where(mine, queries, zero),
            keys,
            (((1,), (1,)), ((), ())),
            preferred_element_type=jnp.float32,
        )
        scores = scores / jnp.sqrt(jnp.float32(head_dim)) + bias_ref[h]
        top = jnp.max(scores, axis=-1, keepdims=True)
        weights = jnp.exp(scores - top)
        attn = (weights / jnp.sum(weights, axis=-1, keepdims=True)).astype(jnp.bfloat16)
        context = context + jnp.dot(
            attn, jnp.where(mine, values, zero), preferred_element_type=jnp.float32
        )
    lifted = jnp.dot(context.astype(jnp.bfloat16), wo_ref[...], preferred_element_type=jnp.float32)
    tile_rows, tile_cols = o_ref.shape[:2]
    per_row = tile_cols // 8
    for i in range(tile_rows // 8):
        spread = jnp.broadcast_to(
            lifted[i * per_row : (i + 1) * per_row][:, None, :], (per_row, 8, channels)
        ).reshape(tile_cols, channels)
        rows = pl.ds(i * 8, 8)
        o_ref[rows] = (bo_ref[rows].astype(jnp.float32) + spread[None]).astype(o_ref.dtype)


def attention(band, w_keyval, queries, bias, w_out, block_out):
    vmem = pl.BlockSpec(memory_space=pltpu.VMEM)
    keys, channels = band.shape
    tokens = queries.shape[0]
    return pl.pallas_call(
        attention_kernel,
        out_shape=jax.ShapeDtypeStruct(block_out.shape, jnp.bfloat16),
        in_specs=[vmem] * 6,
        out_specs=vmem,
        cost_estimate=pl.CostEstimate(
            flops=2 * keys * channels * 2 * channels + 4 * bias.shape[0] * tokens * keys * channels,
            bytes_accessed=2 * (keys * channels + 2 * block_out.size),
            transcendentals=bias.shape[0] * tokens * keys,
        ),
    )(band, w_keyval, queries, bias, w_out, block_out)


def block_pass(
    pieces,
    features,
    dw_kernel,
    dw_bias,
    norm_gain,
    norm_bias,
    w_expand,
    b_expand,
    w_reduce,
    b_reduce,
    layer_scale,
    w_query,
    copies,
):
    tile_rows, tile_cols, channels = features.shape
    normed = conv_norm(features, *pieces, dw_kernel, dw_bias, norm_gain, norm_bias).reshape(
        -1, channels
    )
    summed, queries, sent = mlp(
        normed,
        features.reshape(-1, channels),
        w_expand,
        b_expand,
        w_reduce,
        b_reduce,
        layer_scale,
        w_query,
        tile_cols,
        copies,
    )
    return summed.reshape(tile_rows, tile_cols, channels), queries, sent


def shards(
    features,
    dw_kernel,
    dw_bias,
    norm_gain,
    norm_bias,
    w_expand,
    b_expand,
    w_reduce,
    b_reduce,
    layer_scale,
    w_query,
    w_keyval,
    rel_bias,
    w_out,
):
    tile_rows, tile_cols, channels = features.shape
    head_dim = channels // HEADS
    pieces = halo_pieces(features, 3)
    columns = lax.axis_size("col")
    position = lax.axis_index("col")
    block_out, queries, sent = block_pass(
        pieces,
        features,
        dw_kernel,
        dw_bias,
        norm_gain,
        norm_bias,
        w_expand,
        b_expand,
        w_reduce,
        b_reduce,
        layer_scale,
        w_query,
        columns,
    )
    region_side = tile_rows // 8
    local_count = region_side * region_side
    queries = queries.astype(jnp.bfloat16)
    span_cols = region_side * columns
    key_count = local_count * columns
    band_pooled = lax.all_to_all(sent, "col", 0, 0)
    band_pooled = (
        band_pooled.reshape(columns, region_side, region_side, channels)
        .transpose(1, 0, 2, 3)
        .reshape(key_count, channels)
    )
    windows = []
    for query_col in range(region_side):
        first = span_cols - 1 - (position * region_side + query_col)
        windows.append(lax.dynamic_slice_in_dim(rel_bias, first, span_cols, axis=2))
    rows_of = []
    for query_row in range(region_side):
        per_col = [
            w[:, region_side - 1 - query_row : 2 * region_side - 1 - query_row, :] for w in windows
        ]
        rows_of.append(jnp.stack(per_col, axis=1))
    bias_block = jnp.stack(rows_of, axis=1).reshape(HEADS, local_count, key_count)
    return attention(band_pooled, w_keyval, queries, bias_block, w_out, block_out)


def solution(mesh):
    return jax.shard_map(
        shards,
        mesh=mesh,
        in_specs=(
            P("row", "col", None),
            P(),
            P(),
            P(),
            P(),
            P(),
            P(),
            P(),
            P(),
            P(),
            P(),
            P(),
            P(),
            P(),
        ),
        out_specs=P("row", "col", None),
        check_vma=False,
    )
```

```python
import jax
import jax.numpy as jnp
from jax import lax
from jax.sharding import PartitionSpec as P
from jax.experimental import pallas as pl
from jax.experimental.pallas import tpu as pltpu

HEADS = 8


def shifted(piece, axis):
    devices = lax.axis_size(axis)
    up = [(i, i + 1) for i in range(devices - 1)]
    down = [(i + 1, i) for i in range(devices - 1)]
    return lax.ppermute(piece, axis, up), lax.ppermute(piece, axis, down)


def halo_pieces(features, width):
    rows, cols = features.shape[:2]
    top, _ = shifted(features[rows - width :], "row")
    _, bottom = shifted(features[:width], "row")
    last_cols = jnp.concatenate(
        [top[:, cols - width :], features[:, cols - width :], bottom[:, cols - width :]], axis=0
    )
    first_cols = jnp.concatenate([top[:, :width], features[:, :width], bottom[:, :width]], axis=0)
    left, _ = shifted(last_cols, "col")
    _, right = shifted(first_cols, "col")
    return top, bottom, left, right

TAPS = 7
ROW_BLOCK = 8


def conv_norm_kernel(x_ref, k_ref, db_ref, g_ref, nb_ref, o_ref, kf_ref, sh_ref):
    rows_p = x_ref.shape[0]
    tile_rows, tile_cols, channels = o_ref.shape
    for a in range(TAPS):
        kf_ref[a, pl.ds(0, TAPS), :] = k_ref[a].astype(jnp.float32)

    def widen(r, carry):
        row = x_ref[r].astype(jnp.float32)
        for b in range(TAPS):
            sh_ref[b, r] = row[b : b + tile_cols]
        return carry

    lax.fori_loop(0, rows_p, widen, 0)
    db = db_ref[...]
    g = g_ref[...]
    nb = nb_ref[...]
    lanes = 128
    halves = channels // lanes

    def body(i, carry):
        r0 = pl.multiple_of(i * ROW_BLOCK, ROW_BLOCK)
        for s0 in range(0, tile_cols, 8):
            parts = []
            for h in range(halves):
                lane = pl.ds(h * lanes, lanes)
                acc = jnp.zeros((ROW_BLOCK, 8, lanes), jnp.float32)
                for b in range(TAPS):
                    x = sh_ref[b, pl.ds(r0, ROW_BLOCK + TAPS - 1), pl.ds(s0, 8), lane]
                    for a in range(TAPS):
                        acc = acc + x[a : a + ROW_BLOCK] * kf_ref[a, pl.ds(b, 1), lane]
                parts.append(acc)
            acc = jnp.concatenate(parts, axis=-1) + db
            mean = jnp.mean(acc, axis=-1, keepdims=True)
            cen = acc - mean
            var = jnp.mean(cen * cen, axis=-1, keepdims=True)
            normed = cen * lax.rsqrt(var + 1e-06) * g + nb
            o_ref[pl.ds(r0, ROW_BLOCK), pl.ds(s0, 8), :] = normed.astype(o_ref.dtype)
        return carry

    lax.fori_loop(0, tile_rows // ROW_BLOCK, body, 0)


def conv_norm(padded, dw_kernel, dw_bias, norm_gain, norm_bias, tile_rows, tile_cols):
    rows_p, cols_p, channels = padded.shape
    vmem = pl.BlockSpec(memory_space=pltpu.VMEM)
    return pl.pallas_call(
        conv_norm_kernel,
        out_shape=jax.ShapeDtypeStruct((tile_rows, tile_cols, channels), jnp.bfloat16),
        in_specs=[vmem] * 5,
        out_specs=vmem,
        scratch_shapes=[
            pltpu.VMEM((TAPS, 8, channels), jnp.float32),
            pltpu.VMEM((TAPS, rows_p, tile_cols, channels), jnp.float32),
        ],
        cost_estimate=pl.CostEstimate(
            flops=2 * TAPS * TAPS * tile_rows * tile_cols * channels,
            bytes_accessed=2 * (rows_p * cols_p + tile_rows * tile_cols) * channels,
            transcendentals=tile_rows * tile_cols,
        ),
    )(
        padded,
        dw_kernel,
        dw_bias.reshape(1, channels),
        norm_gain.reshape(1, channels),
        norm_bias.reshape(1, channels),
    )


ERFC_COEFFS = (
    -1.26551223,
    1.00002368,
    0.37409196,
    0.09678418,
    -0.18628806,
    0.27886807,
    -1.13520398,
    1.48851587,
    -0.82215223,
    0.17087277,
)
PIXEL_BLOCK = 256
HIDDEN_BLOCK = 256


def gelu_exact(pre):
    z = jnp.abs(pre) * jnp.float32(0.7071067811865476)
    t = 1.0 / (1.0 + 0.5 * z)
    poly = jnp.float32(ERFC_COEFFS[-1])
    for coeff in ERFC_COEFFS[-2::-1]:
        poly = poly * t + jnp.float32(coeff)
    tail = t * jnp.exp(poly - z * z)
    one_plus_erf = jnp.where(pre >= 0, 2.0 - tail, tail)
    return 0.5 * pre * one_plus_erf


def mlp_kernel(n_ref, f_ref, we_ref, be_ref, wr_ref, br_ref, ls_ref, wq_ref, o_ref, q_ref, s_ref):
    normed = n_ref[...]
    hidden_total = we_ref.shape[1]
    acc = jnp.zeros(o_ref.shape, jnp.float32)
    for h0 in range(0, hidden_total, HIDDEN_BLOCK):
        pre = (
            jnp.dot(normed, we_ref[:, h0 : h0 + HIDDEN_BLOCK], preferred_element_type=jnp.float32)
            + be_ref[:, h0 : h0 + HIDDEN_BLOCK]
        )
        hidden = gelu_exact(pre).astype(jnp.bfloat16)
        acc = acc + jnp.dot(hidden, wr_ref[h0 : h0 + HIDDEN_BLOCK, :], preferred_element_type=jnp.float32)
    reduced = acc + br_ref[...]
    out = (f_ref[...].astype(jnp.float32) + ls_ref[...] * reduced).astype(o_ref.dtype)
    o_ref[...] = out
    pixels, channels = o_ref.shape
    tile_cols = pixels // 8
    per_row = tile_cols // 8
    column_sums = out.astype(jnp.float32).reshape(8, tile_cols, channels).sum(axis=0)
    region_sums = column_sums.reshape(per_row, 8, channels).sum(axis=1)
    pooled = (region_sums * jnp.float32(1.0 / 64.0)).astype(jnp.bfloat16)
    queries = jnp.dot(pooled, wq_ref[...], preferred_element_type=jnp.float32)
    queries = queries.astype(jnp.bfloat16).astype(jnp.float32)
    copies = jnp.broadcast_to(pooled[None], (s_ref.shape[0], per_row, channels))
    step = pl.program_id(0)
    for k in range(s_ref.shape[1] // per_row):

        @pl.when(step == k)
        def _():
            q_ref[pl.ds(k * per_row, per_row), :] = queries
            s_ref[:, pl.ds(k * per_row, per_row), :] = copies


def mlp(normed, features, w_expand, b_expand, w_reduce, b_reduce, layer_scale, w_query, tile_cols, copies):
    pixels, channels = normed.shape
    hidden_total = w_expand.shape[1]
    block = 8 * tile_cols
    steps = pixels // block
    tokens = steps * (tile_cols // 8)
    rows = pl.BlockSpec((block, channels), lambda i: (i, 0))
    whole = lambda shape: pl.BlockSpec(shape, lambda i: (0,) * len(shape))
    return pl.pallas_call(
        mlp_kernel,
        out_shape=(
            jax.ShapeDtypeStruct((pixels, channels), jnp.bfloat16),
            jax.ShapeDtypeStruct((tokens, channels), jnp.float32),
            jax.ShapeDtypeStruct((copies, tokens, channels), jnp.bfloat16),
        ),
        grid=(steps,),
        in_specs=[
            rows,
            rows,
            whole((channels, hidden_total)),
            whole((1, hidden_total)),
            whole((hidden_total, channels)),
            whole((1, channels)),
            whole((1, channels)),
            whole((channels, channels)),
        ],
        out_specs=(rows, whole((tokens, channels)), whole((copies, tokens, channels))),
        cost_estimate=pl.CostEstimate(
            flops=4 * pixels * channels * hidden_total,
            bytes_accessed=2 * (3 * pixels * channels + 2 * channels * hidden_total),
            transcendentals=2 * pixels * hidden_total,
        ),
    )(
        normed,
        features,
        w_expand,
        b_expand.reshape(1, hidden_total),
        w_reduce,
        b_reduce.reshape(1, channels),
        layer_scale.reshape(1, channels),
        w_query,
    )

def block_pass(
    pieces,
    features,
    dw_kernel,
    dw_bias,
    norm_gain,
    norm_bias,
    w_expand,
    b_expand,
    w_reduce,
    b_reduce,
    layer_scale,
    w_query,
    copies,
):
    tile_rows, tile_cols, channels = features.shape
    top, bottom, left, right = pieces
    extended = jnp.concatenate([top, features, bottom], axis=0)
    padded = jnp.concatenate(
        [left, extended, right, jnp.zeros_like(right)[:, : -(tile_cols + 3 * 3) % 8]], axis=1
    )
    normed = conv_norm(
        padded, dw_kernel, dw_bias, norm_gain, norm_bias, tile_rows, tile_cols
    ).reshape(-1, channels)
    summed, queries, sent = mlp(
        normed,
        features.reshape(-1, channels),
        w_expand,
        b_expand,
        w_reduce,
        b_reduce,
        layer_scale,
        w_query,
        tile_cols,
        copies,
    )
    return summed.reshape(tile_rows, tile_cols, channels), queries, sent


def shards(
    features,
    dw_kernel,
    dw_bias,
    norm_gain,
    norm_bias,
    w_expand,
    b_expand,
    w_reduce,
    b_reduce,
    layer_scale,
    w_query,
    w_keyval,
    rel_bias,
    w_out,
):
    tile_rows, tile_cols, channels = features.shape
    head_dim = channels // HEADS
    pieces = halo_pieces(features, 3)
    columns = lax.axis_size("col")
    position = lax.axis_index("col")
    block_out, queries, sent = block_pass(
        pieces,
        features,
        dw_kernel,
        dw_bias,
        norm_gain,
        norm_bias,
        w_expand,
        b_expand,
        w_reduce,
        b_reduce,
        layer_scale,
        w_query,
        columns,
    )
    region_side = tile_rows // 8
    local_count = region_side * region_side
    queries = queries.astype(jnp.bfloat16)
    span_cols = region_side * columns
    key_count = local_count * columns
    band_pooled = lax.all_to_all(sent, "col", 0, 0)
    band_pooled = (
        band_pooled.reshape(columns, region_side, region_side, channels)
        .transpose(1, 0, 2, 3)
        .reshape(key_count, channels)
    )
    band_keyval = jnp.dot(band_pooled, w_keyval, preferred_element_type=jnp.float32).astype(
        jnp.bfloat16
    )
    windows = []
    for query_col in range(region_side):
        first = span_cols - 1 - (position * region_side + query_col)
        windows.append(lax.dynamic_slice_in_dim(rel_bias, first, span_cols, axis=2))
    rows_of = []
    for query_row in range(region_side):
        per_col = [
            w[:, region_side - 1 - query_row : 2 * region_side - 1 - query_row, :] for w in windows
        ]
        rows_of.append(jnp.stack(per_col, axis=1))
    bias_block = jnp.stack(rows_of, axis=1).reshape(HEADS, local_count, key_count)
    query_heads = queries.reshape(local_count, HEADS, head_dim)
    key_heads = band_keyval[:, :channels].reshape(key_count, HEADS, head_dim)
    value_heads = band_keyval[:, channels:].reshape(key_count, HEADS, head_dim)
    scores = (
        jnp.einsum("qhd,khd->hqk", query_heads, key_heads, preferred_element_type=jnp.float32)
        / jnp.sqrt(jnp.float32(head_dim))
        + bias_block
    )
    attn = jax.nn.softmax(scores, axis=-1).astype(jnp.bfloat16)
    context = (
        jnp.einsum("hqk,khd->qhd", attn, value_heads, preferred_element_type=jnp.float32)
        .reshape(local_count, channels)
        .astype(jnp.bfloat16)
    )
    lifted = jnp.dot(context, w_out, preferred_element_type=jnp.float32).reshape(
        region_side, 1, region_side, 1, channels
    )
    spread = jnp.broadcast_to(lifted, (region_side, 8, region_side, 8, channels)).reshape(
        tile_rows, tile_cols, channels
    )
    return (block_out.astype(jnp.float32) + spread).astype(jnp.bfloat16)


def solution(mesh):
    return jax.shard_map(
        shards,
        mesh=mesh,
        in_specs=(
            P("row", "col", None),
            P(),
            P(),
            P(),
            P(),
            P(),
            P(),
            P(),
            P(),
            P(),
            P(),
            P(),
            P(),
            P(),
        ),
        out_specs=P("row", "col", None),
        check_vma=False,
    )
```

```python
import jax
import jax.numpy as jnp
from jax import lax
from jax.sharding import PartitionSpec as P
from jax.experimental import pallas as pl
from jax.experimental.pallas import tpu as pltpu

HEADS = 8


def shifted(piece, axis):
    devices = lax.axis_size(axis)
    up = [(i, i + 1) for i in range(devices - 1)]
    down = [(i + 1, i) for i in range(devices - 1)]
    return lax.ppermute(piece, axis, up), lax.ppermute(piece, axis, down)


def halo_pieces(features, width):
    rows, cols = features.shape[:2]
    top, _ = shifted(features[rows - width :], "row")
    _, bottom = shifted(features[:width], "row")
    last_cols = jnp.concatenate(
        [top[:, cols - width :], features[:, cols - width :], bottom[:, cols - width :]], axis=0
    )
    first_cols = jnp.concatenate([top[:, :width], features[:, :width], bottom[:, :width]], axis=0)
    left, _ = shifted(last_cols, "col")
    _, right = shifted(first_cols, "col")
    return top, bottom, left, right

TAPS = 7
ROW_BLOCK = 8


def conv_norm_kernel(x_ref, k_ref, db_ref, g_ref, nb_ref, o_ref, kf_ref, sh_ref):
    rows_p = x_ref.shape[0]
    tile_rows, tile_cols, channels = o_ref.shape
    for a in range(TAPS):
        taps = k_ref[a].astype(jnp.float32)
        for b in range(TAPS):
            kf_ref[b, a] = jnp.broadcast_to(taps[b : b + 1], (8, channels))

    def widen(r, carry):
        row = x_ref[r].astype(jnp.float32)
        for b in range(TAPS):
            sh_ref[b, r] = row[b : b + tile_cols]
        return carry

    lax.fori_loop(0, rows_p, widen, 0)
    db = db_ref[...]
    g = g_ref[...]
    nb = nb_ref[...]
    lanes = 128
    halves = channels // lanes

    col_blocks = tile_cols // 8

    def body(i, carry):
        r0 = pl.multiple_of((i // col_blocks) * ROW_BLOCK, ROW_BLOCK)
        s0 = pl.multiple_of((i % col_blocks) * 8, 8)

        def tap_column(b, accs):
            new = []
            for h in range(halves):
                lane = pl.ds(h * lanes, lanes)
                x = sh_ref[b, pl.ds(r0, ROW_BLOCK + TAPS - 1), pl.ds(s0, 8), lane]
                acc = accs[h]
                for a in range(TAPS):
                    acc = acc + x[a : a + ROW_BLOCK] * kf_ref[b, a, :, lane][None]
                new.append(acc)
            return tuple(new)

        zero = jnp.zeros((ROW_BLOCK, 8, lanes), jnp.float32)
        parts = lax.fori_loop(0, TAPS, tap_column, (zero,) * halves)
        acc = jnp.concatenate(parts, axis=-1) + db
        mean = jnp.mean(acc, axis=-1, keepdims=True)
        cen = acc - mean
        var = jnp.mean(cen * cen, axis=-1, keepdims=True)
        normed = cen * lax.rsqrt(var + 1e-06) * g + nb
        o_ref[pl.ds(r0, ROW_BLOCK), pl.ds(s0, 8), :] = normed.astype(o_ref.dtype)
        return carry

    lax.fori_loop(0, (tile_rows // ROW_BLOCK) * col_blocks, body, 0)


def conv_norm(padded, dw_kernel, dw_bias, norm_gain, norm_bias, tile_rows, tile_cols):
    rows_p, cols_p, channels = padded.shape
    vmem = pl.BlockSpec(memory_space=pltpu.VMEM)
    return pl.pallas_call(
        conv_norm_kernel,
        out_shape=jax.ShapeDtypeStruct((tile_rows, tile_cols, channels), jnp.bfloat16),
        in_specs=[vmem] * 5,
        out_specs=vmem,
        scratch_shapes=[
            pltpu.VMEM((TAPS, TAPS, 8, channels), jnp.float32),
            pltpu.VMEM((TAPS, rows_p, tile_cols, channels), jnp.float32),
        ],
        cost_estimate=pl.CostEstimate(
            flops=2 * TAPS * TAPS * tile_rows * tile_cols * channels,
            bytes_accessed=2 * (rows_p * cols_p + tile_rows * tile_cols) * channels,
            transcendentals=tile_rows * tile_cols,
        ),
    )(
        padded,
        dw_kernel,
        dw_bias.reshape(1, channels),
        norm_gain.reshape(1, channels),
        norm_bias.reshape(1, channels),
    )


ERFC_COEFFS = (
    -1.26551223,
    1.00002368,
    0.37409196,
    0.09678418,
    -0.18628806,
    0.27886807,
    -1.13520398,
    1.48851587,
    -0.82215223,
    0.17087277,
)
PIXEL_BLOCK = 256
HIDDEN_BLOCK = 256


def gelu_exact(pre):
    z = jnp.abs(pre) * jnp.float32(0.7071067811865476)
    t = 1.0 / (1.0 + 0.5 * z)
    poly = jnp.float32(ERFC_COEFFS[-1])
    for coeff in ERFC_COEFFS[-2::-1]:
        poly = poly * t + jnp.float32(coeff)
    tail = t * jnp.exp(poly - z * z)
    one_plus_erf = jnp.where(pre >= 0, 2.0 - tail, tail)
    return 0.5 * pre * one_plus_erf


def mlp_kernel(n_ref, f_ref, we_ref, be_ref, wr_ref, br_ref, ls_ref, wq_ref, o_ref, q_ref, s_ref):
    normed = n_ref[...]
    hidden_total = we_ref.shape[1]
    acc = jnp.zeros(o_ref.shape, jnp.float32)
    for h0 in range(0, hidden_total, HIDDEN_BLOCK):
        pre = (
            jnp.dot(normed, we_ref[:, h0 : h0 + HIDDEN_BLOCK], preferred_element_type=jnp.float32)
            + be_ref[:, h0 : h0 + HIDDEN_BLOCK]
        )
        hidden = gelu_exact(pre).astype(jnp.bfloat16)
        acc = acc + jnp.dot(hidden, wr_ref[h0 : h0 + HIDDEN_BLOCK, :], preferred_element_type=jnp.float32)
    reduced = acc + br_ref[...]
    out = (f_ref[...].astype(jnp.float32) + ls_ref[...] * reduced).astype(o_ref.dtype)
    o_ref[...] = out
    pixels, channels = o_ref.shape
    tile_cols = pixels // 8
    per_row = tile_cols // 8
    column_sums = out.astype(jnp.float32).reshape(8, tile_cols, channels).sum(axis=0)
    region_sums = column_sums.reshape(per_row, 8, channels).sum(axis=1)
    pooled = (region_sums * jnp.float32(1.0 / 64.0)).astype(jnp.bfloat16)
    queries = jnp.dot(pooled, wq_ref[...], preferred_element_type=jnp.float32)
    queries = queries.astype(jnp.bfloat16).astype(jnp.float32)
    copies = jnp.broadcast_to(pooled[None], (s_ref.shape[0], per_row, channels))
    step = pl.program_id(0)
    for k in range(s_ref.shape[1] // per_row):

        @pl.when(step == k)
        def _():
            q_ref[pl.ds(k * per_row, per_row), :] = queries
            s_ref[:, pl.ds(k * per_row, per_row), :] = copies


def mlp(normed, features, w_expand, b_expand, w_reduce, b_reduce, layer_scale, w_query, tile_cols, copies):
    pixels, channels = normed.shape
    hidden_total = w_expand.shape[1]
    block = 8 * tile_cols
    steps = pixels // block
    tokens = steps * (tile_cols // 8)
    rows = pl.BlockSpec((block, channels), lambda i: (i, 0))
    whole = lambda shape: pl.BlockSpec(shape, lambda i: (0,) * len(shape))
    return pl.pallas_call(
        mlp_kernel,
        out_shape=(
            jax.ShapeDtypeStruct((pixels, channels), jnp.bfloat16),
            jax.ShapeDtypeStruct((tokens, channels), jnp.float32),
            jax.ShapeDtypeStruct((copies, tokens, channels), jnp.bfloat16),
        ),
        grid=(steps,),
        in_specs=[
            rows,
            rows,
            whole((channels, hidden_total)),
            whole((1, hidden_total)),
            whole((hidden_total, channels)),
            whole((1, channels)),
            whole((1, channels)),
            whole((channels, channels)),
        ],
        out_specs=(rows, whole((tokens, channels)), whole((copies, tokens, channels))),
        cost_estimate=pl.CostEstimate(
            flops=4 * pixels * channels * hidden_total,
            bytes_accessed=2 * (3 * pixels * channels + 2 * channels * hidden_total),
            transcendentals=2 * pixels * hidden_total,
        ),
    )(
        normed,
        features,
        w_expand,
        b_expand.reshape(1, hidden_total),
        w_reduce,
        b_reduce.reshape(1, channels),
        layer_scale.reshape(1, channels),
        w_query,
    )

def block_pass(
    pieces,
    features,
    dw_kernel,
    dw_bias,
    norm_gain,
    norm_bias,
    w_expand,
    b_expand,
    w_reduce,
    b_reduce,
    layer_scale,
    w_query,
    copies,
):
    tile_rows, tile_cols, channels = features.shape
    top, bottom, left, right = pieces
    extended = jnp.concatenate([top, features, bottom], axis=0)
    padded = jnp.concatenate(
        [left, extended, right, jnp.zeros_like(right)[:, : -(tile_cols + 3 * 3) % 8]], axis=1
    )
    normed = conv_norm(
        padded, dw_kernel, dw_bias, norm_gain, norm_bias, tile_rows, tile_cols
    ).reshape(-1, channels)
    summed, queries, sent = mlp(
        normed,
        features.reshape(-1, channels),
        w_expand,
        b_expand,
        w_reduce,
        b_reduce,
        layer_scale,
        w_query,
        tile_cols,
        copies,
    )
    return summed.reshape(tile_rows, tile_cols, channels), queries, sent


def shards(
    features,
    dw_kernel,
    dw_bias,
    norm_gain,
    norm_bias,
    w_expand,
    b_expand,
    w_reduce,
    b_reduce,
    layer_scale,
    w_query,
    w_keyval,
    rel_bias,
    w_out,
):
    tile_rows, tile_cols, channels = features.shape
    head_dim = channels // HEADS
    pieces = halo_pieces(features, 3)
    columns = lax.axis_size("col")
    position = lax.axis_index("col")
    block_out, queries, sent = block_pass(
        pieces,
        features,
        dw_kernel,
        dw_bias,
        norm_gain,
        norm_bias,
        w_expand,
        b_expand,
        w_reduce,
        b_reduce,
        layer_scale,
        w_query,
        columns,
    )
    region_side = tile_rows // 8
    local_count = region_side * region_side
    queries = queries.astype(jnp.bfloat16)
    span_cols = region_side * columns
    key_count = local_count * columns
    band_pooled = lax.all_to_all(sent, "col", 0, 0)
    band_pooled = (
        band_pooled.reshape(columns, region_side, region_side, channels)
        .transpose(1, 0, 2, 3)
        .reshape(key_count, channels)
    )
    band_keyval = jnp.dot(band_pooled, w_keyval, preferred_element_type=jnp.float32).astype(
        jnp.bfloat16
    )
    window_all = lax.dynamic_slice_in_dim(
        rel_bias, span_cols - region_side - position * region_side, span_cols + region_side - 1, axis=2
    )
    windows = [
        window_all[:, :, region_side - 1 - query_col : region_side - 1 - query_col + span_cols]
        for query_col in range(region_side)
    ]
    rows_of = []
    for query_row in range(region_side):
        per_col = [
            w[:, region_side - 1 - query_row : 2 * region_side - 1 - query_row, :] for w in windows
        ]
        rows_of.append(jnp.stack(per_col, axis=1))
    bias_block = jnp.stack(rows_of, axis=1).reshape(HEADS, local_count, key_count)
    query_heads = queries.reshape(local_count, HEADS, head_dim)
    key_heads = band_keyval[:, :channels].reshape(key_count, HEADS, head_dim)
    value_heads = band_keyval[:, channels:].reshape(key_count, HEADS, head_dim)
    scores = (
        jnp.einsum("qhd,khd->hqk", query_heads, key_heads, preferred_element_type=jnp.float32)
        / jnp.sqrt(jnp.float32(head_dim))
        + bias_block
    )
    attn = jax.nn.softmax(scores, axis=-1).astype(jnp.bfloat16)
    context = (
        jnp.einsum("hqk,khd->qhd", attn, value_heads, preferred_element_type=jnp.float32)
        .reshape(local_count, channels)
        .astype(jnp.bfloat16)
    )
    lifted = jnp.dot(context, w_out, preferred_element_type=jnp.float32).reshape(
        region_side, 1, region_side, 1, channels
    )
    spread = jnp.broadcast_to(lifted, (region_side, 8, region_side, 8, channels)).reshape(
        tile_rows, tile_cols, channels
    )
    return (block_out.astype(jnp.float32) + spread).astype(jnp.bfloat16)


def solution(mesh):
    return jax.shard_map(
        shards,
        mesh=mesh,
        in_specs=(
            P("row", "col", None),
            P(),
            P(),
            P(),
            P(),
            P(),
            P(),
            P(),
            P(),
            P(),
            P(),
            P(),
            P(),
            P(),
        ),
        out_specs=P("row", "col", None),
        check_vma=False,
    )
```

```python
import jax
import jax.numpy as jnp
from jax import lax
from jax.sharding import PartitionSpec as P
from jax.experimental import pallas as pl
from jax.experimental.pallas import tpu as pltpu

HEADS = 8


def shifted(piece, axis):
    devices = lax.axis_size(axis)
    up = [(i, i + 1) for i in range(devices - 1)]
    down = [(i + 1, i) for i in range(devices - 1)]
    return lax.ppermute(piece, axis, up), lax.ppermute(piece, axis, down)


def halo_pieces(features, width):
    rows, cols = features.shape[:2]
    top, _ = shifted(features[rows - width :], "row")
    _, bottom = shifted(features[:width], "row")
    last_cols = jnp.concatenate(
        [top[:, cols - width :], features[:, cols - width :], bottom[:, cols - width :]], axis=0
    )
    first_cols = jnp.concatenate([top[:, :width], features[:, :width], bottom[:, :width]], axis=0)
    left, _ = shifted(last_cols, "col")
    _, right = shifted(first_cols, "col")
    return top, bottom, left, right

TAPS = 7
ROW_BLOCK = 8


def conv_norm_kernel(x_ref, k_ref, db_ref, g_ref, nb_ref, o_ref, kf_ref, sh_ref):
    rows_p = x_ref.shape[0]
    tile_rows, tile_cols, channels = o_ref.shape
    for a in range(TAPS):
        kf_ref[a, pl.ds(0, TAPS), :] = k_ref[a].astype(jnp.float32)

    def widen(r, carry):
        row = x_ref[r].astype(jnp.float32)
        for b in range(TAPS):
            sh_ref[b, r] = row[b : b + tile_cols]
        return carry

    lax.fori_loop(0, rows_p, widen, 0)
    db = db_ref[...]
    g = g_ref[...]
    nb = nb_ref[...]
    lanes = 128
    halves = channels // lanes

    def body(i, carry):
        r0 = pl.multiple_of(i * ROW_BLOCK, ROW_BLOCK)
        for s0 in range(0, tile_cols, 8):
            parts = []
            for h in range(halves):
                lane = pl.ds(h * lanes, lanes)
                acc = jnp.zeros((ROW_BLOCK, 8, lanes), jnp.float32)
                for b in range(TAPS):
                    x = sh_ref[b, pl.ds(r0, ROW_BLOCK + TAPS - 1), pl.ds(s0, 8), lane]
                    for a in range(TAPS):
                        acc = acc + x[a : a + ROW_BLOCK] * kf_ref[a, pl.ds(b, 1), lane]
                parts.append(acc)
            acc = jnp.concatenate(parts, axis=-1) + db
            mean = jnp.mean(acc, axis=-1, keepdims=True)
            cen = acc - mean
            var = jnp.mean(cen * cen, axis=-1, keepdims=True)
            normed = cen * lax.rsqrt(var + 1e-06) * g + nb
            o_ref[pl.ds(r0, ROW_BLOCK), pl.ds(s0, 8), :] = normed.astype(o_ref.dtype)
        return carry

    lax.fori_loop(0, tile_rows // ROW_BLOCK, body, 0)

ERFC_COEFFS = (
    -1.26551223,
    1.00002368,
    0.37409196,
    0.09678418,
    -0.18628806,
    0.27886807,
    -1.13520398,
    1.48851587,
    -0.82215223,
    0.17087277,
)
PIXEL_BLOCK = 256
HIDDEN_BLOCK = 256


def gelu_exact(pre):
    z = jnp.abs(pre) * jnp.float32(0.7071067811865476)
    t = 1.0 / (1.0 + 0.5 * z)
    poly = jnp.float32(ERFC_COEFFS[-1])
    for coeff in ERFC_COEFFS[-2::-1]:
        poly = poly * t + jnp.float32(coeff)
    tail = t * jnp.exp(poly - z * z)
    one_plus_erf = jnp.where(pre >= 0, 2.0 - tail, tail)
    return 0.5 * pre * one_plus_erf


def mlp_block(normed, features, we_ref, be_ref, wr_ref, br_ref, ls_ref, out_dtype):
    hidden_total = we_ref.shape[1]
    acc = jnp.zeros(features.shape, jnp.float32)
    for h0 in range(0, hidden_total, HIDDEN_BLOCK):
        pre = (
            jnp.dot(normed, we_ref[:, h0 : h0 + HIDDEN_BLOCK], preferred_element_type=jnp.float32)
            + be_ref[:, h0 : h0 + HIDDEN_BLOCK]
        )
        hidden = gelu_exact(pre).astype(jnp.bfloat16)
        acc = acc + jnp.dot(hidden, wr_ref[h0 : h0 + HIDDEN_BLOCK, :], preferred_element_type=jnp.float32)
    reduced = acc + br_ref[...]
    return (features.astype(jnp.float32) + ls_ref[...] * reduced).astype(out_dtype)


def region_tokens(out, wq_ref, copies):
    pixels, channels = out.shape
    tile_cols = pixels // 8
    per_row = tile_cols // 8
    column_sums = out.astype(jnp.float32).reshape(8, tile_cols, channels).sum(axis=0)
    region_sums = column_sums.reshape(per_row, 8, channels).sum(axis=1)
    pooled = (region_sums * jnp.float32(1.0 / 64.0)).astype(jnp.bfloat16)
    queries = jnp.dot(pooled, wq_ref[...], preferred_element_type=jnp.float32)
    queries = queries.astype(jnp.bfloat16).astype(jnp.float32)
    return queries, jnp.broadcast_to(pooled[None], (copies, per_row, channels))


def block_kernel(
    x_ref, k_ref, db_ref, g_ref, nb_ref, f_ref, we_hbm, be_ref, wr_hbm, br_ref, ls_ref, wq_hbm,
    o_ref, q_ref, s_ref, kf_ref, sh_ref, n_ref, we_ref, wr_ref, wq_ref, sem,
):
    loads = [
        pltpu.make_async_copy(source, target, sem.at[i])
        for i, (source, target) in enumerate(((we_hbm, we_ref), (wr_hbm, wr_ref), (wq_hbm, wq_ref)))
    ]
    for load in loads:
        load.start()
    conv_norm_kernel(x_ref, k_ref, db_ref, g_ref, nb_ref, n_ref, kf_ref, sh_ref)
    for load in loads:
        load.wait()
    tile_rows, tile_cols, channels = n_ref.shape
    per_row = tile_cols // 8
    block = 8 * tile_cols
    for step in range(tile_rows // 8):
        rows = pl.ds(step * block, block)
        normed = n_ref[pl.ds(step * 8, 8)].reshape(block, channels)
        out = mlp_block(normed, f_ref[rows], we_ref, be_ref, wr_ref, br_ref, ls_ref, o_ref.dtype)
        o_ref[rows] = out
        queries, copies = region_tokens(out, wq_ref, s_ref.shape[0])
        q_ref[pl.ds(step * per_row, per_row), :] = queries
        s_ref[:, pl.ds(step * per_row, per_row), :] = copies


def block_call(
    padded, features, dw_kernel, dw_bias, norm_gain, norm_bias, w_expand, b_expand, w_reduce,
    b_reduce, layer_scale, w_query, copies,
):
    rows_p, cols_p, channels = padded.shape
    tile_rows, tile_cols = features.shape[:2]
    pixels = tile_rows * tile_cols
    hidden_total = w_expand.shape[1]
    tokens = pixels // 64
    vmem = pl.BlockSpec(memory_space=pltpu.VMEM)
    anywhere = pl.BlockSpec(memory_space=pl.ANY)
    return pl.pallas_call(
        block_kernel,
        out_shape=(
            jax.ShapeDtypeStruct((pixels, channels), jnp.bfloat16),
            jax.ShapeDtypeStruct((tokens, channels), jnp.float32),
            jax.ShapeDtypeStruct((copies, tokens, channels), jnp.bfloat16),
        ),
        in_specs=[vmem] * 6 + [anywhere, vmem, anywhere, vmem, vmem, anywhere],
        out_specs=(vmem, vmem, vmem),
        scratch_shapes=[
            pltpu.VMEM((TAPS, 8, channels), jnp.float32),
            pltpu.VMEM((TAPS, rows_p, tile_cols, channels), jnp.float32),
            pltpu.VMEM((tile_rows, tile_cols, channels), jnp.bfloat16),
            pltpu.VMEM((channels, hidden_total), jnp.bfloat16),
            pltpu.VMEM((hidden_total, channels), jnp.bfloat16),
            pltpu.VMEM((channels, channels), jnp.bfloat16),
            pltpu.SemaphoreType.DMA((3,)),
        ],
        cost_estimate=pl.CostEstimate(
            flops=2 * TAPS * TAPS * pixels * channels + 4 * pixels * channels * hidden_total,
            bytes_accessed=2 * (rows_p * cols_p * channels + 2 * pixels * channels + 2 * channels * hidden_total),
            transcendentals=2 * pixels * hidden_total,
        ),
    )(
        padded,
        dw_kernel,
        dw_bias.reshape(1, channels),
        norm_gain.reshape(1, channels),
        norm_bias.reshape(1, channels),
        features.reshape(pixels, channels),
        w_expand,
        b_expand.reshape(1, hidden_total),
        w_reduce,
        b_reduce.reshape(1, channels),
        layer_scale.reshape(1, channels),
        w_query,
    )

def block_pass(
    pieces,
    features,
    dw_kernel,
    dw_bias,
    norm_gain,
    norm_bias,
    w_expand,
    b_expand,
    w_reduce,
    b_reduce,
    layer_scale,
    w_query,
    copies,
):
    tile_rows, tile_cols, channels = features.shape
    top, bottom, left, right = pieces
    extended = jnp.concatenate([top, features, bottom], axis=0)
    padded = jnp.concatenate(
        [left, extended, right, jnp.zeros_like(right)[:, : -(tile_cols + 3 * 3) % 8]], axis=1
    )
    summed, queries, sent = block_call(
        padded,
        features,
        dw_kernel,
        dw_bias,
        norm_gain,
        norm_bias,
        w_expand,
        b_expand,
        w_reduce,
        b_reduce,
        layer_scale,
        w_query,
        copies,
    )
    return summed.reshape(tile_rows, tile_cols, channels), queries, sent


def shards(
    features,
    dw_kernel,
    dw_bias,
    norm_gain,
    norm_bias,
    w_expand,
    b_expand,
    w_reduce,
    b_reduce,
    layer_scale,
    w_query,
    w_keyval,
    rel_bias,
    w_out,
):
    tile_rows, tile_cols, channels = features.shape
    head_dim = channels // HEADS
    pieces = halo_pieces(features, 3)
    columns = lax.axis_size("col")
    position = lax.axis_index("col")
    block_out, queries, sent = block_pass(
        pieces,
        features,
        dw_kernel,
        dw_bias,
        norm_gain,
        norm_bias,
        w_expand,
        b_expand,
        w_reduce,
        b_reduce,
        layer_scale,
        w_query,
        columns,
    )
    region_side = tile_rows // 8
    local_count = region_side * region_side
    queries = queries.astype(jnp.bfloat16)
    span_cols = region_side * columns
    key_count = local_count * columns
    band_pooled = lax.all_to_all(sent, "col", 0, 0)
    band_pooled = (
        band_pooled.reshape(columns, region_side, region_side, channels)
        .transpose(1, 0, 2, 3)
        .reshape(key_count, channels)
    )
    band_keyval = jnp.dot(band_pooled, w_keyval, preferred_element_type=jnp.float32).astype(
        jnp.bfloat16
    )
    windows = []
    for query_col in range(region_side):
        first = span_cols - 1 - (position * region_side + query_col)
        windows.append(lax.dynamic_slice_in_dim(rel_bias, first, span_cols, axis=2))
    rows_of = []
    for query_row in range(region_side):
        per_col = [
            w[:, region_side - 1 - query_row : 2 * region_side - 1 - query_row, :] for w in windows
        ]
        rows_of.append(jnp.stack(per_col, axis=1))
    bias_block = jnp.stack(rows_of, axis=1).reshape(HEADS, local_count, key_count)
    query_heads = queries.reshape(local_count, HEADS, head_dim)
    key_heads = band_keyval[:, :channels].reshape(key_count, HEADS, head_dim)
    value_heads = band_keyval[:, channels:].reshape(key_count, HEADS, head_dim)
    scores = (
        jnp.einsum("qhd,khd->hqk", query_heads, key_heads, preferred_element_type=jnp.float32)
        / jnp.sqrt(jnp.float32(head_dim))
        + bias_block
    )
    attn = jax.nn.softmax(scores, axis=-1).astype(jnp.bfloat16)
    context = (
        jnp.einsum("hqk,khd->qhd", attn, value_heads, preferred_element_type=jnp.float32)
        .reshape(local_count, channels)
        .astype(jnp.bfloat16)
    )
    lifted = jnp.dot(context, w_out, preferred_element_type=jnp.float32).reshape(
        region_side, 1, region_side, 1, channels
    )
    spread = jnp.broadcast_to(lifted, (region_side, 8, region_side, 8, channels)).reshape(
        tile_rows, tile_cols, channels
    )
    return (block_out.astype(jnp.float32) + spread).astype(jnp.bfloat16)


def solution(mesh):
    return jax.shard_map(
        shards,
        mesh=mesh,
        in_specs=(
            P("row", "col", None),
            P(),
            P(),
            P(),
            P(),
            P(),
            P(),
            P(),
            P(),
            P(),
            P(),
            P(),
            P(),
            P(),
        ),
        out_specs=P("row", "col", None),
        check_vma=False,
    )
```

```python
import jax
import jax.numpy as jnp
from jax import lax
from jax.sharding import PartitionSpec as P
from jax.experimental import pallas as pl
from jax.experimental.pallas import tpu as pltpu

HEADS = 8


def shifted(piece, axis):
    devices = lax.axis_size(axis)
    up = [(i, i + 1) for i in range(devices - 1)]
    down = [(i + 1, i) for i in range(devices - 1)]
    return lax.ppermute(piece, axis, up), lax.ppermute(piece, axis, down)


def halo_pieces(features, width):
    rows, cols = features.shape[:2]
    top, _ = shifted(features[rows - width :], "row")
    _, bottom = shifted(features[:width], "row")
    last_cols = jnp.concatenate(
        [top[:, cols - width :], features[:, cols - width :], bottom[:, cols - width :]], axis=0
    )
    first_cols = jnp.concatenate([top[:, :width], features[:, :width], bottom[:, :width]], axis=0)
    left, _ = shifted(last_cols, "col")
    _, right = shifted(first_cols, "col")
    return top, bottom, left, right

TAPS = 7
ROW_BLOCK = 8


def conv_norm_kernel(
    c_ref, t_ref, b_ref, l_ref, r_ref, k_ref, db_ref, g_ref, nb_ref, o_ref, kf_ref, sh_ref
):
    tile_rows, tile_cols, channels = o_ref.shape
    halo = t_ref.shape[0]
    rows_p = tile_rows + 2 * halo
    for a in range(TAPS):
        kf_ref[a, pl.ds(0, TAPS), :] = k_ref[a].astype(jnp.float32)

    def put(r, mid):
        row = jnp.concatenate([l_ref[r], mid, r_ref[r]], axis=0).astype(jnp.float32)
        for b in range(TAPS):
            sh_ref[b, r] = row[b : b + tile_cols]

    for r in range(halo):
        put(r, t_ref[r])
        put(rows_p - halo + r, b_ref[r])

    def widen(r, carry):
        put(r, c_ref[r - halo])
        return carry

    lax.fori_loop(halo, rows_p - halo, widen, 0)
    db = db_ref[...]
    g = g_ref[...]
    nb = nb_ref[...]
    lanes = 128
    halves = channels // lanes

    def body(i, carry):
        r0 = pl.multiple_of(i * ROW_BLOCK, ROW_BLOCK)
        for s0 in range(0, tile_cols, 8):
            parts = []
            for h in range(halves):
                lane = pl.ds(h * lanes, lanes)
                acc = jnp.zeros((ROW_BLOCK, 8, lanes), jnp.float32)
                for b in range(TAPS):
                    x = sh_ref[b, pl.ds(r0, ROW_BLOCK + TAPS - 1), pl.ds(s0, 8), lane]
                    for a in range(TAPS):
                        acc = acc + x[a : a + ROW_BLOCK] * kf_ref[a, pl.ds(b, 1), lane]
                parts.append(acc)
            acc = jnp.concatenate(parts, axis=-1) + db
            mean = jnp.mean(acc, axis=-1, keepdims=True)
            cen = acc - mean
            var = jnp.mean(cen * cen, axis=-1, keepdims=True)
            normed = cen * lax.rsqrt(var + 1e-06) * g + nb
            o_ref[pl.ds(r0, ROW_BLOCK), pl.ds(s0, 8), :] = normed.astype(o_ref.dtype)
        return carry

    lax.fori_loop(0, tile_rows // ROW_BLOCK, body, 0)

ERFC_COEFFS = (
    -1.26551223,
    1.00002368,
    0.37409196,
    0.09678418,
    -0.18628806,
    0.27886807,
    -1.13520398,
    1.48851587,
    -0.82215223,
    0.17087277,
)
PIXEL_BLOCK = 256
HIDDEN_BLOCK = 256


def gelu_exact(pre):
    z = jnp.abs(pre) * jnp.float32(0.7071067811865476)
    t = 1.0 / (1.0 + 0.5 * z)
    poly = jnp.float32(ERFC_COEFFS[-1])
    for coeff in ERFC_COEFFS[-2::-1]:
        poly = poly * t + jnp.float32(coeff)
    tail = t * jnp.exp(poly - z * z)
    one_plus_erf = jnp.where(pre >= 0, 2.0 - tail, tail)
    return 0.5 * pre * one_plus_erf


def mlp_block(normed, features, we_ref, be_ref, wr_ref, br_ref, ls_ref, out_dtype):
    hidden_total = we_ref.shape[1]
    acc = jnp.zeros(features.shape, jnp.float32)
    for h0 in range(0, hidden_total, HIDDEN_BLOCK):
        pre = (
            jnp.dot(normed, we_ref[:, h0 : h0 + HIDDEN_BLOCK], preferred_element_type=jnp.float32)
            + be_ref[:, h0 : h0 + HIDDEN_BLOCK]
        )
        hidden = gelu_exact(pre).astype(jnp.bfloat16)
        acc = acc + jnp.dot(hidden, wr_ref[h0 : h0 + HIDDEN_BLOCK, :], preferred_element_type=jnp.float32)
    reduced = acc + br_ref[...]
    return (features.astype(jnp.float32) + ls_ref[...] * reduced).astype(out_dtype)


def region_tokens(out, wq_ref, copies):
    pixels, channels = out.shape
    tile_cols = pixels // 8
    per_row = tile_cols // 8
    column_sums = out.astype(jnp.float32).reshape(8, tile_cols, channels).sum(axis=0)
    region_sums = column_sums.reshape(per_row, 8, channels).sum(axis=1)
    pooled = (region_sums * jnp.float32(1.0 / 64.0)).astype(jnp.bfloat16)
    queries = jnp.dot(pooled, wq_ref[...], preferred_element_type=jnp.float32)
    queries = queries.astype(jnp.bfloat16).astype(jnp.float32)
    return queries, jnp.broadcast_to(pooled[None], (copies, per_row, channels))


def block_kernel(
    c_ref, t_ref, b_ref, l_ref, r_ref, k_ref, db_ref, g_ref, nb_ref, f_ref, we_hbm, be_ref, wr_hbm,
    br_ref, ls_ref, wq_hbm, o_ref, q_ref, s_ref, kf_ref, sh_ref, n_ref, we_ref, wr_ref, wq_ref, sem,
):
    loads = [
        pltpu.make_async_copy(source, target, sem.at[i])
        for i, (source, target) in enumerate(((we_hbm, we_ref), (wr_hbm, wr_ref), (wq_hbm, wq_ref)))
    ]
    for load in loads:
        load.start()
    conv_norm_kernel(c_ref, t_ref, b_ref, l_ref, r_ref, k_ref, db_ref, g_ref, nb_ref, n_ref, kf_ref, sh_ref)
    for load in loads:
        load.wait()
    tile_rows, tile_cols, channels = n_ref.shape
    per_row = tile_cols // 8
    block = 8 * tile_cols
    for step in range(tile_rows // 8):
        rows = pl.ds(step * block, block)
        normed = n_ref[pl.ds(step * 8, 8)].reshape(block, channels)
        out = mlp_block(normed, f_ref[rows], we_ref, be_ref, wr_ref, br_ref, ls_ref, o_ref.dtype)
        o_ref[rows] = out
        queries, copies = region_tokens(out, wq_ref, s_ref.shape[0])
        q_ref[pl.ds(step * per_row, per_row), :] = queries
        s_ref[:, pl.ds(step * per_row, per_row), :] = copies


def block_call(
    pieces, features, dw_kernel, dw_bias, norm_gain, norm_bias, w_expand, b_expand, w_reduce,
    b_reduce, layer_scale, w_query, copies,
):
    tile_rows, tile_cols, channels = features.shape
    rows_p = tile_rows + 2 * pieces[0].shape[0]
    cols_p = tile_cols + 2 * pieces[0].shape[0]
    pixels = tile_rows * tile_cols
    hidden_total = w_expand.shape[1]
    tokens = pixels // 64
    vmem = pl.BlockSpec(memory_space=pltpu.VMEM)
    anywhere = pl.BlockSpec(memory_space=pl.ANY)
    return pl.pallas_call(
        block_kernel,
        out_shape=(
            jax.ShapeDtypeStruct((pixels, channels), jnp.bfloat16),
            jax.ShapeDtypeStruct((tokens, channels), jnp.float32),
            jax.ShapeDtypeStruct((copies, tokens, channels), jnp.bfloat16),
        ),
        in_specs=[vmem] * 10 + [anywhere, vmem, anywhere, vmem, vmem, anywhere],
        out_specs=(vmem, vmem, vmem),
        scratch_shapes=[
            pltpu.VMEM((TAPS, 8, channels), jnp.float32),
            pltpu.VMEM((TAPS, rows_p, tile_cols, channels), jnp.float32),
            pltpu.VMEM((tile_rows, tile_cols, channels), jnp.bfloat16),
            pltpu.VMEM((channels, hidden_total), jnp.bfloat16),
            pltpu.VMEM((hidden_total, channels), jnp.bfloat16),
            pltpu.VMEM((channels, channels), jnp.bfloat16),
            pltpu.SemaphoreType.DMA((3,)),
        ],
        cost_estimate=pl.CostEstimate(
            flops=2 * TAPS * TAPS * pixels * channels + 4 * pixels * channels * hidden_total,
            bytes_accessed=2 * (rows_p * cols_p * channels + 2 * pixels * channels + 2 * channels * hidden_total),
            transcendentals=2 * pixels * hidden_total,
        ),
    )(
        features,
        *pieces,
        dw_kernel,
        dw_bias.reshape(1, channels),
        norm_gain.reshape(1, channels),
        norm_bias.reshape(1, channels),
        features.reshape(pixels, channels),
        w_expand,
        b_expand.reshape(1, hidden_total),
        w_reduce,
        b_reduce.reshape(1, channels),
        layer_scale.reshape(1, channels),
        w_query,
    )

def block_pass(
    pieces,
    features,
    dw_kernel,
    dw_bias,
    norm_gain,
    norm_bias,
    w_expand,
    b_expand,
    w_reduce,
    b_reduce,
    layer_scale,
    w_query,
    copies,
):
    tile_rows, tile_cols, channels = features.shape
    summed, queries, sent = block_call(
        pieces,
        features,
        dw_kernel,
        dw_bias,
        norm_gain,
        norm_bias,
        w_expand,
        b_expand,
        w_reduce,
        b_reduce,
        layer_scale,
        w_query,
        copies,
    )
    return summed.reshape(tile_rows, tile_cols, channels), queries, sent


def shards(
    features,
    dw_kernel,
    dw_bias,
    norm_gain,
    norm_bias,
    w_expand,
    b_expand,
    w_reduce,
    b_reduce,
    layer_scale,
    w_query,
    w_keyval,
    rel_bias,
    w_out,
):
    tile_rows, tile_cols, channels = features.shape
    head_dim = channels // HEADS
    pieces = halo_pieces(features, 3)
    columns = lax.axis_size("col")
    position = lax.axis_index("col")
    block_out, queries, sent = block_pass(
        pieces,
        features,
        dw_kernel,
        dw_bias,
        norm_gain,
        norm_bias,
        w_expand,
        b_expand,
        w_reduce,
        b_reduce,
        layer_scale,
        w_query,
        columns,
    )
    region_side = tile_rows // 8
    local_count = region_side * region_side
    queries = queries.astype(jnp.bfloat16)
    span_cols = region_side * columns
    key_count = local_count * columns
    band_pooled = lax.all_to_all(sent, "col", 0, 0)
    band_pooled = (
        band_pooled.reshape(columns, region_side, region_side, channels)
        .transpose(1, 0, 2, 3)
        .reshape(key_count, channels)
    )
    band_keyval = jnp.dot(band_pooled, w_keyval, preferred_element_type=jnp.float32).astype(
        jnp.bfloat16
    )
    windows = []
    for query_col in range(region_side):
        first = span_cols - 1 - (position * region_side + query_col)
        windows.append(lax.dynamic_slice_in_dim(rel_bias, first, span_cols, axis=2))
    rows_of = []
    for query_row in range(region_side):
        per_col = [
            w[:, region_side - 1 - query_row : 2 * region_side - 1 - query_row, :] for w in windows
        ]
        rows_of.append(jnp.stack(per_col, axis=1))
    bias_block = jnp.stack(rows_of, axis=1).reshape(HEADS, local_count, key_count)
    query_heads = queries.reshape(local_count, HEADS, head_dim)
    key_heads = band_keyval[:, :channels].reshape(key_count, HEADS, head_dim)
    value_heads = band_keyval[:, channels:].reshape(key_count, HEADS, head_dim)
    scores = (
        jnp.einsum("qhd,khd->hqk", query_heads, key_heads, preferred_element_type=jnp.float32)
        / jnp.sqrt(jnp.float32(head_dim))
        + bias_block
    )
    attn = jax.nn.softmax(scores, axis=-1).astype(jnp.bfloat16)
    context = (
        jnp.einsum("hqk,khd->qhd", attn, value_heads, preferred_element_type=jnp.float32)
        .reshape(local_count, channels)
        .astype(jnp.bfloat16)
    )
    lifted = jnp.dot(context, w_out, preferred_element_type=jnp.float32).reshape(
        region_side, 1, region_side, 1, channels
    )
    spread = jnp.broadcast_to(lifted, (region_side, 8, region_side, 8, channels)).reshape(
        tile_rows, tile_cols, channels
    )
    return (block_out.astype(jnp.float32) + spread).astype(jnp.bfloat16)


def solution(mesh):
    return jax.shard_map(
        shards,
        mesh=mesh,
        in_specs=(
            P("row", "col", None),
            P(),
            P(),
            P(),
            P(),
            P(),
            P(),
            P(),
            P(),
            P(),
            P(),
            P(),
            P(),
            P(),
        ),
        out_specs=P("row", "col", None),
        check_vma=False,
    )
```

```python
import jax
import jax.numpy as jnp
from jax import lax
from jax.sharding import PartitionSpec as P
from jax.experimental import pallas as pl
from jax.experimental.pallas import tpu as pltpu

HEADS = 8


def shifted(piece, axis):
    devices = lax.axis_size(axis)
    up = [(i, i + 1) for i in range(devices - 1)]
    down = [(i + 1, i) for i in range(devices - 1)]
    return lax.ppermute(piece, axis, up), lax.ppermute(piece, axis, down)


def halo_pieces(features, width):
    rows, cols = features.shape[:2]
    top, _ = shifted(features[rows - width :], "row")
    _, bottom = shifted(features[:width], "row")
    last_cols = jnp.concatenate(
        [top[:, cols - width :], features[:, cols - width :], bottom[:, cols - width :]], axis=0
    )
    first_cols = jnp.concatenate([top[:, :width], features[:, :width], bottom[:, :width]], axis=0)
    left, _ = shifted(last_cols, "col")
    _, right = shifted(first_cols, "col")
    return top, bottom, left, right

TAPS = 7
ROW_BLOCK = 8


def conv_norm_kernel(x_ref, k_ref, db_ref, g_ref, nb_ref, o_ref, kf_ref, sh_ref):
    rows_p = x_ref.shape[0]
    tile_rows, tile_cols, channels = o_ref.shape
    for a in range(TAPS):
        kf_ref[a, pl.ds(0, TAPS), :] = k_ref[a].astype(jnp.float32)

    def widen(r, carry):
        row = x_ref[r].astype(jnp.float32)
        for b in range(TAPS):
            sh_ref[b, r] = row[b : b + tile_cols]
        return carry

    lax.fori_loop(0, rows_p, widen, 0)
    db = db_ref[...]
    g = g_ref[...]
    nb = nb_ref[...]
    lanes = 128
    halves = channels // lanes

    def body(i, carry):
        r0 = pl.multiple_of(i * ROW_BLOCK, ROW_BLOCK)
        for s0 in range(0, tile_cols, 8):
            parts = []
            for h in range(halves):
                lane = pl.ds(h * lanes, lanes)
                acc = jnp.zeros((ROW_BLOCK, 8, lanes), jnp.float32)
                for b in range(TAPS):
                    x = sh_ref[b, pl.ds(r0, ROW_BLOCK + TAPS - 1), pl.ds(s0, 8), lane]
                    for a in range(TAPS):
                        acc = acc + x[a : a + ROW_BLOCK] * kf_ref[a, pl.ds(b, 1), lane]
                parts.append(acc)
            acc = jnp.concatenate(parts, axis=-1) + db
            mean = jnp.mean(acc, axis=-1, keepdims=True)
            cen = acc - mean
            var = jnp.mean(cen * cen, axis=-1, keepdims=True)
            normed = cen * lax.rsqrt(var + 1e-06) * g + nb
            o_ref[pl.ds(r0, ROW_BLOCK), pl.ds(s0, 8), :] = normed.astype(o_ref.dtype)
        return carry

    lax.fori_loop(0, tile_rows // ROW_BLOCK, body, 0)

ERFC_COEFFS = (
    -1.26551223,
    1.00002368,
    0.37409196,
    0.09678418,
    -0.18628806,
    0.27886807,
    -1.13520398,
    1.48851587,
    -0.82215223,
    0.17087277,
)
PIXEL_BLOCK = 256
HIDDEN_BLOCK = 256


LOG2E = 1.4426950408889634


def gelu_exact(pre):
    t = 1.0 / (1.0 + jnp.abs(pre) * jnp.float32(0.5 * 0.7071067811865476))
    poly = jnp.float32(ERFC_COEFFS[-1] * LOG2E)
    for coeff in ERFC_COEFFS[-2:0:-1]:
        poly = poly * t + jnp.float32(coeff * LOG2E)
    poly = poly * t + jnp.float32(ERFC_COEFFS[0] * LOG2E - 1.0)
    half_tail = t * jnp.exp2(poly - (pre * pre) * jnp.float32(0.5 * LOG2E))
    return pre * jnp.where(pre >= 0, 1.0 - half_tail, half_tail)


def mlp_block(normed, features, we_ref, be_ref, wr_ref, br_ref, ls_ref, out_dtype):
    hidden_total = we_ref.shape[1]
    acc = jnp.zeros(features.shape, jnp.float32)
    for h0 in range(0, hidden_total, HIDDEN_BLOCK):
        pre = (
            jnp.dot(normed, we_ref[:, h0 : h0 + HIDDEN_BLOCK], preferred_element_type=jnp.float32)
            + be_ref[:, h0 : h0 + HIDDEN_BLOCK]
        )
        hidden = gelu_exact(pre).astype(jnp.bfloat16)
        acc = acc + jnp.dot(hidden, wr_ref[h0 : h0 + HIDDEN_BLOCK, :], preferred_element_type=jnp.float32)
    reduced = acc + br_ref[...]
    return (features.astype(jnp.float32) + ls_ref[...] * reduced).astype(out_dtype)


def region_tokens(out, wq_ref, copies):
    pixels, channels = out.shape
    tile_cols = pixels // 8
    per_row = tile_cols // 8
    column_sums = out.astype(jnp.float32).reshape(8, tile_cols, channels).sum(axis=0)
    region_sums = column_sums.reshape(per_row, 8, channels).sum(axis=1)
    pooled = (region_sums * jnp.float32(1.0 / 64.0)).astype(jnp.bfloat16)
    queries = jnp.dot(pooled, wq_ref[...], preferred_element_type=jnp.float32)
    queries = queries.astype(jnp.bfloat16).astype(jnp.float32)
    return queries, jnp.broadcast_to(pooled[None], (copies, per_row, channels))


def block_kernel(
    x_ref, k_ref, db_ref, g_ref, nb_ref, f_ref, we_hbm, be_ref, wr_hbm, br_ref, ls_ref, wq_hbm,
    o_ref, q_ref, s_ref, kf_ref, sh_ref, n_ref, we_ref, wr_ref, wq_ref, sem,
):
    loads = [
        pltpu.make_async_copy(source, target, sem.at[i])
        for i, (source, target) in enumerate(((we_hbm, we_ref), (wr_hbm, wr_ref), (wq_hbm, wq_ref)))
    ]
    for load in loads:
        load.start()
    conv_norm_kernel(x_ref, k_ref, db_ref, g_ref, nb_ref, n_ref, kf_ref, sh_ref)
    for load in loads:
        load.wait()
    tile_rows, tile_cols, channels = n_ref.shape
    per_row = tile_cols // 8
    block = 8 * tile_cols
    for step in range(tile_rows // 8):
        rows = pl.ds(step * block, block)
        normed = n_ref[pl.ds(step * 8, 8)].reshape(block, channels)
        out = mlp_block(normed, f_ref[rows], we_ref, be_ref, wr_ref, br_ref, ls_ref, o_ref.dtype)
        o_ref[rows] = out
        queries, copies = region_tokens(out, wq_ref, s_ref.shape[0])
        q_ref[pl.ds(step * per_row, per_row), :] = queries
        s_ref[:, pl.ds(step * per_row, per_row), :] = copies


def block_call(
    padded, features, dw_kernel, dw_bias, norm_gain, norm_bias, w_expand, b_expand, w_reduce,
    b_reduce, layer_scale, w_query, copies,
):
    rows_p, cols_p, channels = padded.shape
    tile_rows, tile_cols = features.shape[:2]
    pixels = tile_rows * tile_cols
    hidden_total = w_expand.shape[1]
    tokens = pixels // 64
    vmem = pl.BlockSpec(memory_space=pltpu.VMEM)
    anywhere = pl.BlockSpec(memory_space=pl.ANY)
    return pl.pallas_call(
        block_kernel,
        out_shape=(
            jax.ShapeDtypeStruct((pixels, channels), jnp.bfloat16),
            jax.ShapeDtypeStruct((tokens, channels), jnp.float32),
            jax.ShapeDtypeStruct((copies, tokens, channels), jnp.bfloat16),
        ),
        in_specs=[vmem] * 6 + [anywhere, vmem, anywhere, vmem, vmem, anywhere],
        out_specs=(vmem, vmem, vmem),
        scratch_shapes=[
            pltpu.VMEM((TAPS, 8, channels), jnp.float32),
            pltpu.VMEM((TAPS, rows_p, tile_cols, channels), jnp.float32),
            pltpu.VMEM((tile_rows, tile_cols, channels), jnp.bfloat16),
            pltpu.VMEM((channels, hidden_total), jnp.bfloat16),
            pltpu.VMEM((hidden_total, channels), jnp.bfloat16),
            pltpu.VMEM((channels, channels), jnp.bfloat16),
            pltpu.SemaphoreType.DMA((3,)),
        ],
        cost_estimate=pl.CostEstimate(
            flops=2 * TAPS * TAPS * pixels * channels + 4 * pixels * channels * hidden_total,
            bytes_accessed=2 * (rows_p * cols_p * channels + 2 * pixels * channels + 2 * channels * hidden_total),
            transcendentals=2 * pixels * hidden_total,
        ),
    )(
        padded,
        dw_kernel,
        dw_bias.reshape(1, channels),
        norm_gain.reshape(1, channels),
        norm_bias.reshape(1, channels),
        features.reshape(pixels, channels),
        w_expand,
        b_expand.reshape(1, hidden_total),
        w_reduce,
        b_reduce.reshape(1, channels),
        layer_scale.reshape(1, channels),
        w_query,
    )

def block_pass(
    pieces,
    features,
    dw_kernel,
    dw_bias,
    norm_gain,
    norm_bias,
    w_expand,
    b_expand,
    w_reduce,
    b_reduce,
    layer_scale,
    w_query,
    copies,
):
    tile_rows, tile_cols, channels = features.shape
    top, bottom, left, right = pieces
    extended = jnp.concatenate([top, features, bottom], axis=0)
    padded = jnp.concatenate(
        [left, extended, right, jnp.zeros_like(right)[:, : -(tile_cols + 3 * 3) % 8]], axis=1
    )
    summed, queries, sent = block_call(
        padded,
        features,
        dw_kernel,
        dw_bias,
        norm_gain,
        norm_bias,
        w_expand,
        b_expand,
        w_reduce,
        b_reduce,
        layer_scale,
        w_query,
        copies,
    )
    return summed.reshape(tile_rows, tile_cols, channels), queries, sent


def shards(
    features,
    dw_kernel,
    dw_bias,
    norm_gain,
    norm_bias,
    w_expand,
    b_expand,
    w_reduce,
    b_reduce,
    layer_scale,
    w_query,
    w_keyval,
    rel_bias,
    w_out,
):
    tile_rows, tile_cols, channels = features.shape
    head_dim = channels // HEADS
    pieces = halo_pieces(features, 3)
    columns = lax.axis_size("col")
    position = lax.axis_index("col")
    block_out, queries, sent = block_pass(
        pieces,
        features,
        dw_kernel,
        dw_bias,
        norm_gain,
        norm_bias,
        w_expand,
        b_expand,
        w_reduce,
        b_reduce,
        layer_scale,
        w_query,
        columns,
    )
    region_side = tile_rows // 8
    local_count = region_side * region_side
    queries = queries.astype(jnp.bfloat16)
    span_cols = region_side * columns
    key_count = local_count * columns
    band_pooled = lax.all_to_all(sent, "col", 0, 0)
    band_pooled = (
        band_pooled.reshape(columns, region_side, region_side, channels)
        .transpose(1, 0, 2, 3)
        .reshape(key_count, channels)
    )
    band_keyval = jnp.dot(band_pooled, w_keyval, preferred_element_type=jnp.float32).astype(
        jnp.bfloat16
    )
    windows = []
    for query_col in range(region_side):
        first = span_cols - 1 - (position * region_side + query_col)
        windows.append(lax.dynamic_slice_in_dim(rel_bias, first, span_cols, axis=2))
    rows_of = []
    for query_row in range(region_side):
        per_col = [
            w[:, region_side - 1 - query_row : 2 * region_side - 1 - query_row, :] for w in windows
        ]
        rows_of.append(jnp.stack(per_col, axis=1))
    bias_block = jnp.stack(rows_of, axis=1).reshape(HEADS, local_count, key_count)
    query_heads = queries.reshape(local_count, HEADS, head_dim)
    key_heads = band_keyval[:, :channels].reshape(key_count, HEADS, head_dim)
    value_heads = band_keyval[:, channels:].reshape(key_count, HEADS, head_dim)
    scores = (
        jnp.einsum("qhd,khd->hqk", query_heads, key_heads, preferred_element_type=jnp.float32)
        / jnp.sqrt(jnp.float32(head_dim))
        + bias_block
    )
    attn = jax.nn.softmax(scores, axis=-1).astype(jnp.bfloat16)
    context = (
        jnp.einsum("hqk,khd->qhd", attn, value_heads, preferred_element_type=jnp.float32)
        .reshape(local_count, channels)
        .astype(jnp.bfloat16)
    )
    lifted = jnp.dot(context, w_out, preferred_element_type=jnp.float32).reshape(
        region_side, 1, region_side, 1, channels
    )
    spread = jnp.broadcast_to(lifted, (region_side, 8, region_side, 8, channels)).reshape(
        tile_rows, tile_cols, channels
    )
    return (block_out.astype(jnp.float32) + spread).astype(jnp.bfloat16)


def solution(mesh):
    return jax.shard_map(
        shards,
        mesh=mesh,
        in_specs=(
            P("row", "col", None),
            P(),
            P(),
            P(),
            P(),
            P(),
            P(),
            P(),
            P(),
            P(),
            P(),
            P(),
            P(),
            P(),
        ),
        out_specs=P("row", "col", None),
        check_vma=False,
    )
```

```python
import jax
import jax.numpy as jnp
from jax import lax
from jax.sharding import PartitionSpec as P
from jax.experimental import pallas as pl
from jax.experimental.pallas import tpu as pltpu

HEADS = 8


def shifted(piece, axis):
    devices = lax.axis_size(axis)
    up = [(i, i + 1) for i in range(devices - 1)]
    down = [(i + 1, i) for i in range(devices - 1)]
    return lax.ppermute(piece, axis, up), lax.ppermute(piece, axis, down)


def halo_pieces(features, width):
    rows, cols = features.shape[:2]
    top, _ = shifted(features[rows - width :], "row")
    _, bottom = shifted(features[:width], "row")
    last_cols = jnp.concatenate(
        [top[:, cols - width :], features[:, cols - width :], bottom[:, cols - width :]], axis=0
    )
    first_cols = jnp.concatenate([top[:, :width], features[:, :width], bottom[:, :width]], axis=0)
    left, _ = shifted(last_cols, "col")
    _, right = shifted(first_cols, "col")
    return top, bottom, left, right

TAPS = 7
ROW_BLOCK = 8


def conv_norm_kernel(x_ref, k_ref, db_ref, g_ref, nb_ref, o_ref, kf_ref, sh_ref):
    rows_p = x_ref.shape[0]
    tile_rows, tile_cols, channels = o_ref.shape
    for a in range(TAPS):
        kf_ref[a, pl.ds(0, TAPS), :] = k_ref[a].astype(jnp.float32)

    def widen(r, carry):
        row = x_ref[r].astype(jnp.float32)
        for b in range(TAPS):
            sh_ref[b, r] = row[b : b + tile_cols]
        return carry

    lax.fori_loop(0, rows_p, widen, 0)
    db = db_ref[...]
    g = g_ref[...]
    nb = nb_ref[...]
    lanes = 128
    halves = channels // lanes

    def body(i, carry):
        r0 = pl.multiple_of(i * ROW_BLOCK, ROW_BLOCK)
        for s0 in range(0, tile_cols, 8):
            parts = []
            for h in range(halves):
                lane = pl.ds(h * lanes, lanes)
                acc = jnp.zeros((ROW_BLOCK, 8, lanes), jnp.float32)
                for b in range(TAPS):
                    x = sh_ref[b, pl.ds(r0, ROW_BLOCK + TAPS - 1), pl.ds(s0, 8), lane]
                    for a in range(TAPS):
                        acc = acc + x[a : a + ROW_BLOCK] * kf_ref[a, pl.ds(b, 1), lane]
                parts.append(acc)
            acc = jnp.concatenate(parts, axis=-1) + db
            mean = jnp.mean(acc, axis=-1, keepdims=True)
            cen = acc - mean
            var = jnp.mean(cen * cen, axis=-1, keepdims=True)
            normed = cen * lax.rsqrt(var + 1e-06) * g + nb
            o_ref[pl.ds(r0, ROW_BLOCK), pl.ds(s0, 8), :] = normed.astype(o_ref.dtype)
        return carry

    lax.fori_loop(0, tile_rows // ROW_BLOCK, body, 0)

ERFC_COEFFS = (
    -1.26551223,
    1.00002368,
    0.37409196,
    0.09678418,
    -0.18628806,
    0.27886807,
    -1.13520398,
    1.48851587,
    -0.82215223,
    0.17087277,
)
PIXEL_BLOCK = 256
HIDDEN_BLOCK = 256


LOG2E = 1.4426950408889634


def gelu_exact(pre):
    t = 1.0 / (1.0 + jnp.abs(pre) * jnp.float32(0.5 * 0.7071067811865476))
    poly = jnp.float32(ERFC_COEFFS[-1] * LOG2E)
    for coeff in ERFC_COEFFS[-2:0:-1]:
        poly = poly * t + jnp.float32(coeff * LOG2E)
    poly = poly * t + jnp.float32(ERFC_COEFFS[0] * LOG2E - 1.0)
    half_tail = t * jnp.exp2(poly - (pre * pre) * jnp.float32(0.5 * LOG2E))
    return pre * jnp.where(pre >= 0, 1.0 - half_tail, half_tail)


def mlp_block(normed, features, we_ref, be_ref, wr_ref, br_ref, ls_ref, out_dtype):
    hidden_total = we_ref.shape[1]
    acc = jnp.zeros(features.shape, jnp.float32)
    for h0 in range(0, hidden_total, HIDDEN_BLOCK):
        pre = (
            jnp.dot(normed, we_ref[:, h0 : h0 + HIDDEN_BLOCK], preferred_element_type=jnp.float32)
            + be_ref[:, h0 : h0 + HIDDEN_BLOCK]
        )
        hidden = gelu_exact(pre).astype(jnp.bfloat16)
        acc = acc + jnp.dot(hidden, wr_ref[h0 : h0 + HIDDEN_BLOCK, :], preferred_element_type=jnp.float32)
    reduced = acc + br_ref[...]
    return (features.astype(jnp.float32) + ls_ref[...] * reduced).astype(out_dtype)


def region_tokens(out, wq_ref, copies):
    pixels, channels = out.shape
    tile_cols = pixels // 8
    per_row = tile_cols // 8
    column_sums = out.astype(jnp.float32).reshape(8, tile_cols, channels).sum(axis=0)
    region_sums = column_sums.reshape(per_row, 8, channels).sum(axis=1)
    pooled = (region_sums * jnp.float32(1.0 / 64.0)).astype(jnp.bfloat16)
    queries = jnp.dot(pooled, wq_ref[...], preferred_element_type=jnp.float32)
    queries = queries.astype(jnp.bfloat16).astype(jnp.float32)
    return queries, jnp.broadcast_to(pooled[None], (copies, per_row, channels))


def block_kernel(
    x_ref, k_ref, db_ref, g_ref, nb_ref, f_ref, we_hbm, be_ref, wr_hbm, br_ref, ls_ref, wq_hbm,
    o_ref, q_ref, s_ref, kf_ref, sh_ref, n_ref, we_ref, wr_ref, wq_ref, sem,
):
    loads = [
        pltpu.make_async_copy(source, target, sem.at[i])
        for i, (source, target) in enumerate(((we_hbm, we_ref), (wr_hbm, wr_ref), (wq_hbm, wq_ref)))
    ]
    for load in loads:
        load.start()
    conv_norm_kernel(x_ref, k_ref, db_ref, g_ref, nb_ref, n_ref, kf_ref, sh_ref)
    for load in loads:
        load.wait()
    tile_rows, tile_cols, channels = n_ref.shape
    per_row = tile_cols // 8
    block = 8 * tile_cols
    for step in range(tile_rows // 8):
        rows = pl.ds(step * block, block)
        normed = n_ref[pl.ds(step * 8, 8)].reshape(block, channels)
        out = mlp_block(normed, f_ref[rows], we_ref, be_ref, wr_ref, br_ref, ls_ref, o_ref.dtype)
        o_ref[rows] = out
        queries, copies = region_tokens(out, wq_ref, s_ref.shape[0])
        q_ref[pl.ds(step * per_row, per_row), :] = queries
        s_ref[:, pl.ds(step * per_row, per_row), :] = copies


def block_call(
    padded, features, dw_kernel, dw_bias, norm_gain, norm_bias, w_expand, b_expand, w_reduce,
    b_reduce, layer_scale, w_query, copies,
):
    rows_p, cols_p, channels = padded.shape
    tile_rows, tile_cols = features.shape[:2]
    pixels = tile_rows * tile_cols
    hidden_total = w_expand.shape[1]
    tokens = pixels // 64
    vmem = pl.BlockSpec(memory_space=pltpu.VMEM)
    anywhere = pl.BlockSpec(memory_space=pl.ANY)
    return pl.pallas_call(
        block_kernel,
        out_shape=(
            jax.ShapeDtypeStruct((pixels, channels), jnp.bfloat16),
            jax.ShapeDtypeStruct((tokens, channels), jnp.float32),
            jax.ShapeDtypeStruct((copies, tokens, channels), jnp.bfloat16),
        ),
        in_specs=[vmem] * 6 + [anywhere, vmem, anywhere, vmem, vmem, anywhere],
        out_specs=(vmem, vmem, vmem),
        scratch_shapes=[
            pltpu.VMEM((TAPS, 8, channels), jnp.float32),
            pltpu.VMEM((TAPS, rows_p, tile_cols, channels), jnp.float32),
            pltpu.VMEM((tile_rows, tile_cols, channels), jnp.bfloat16),
            pltpu.VMEM((channels, hidden_total), jnp.bfloat16),
            pltpu.VMEM((hidden_total, channels), jnp.bfloat16),
            pltpu.VMEM((channels, channels), jnp.bfloat16),
            pltpu.SemaphoreType.DMA((3,)),
        ],
        cost_estimate=pl.CostEstimate(
            flops=2 * TAPS * TAPS * pixels * channels + 4 * pixels * channels * hidden_total,
            bytes_accessed=2 * (rows_p * cols_p * channels + 2 * pixels * channels + 2 * channels * hidden_total),
            transcendentals=2 * pixels * hidden_total,
        ),
    )(
        padded,
        dw_kernel,
        dw_bias.reshape(1, channels),
        norm_gain.reshape(1, channels),
        norm_bias.reshape(1, channels),
        features.reshape(pixels, channels),
        w_expand,
        b_expand.reshape(1, hidden_total),
        w_reduce,
        b_reduce.reshape(1, channels),
        layer_scale.reshape(1, channels),
        w_query,
    )

def spread_kernel(bo_ref, lifted_ref, o_ref):
    tile_rows, tile_cols, channels = o_ref.shape
    per_row = tile_cols // 8
    lifted = lifted_ref[...]
    for i in range(tile_rows // 8):
        spread = jnp.broadcast_to(
            lifted[i * per_row : (i + 1) * per_row][:, None, :], (per_row, 8, channels)
        ).reshape(tile_cols, channels)
        rows = pl.ds(i * 8, 8)
        o_ref[rows] = (bo_ref[rows].astype(jnp.float32) + spread[None]).astype(o_ref.dtype)


def spread_add(block_out, lifted):
    vmem = pl.BlockSpec(memory_space=pltpu.VMEM)
    return pl.pallas_call(
        spread_kernel,
        out_shape=jax.ShapeDtypeStruct(block_out.shape, jnp.bfloat16),
        in_specs=[vmem, vmem],
        out_specs=vmem,
        cost_estimate=pl.CostEstimate(
            flops=block_out.size, bytes_accessed=4 * block_out.size, transcendentals=0
        ),
    )(block_out, lifted)


def block_pass(
    pieces,
    features,
    dw_kernel,
    dw_bias,
    norm_gain,
    norm_bias,
    w_expand,
    b_expand,
    w_reduce,
    b_reduce,
    layer_scale,
    w_query,
    copies,
):
    tile_rows, tile_cols, channels = features.shape
    top, bottom, left, right = pieces
    extended = jnp.concatenate([top, features, bottom], axis=0)
    padded = jnp.concatenate(
        [left, extended, right, jnp.zeros_like(right)[:, : -(tile_cols + 3 * 3) % 8]], axis=1
    )
    summed, queries, sent = block_call(
        padded,
        features,
        dw_kernel,
        dw_bias,
        norm_gain,
        norm_bias,
        w_expand,
        b_expand,
        w_reduce,
        b_reduce,
        layer_scale,
        w_query,
        copies,
    )
    return summed.reshape(tile_rows, tile_cols, channels), queries, sent


def shards(
    features,
    dw_kernel,
    dw_bias,
    norm_gain,
    norm_bias,
    w_expand,
    b_expand,
    w_reduce,
    b_reduce,
    layer_scale,
    w_query,
    w_keyval,
    rel_bias,
    w_out,
):
    tile_rows, tile_cols, channels = features.shape
    head_dim = channels // HEADS
    pieces = halo_pieces(features, 3)
    columns = lax.axis_size("col")
    position = lax.axis_index("col")
    block_out, queries, sent = block_pass(
        pieces,
        features,
        dw_kernel,
        dw_bias,
        norm_gain,
        norm_bias,
        w_expand,
        b_expand,
        w_reduce,
        b_reduce,
        layer_scale,
        w_query,
        columns,
    )
    region_side = tile_rows // 8
    local_count = region_side * region_side
    queries = queries.astype(jnp.bfloat16)
    span_cols = region_side * columns
    key_count = local_count * columns
    band_pooled = lax.all_to_all(sent, "col", 0, 0)
    band_pooled = (
        band_pooled.reshape(columns, region_side, region_side, channels)
        .transpose(1, 0, 2, 3)
        .reshape(key_count, channels)
    )
    band_keyval = jnp.dot(band_pooled, w_keyval, preferred_element_type=jnp.float32).astype(
        jnp.bfloat16
    )
    windows = []
    for query_col in range(region_side):
        first = span_cols - 1 - (position * region_side + query_col)
        windows.append(lax.dynamic_slice_in_dim(rel_bias, first, span_cols, axis=2))
    rows_of = []
    for query_row in range(region_side):
        per_col = [
            w[:, region_side - 1 - query_row : 2 * region_side - 1 - query_row, :] for w in windows
        ]
        rows_of.append(jnp.stack(per_col, axis=1))
    bias_block = jnp.stack(rows_of, axis=1).reshape(HEADS, local_count, key_count)
    query_heads = queries.reshape(local_count, HEADS, head_dim)
    key_heads = band_keyval[:, :channels].reshape(key_count, HEADS, head_dim)
    value_heads = band_keyval[:, channels:].reshape(key_count, HEADS, head_dim)
    scores = (
        jnp.einsum("qhd,khd->hqk", query_heads, key_heads, preferred_element_type=jnp.float32)
        / jnp.sqrt(jnp.float32(head_dim))
        + bias_block
    )
    attn = jax.nn.softmax(scores, axis=-1).astype(jnp.bfloat16)
    context = (
        jnp.einsum("hqk,khd->qhd", attn, value_heads, preferred_element_type=jnp.float32)
        .reshape(local_count, channels)
        .astype(jnp.bfloat16)
    )
    lifted = jnp.dot(context, w_out, preferred_element_type=jnp.float32)
    return spread_add(block_out, lifted)


def solution(mesh):
    return jax.shard_map(
        shards,
        mesh=mesh,
        in_specs=(
            P("row", "col", None),
            P(),
            P(),
            P(),
            P(),
            P(),
            P(),
            P(),
            P(),
            P(),
            P(),
            P(),
            P(),
            P(),
        ),
        out_specs=P("row", "col", None),
        check_vma=False,
    )
```

```python
import jax
import jax.numpy as jnp
from jax import lax
from jax.sharding import PartitionSpec as P
from jax.experimental import pallas as pl
from jax.experimental.pallas import tpu as pltpu

HEADS = 8


def shifted(piece, axis):
    devices = lax.axis_size(axis)
    up = [(i, i + 1) for i in range(devices - 1)]
    down = [(i + 1, i) for i in range(devices - 1)]
    return lax.ppermute(piece, axis, up), lax.ppermute(piece, axis, down)


def halo_pieces(features, width):
    rows, cols = features.shape[:2]
    top, _ = shifted(features[rows - width :], "row")
    _, bottom = shifted(features[:width], "row")
    last_cols = jnp.concatenate(
        [top[:, cols - width :], features[:, cols - width :], bottom[:, cols - width :]], axis=0
    )
    first_cols = jnp.concatenate([top[:, :width], features[:, :width], bottom[:, :width]], axis=0)
    left, _ = shifted(last_cols, "col")
    _, right = shifted(first_cols, "col")
    return top, bottom, left, right

TAPS = 7
ROW_BLOCK = 8


def conv_norm_kernel(x_ref, k_ref, db_ref, g_ref, nb_ref, o_ref, kf_ref, sh_ref):
    rows_p = x_ref.shape[0]
    tile_rows, tile_cols, channels = o_ref.shape
    for a in range(TAPS):
        kf_ref[a, pl.ds(0, TAPS), :] = k_ref[a].astype(jnp.float32)

    def widen(r, carry):
        row = x_ref[r].astype(jnp.float32)
        for b in range(TAPS):
            sh_ref[b, r] = row[b : b + tile_cols]
        return carry

    lax.fori_loop(0, rows_p, widen, 0)
    db = db_ref[...]
    g = g_ref[...]
    nb = nb_ref[...]
    lanes = 128
    halves = channels // lanes

    def body(i, carry):
        r0 = pl.multiple_of(i * ROW_BLOCK, ROW_BLOCK)
        for s0 in range(0, tile_cols, 8):
            parts = []
            for h in range(halves):
                lane = pl.ds(h * lanes, lanes)
                acc = jnp.zeros((ROW_BLOCK, 8, lanes), jnp.float32)
                for b in range(TAPS):
                    x = sh_ref[b, pl.ds(r0, ROW_BLOCK + TAPS - 1), pl.ds(s0, 8), lane]
                    for a in range(TAPS):
                        acc = acc + x[a : a + ROW_BLOCK] * kf_ref[a, pl.ds(b, 1), lane]
                parts.append(acc)
            acc = jnp.concatenate(parts, axis=-1) + db
            mean = jnp.mean(acc, axis=-1, keepdims=True)
            cen = acc - mean
            var = jnp.mean(cen * cen, axis=-1, keepdims=True)
            normed = cen * lax.rsqrt(var + 1e-06) * g + nb
            o_ref[pl.ds(r0, ROW_BLOCK), pl.ds(s0, 8), :] = normed.astype(o_ref.dtype)
        return carry

    lax.fori_loop(0, tile_rows // ROW_BLOCK, body, 0)

ERFC_COEFFS = (
    -1.26551223,
    1.00002368,
    0.37409196,
    0.09678418,
    -0.18628806,
    0.27886807,
    -1.13520398,
    1.48851587,
    -0.82215223,
    0.17087277,
)
PIXEL_BLOCK = 256
HIDDEN_BLOCK = 256


LOG2E = 1.4426950408889634


def gelu_exact(pre):
    t = 1.0 / (1.0 + jnp.abs(pre) * jnp.float32(0.5 * 0.7071067811865476))
    poly = jnp.float32(ERFC_COEFFS[-1] * LOG2E)
    for coeff in ERFC_COEFFS[-2:0:-1]:
        poly = poly * t + jnp.float32(coeff * LOG2E)
    poly = poly * t + jnp.float32(ERFC_COEFFS[0] * LOG2E - 1.0)
    half_tail = t * jnp.exp2(poly - (pre * pre) * jnp.float32(0.5 * LOG2E))
    return pre * jnp.where(pre >= 0, 1.0 - half_tail, half_tail)


def mlp_block(normed, features, we_ref, be_ref, wr_ref, br_ref, ls_ref, out_dtype):
    hidden_total = we_ref.shape[1]
    acc = jnp.zeros(features.shape, jnp.float32)
    for h0 in range(0, hidden_total, HIDDEN_BLOCK):
        pre = (
            jnp.dot(normed, we_ref[:, h0 : h0 + HIDDEN_BLOCK], preferred_element_type=jnp.float32)
            + be_ref[:, h0 : h0 + HIDDEN_BLOCK]
        )
        hidden = gelu_exact(pre).astype(jnp.bfloat16)
        acc = acc + jnp.dot(hidden, wr_ref[h0 : h0 + HIDDEN_BLOCK, :], preferred_element_type=jnp.float32)
    reduced = acc + br_ref[...]
    return (features.astype(jnp.float32) + ls_ref[...] * reduced).astype(out_dtype)


def region_tokens(out, wq_ref, copies):
    pixels, channels = out.shape
    tile_cols = pixels // 8
    per_row = tile_cols // 8
    column_sums = out.astype(jnp.float32).reshape(8, tile_cols, channels).sum(axis=0)
    region_sums = column_sums.reshape(per_row, 8, channels).sum(axis=1)
    pooled = (region_sums * jnp.float32(1.0 / 64.0)).astype(jnp.bfloat16)
    queries = jnp.dot(pooled, wq_ref[...], preferred_element_type=jnp.float32)
    queries = queries.astype(jnp.bfloat16).astype(jnp.float32)
    return queries, jnp.broadcast_to(pooled[None], (copies, per_row, channels))


def block_kernel(
    x_ref, k_ref, db_ref, g_ref, nb_ref, f_hbm, we_hbm, be_ref, wr_hbm, br_ref, ls_ref, wq_hbm,
    o_hbm, q_ref, s_ref, kf_ref, sh_ref, n_ref, we_ref, wr_ref, wq_ref, f_ref, o_ref, sem, out_sem,
):
    loads = [
        pltpu.make_async_copy(source, target, sem.at[i])
        for i, (source, target) in enumerate(
            ((we_hbm, we_ref), (wr_hbm, wr_ref), (wq_hbm, wq_ref), (f_hbm, f_ref))
        )
    ]
    for load in loads:
        load.start()
    conv_norm_kernel(x_ref, k_ref, db_ref, g_ref, nb_ref, n_ref, kf_ref, sh_ref)
    for load in loads:
        load.wait()
    tile_rows, tile_cols, channels = n_ref.shape
    per_row = tile_cols // 8
    block = 8 * tile_cols
    stores = []
    for step in range(tile_rows // 8):
        rows = pl.ds(step * block, block)
        normed = n_ref[pl.ds(step * 8, 8)].reshape(block, channels)
        out = mlp_block(normed, f_ref[rows], we_ref, be_ref, wr_ref, br_ref, ls_ref, o_ref.dtype)
        o_ref[rows] = out
        store = pltpu.make_async_copy(o_ref.at[rows], o_hbm.at[rows], out_sem.at[step])
        store.start()
        stores.append(store)
        queries, copies = region_tokens(out, wq_ref, s_ref.shape[0])
        q_ref[pl.ds(step * per_row, per_row), :] = queries
        s_ref[:, pl.ds(step * per_row, per_row), :] = copies
    for store in stores:
        store.wait()


def block_call(
    padded, features, dw_kernel, dw_bias, norm_gain, norm_bias, w_expand, b_expand, w_reduce,
    b_reduce, layer_scale, w_query, copies,
):
    rows_p, cols_p, channels = padded.shape
    tile_rows, tile_cols = features.shape[:2]
    pixels = tile_rows * tile_cols
    hidden_total = w_expand.shape[1]
    tokens = pixels // 64
    vmem = pl.BlockSpec(memory_space=pltpu.VMEM)
    anywhere = pl.BlockSpec(memory_space=pl.ANY)
    return pl.pallas_call(
        block_kernel,
        out_shape=(
            jax.ShapeDtypeStruct((pixels, channels), jnp.bfloat16),
            jax.ShapeDtypeStruct((tokens, channels), jnp.float32),
            jax.ShapeDtypeStruct((copies, tokens, channels), jnp.bfloat16),
        ),
        in_specs=[vmem] * 5 + [anywhere, anywhere, vmem, anywhere, vmem, vmem, anywhere],
        out_specs=(anywhere, vmem, vmem),
        scratch_shapes=[
            pltpu.VMEM((TAPS, 8, channels), jnp.float32),
            pltpu.VMEM((TAPS, rows_p, tile_cols, channels), jnp.float32),
            pltpu.VMEM((tile_rows, tile_cols, channels), jnp.bfloat16),
            pltpu.VMEM((channels, hidden_total), jnp.bfloat16),
            pltpu.VMEM((hidden_total, channels), jnp.bfloat16),
            pltpu.VMEM((channels, channels), jnp.bfloat16),
            pltpu.VMEM((pixels, channels), jnp.bfloat16),
            pltpu.VMEM((pixels, channels), jnp.bfloat16),
            pltpu.SemaphoreType.DMA((4,)),
            pltpu.SemaphoreType.DMA((tile_rows // 8,)),
        ],
        cost_estimate=pl.CostEstimate(
            flops=2 * TAPS * TAPS * pixels * channels + 4 * pixels * channels * hidden_total,
            bytes_accessed=2 * (rows_p * cols_p * channels + 2 * pixels * channels + 2 * channels * hidden_total),
            transcendentals=2 * pixels * hidden_total,
        ),
    )(
        padded,
        dw_kernel,
        dw_bias.reshape(1, channels),
        norm_gain.reshape(1, channels),
        norm_bias.reshape(1, channels),
        features.reshape(pixels, channels),
        w_expand,
        b_expand.reshape(1, hidden_total),
        w_reduce,
        b_reduce.reshape(1, channels),
        layer_scale.reshape(1, channels),
        w_query,
    )

def block_pass(
    pieces,
    features,
    dw_kernel,
    dw_bias,
    norm_gain,
    norm_bias,
    w_expand,
    b_expand,
    w_reduce,
    b_reduce,
    layer_scale,
    w_query,
    copies,
):
    tile_rows, tile_cols, channels = features.shape
    top, bottom, left, right = pieces
    extended = jnp.concatenate([top, features, bottom], axis=0)
    padded = jnp.concatenate(
        [left, extended, right, jnp.zeros_like(right)[:, : -(tile_cols + 3 * 3) % 8]], axis=1
    )
    summed, queries, sent = block_call(
        padded,
        features,
        dw_kernel,
        dw_bias,
        norm_gain,
        norm_bias,
        w_expand,
        b_expand,
        w_reduce,
        b_reduce,
        layer_scale,
        w_query,
        copies,
    )
    return summed.reshape(tile_rows, tile_cols, channels), queries, sent


def shards(
    features,
    dw_kernel,
    dw_bias,
    norm_gain,
    norm_bias,
    w_expand,
    b_expand,
    w_reduce,
    b_reduce,
    layer_scale,
    w_query,
    w_keyval,
    rel_bias,
    w_out,
):
    tile_rows, tile_cols, channels = features.shape
    head_dim = channels // HEADS
    pieces = halo_pieces(features, 3)
    columns = lax.axis_size("col")
    position = lax.axis_index("col")
    block_out, queries, sent = block_pass(
        pieces,
        features,
        dw_kernel,
        dw_bias,
        norm_gain,
        norm_bias,
        w_expand,
        b_expand,
        w_reduce,
        b_reduce,
        layer_scale,
        w_query,
        columns,
    )
    region_side = tile_rows // 8
    local_count = region_side * region_side
    queries = queries.astype(jnp.bfloat16)
    span_cols = region_side * columns
    key_count = local_count * columns
    band_pooled = lax.all_to_all(sent, "col", 0, 0)
    band_pooled = (
        band_pooled.reshape(columns, region_side, region_side, channels)
        .transpose(1, 0, 2, 3)
        .reshape(key_count, channels)
    )
    band_keyval = jnp.dot(band_pooled, w_keyval, preferred_element_type=jnp.float32).astype(
        jnp.bfloat16
    )
    windows = []
    for query_col in range(region_side):
        first = span_cols - 1 - (position * region_side + query_col)
        windows.append(lax.dynamic_slice_in_dim(rel_bias, first, span_cols, axis=2))
    rows_of = []
    for query_row in range(region_side):
        per_col = [
            w[:, region_side - 1 - query_row : 2 * region_side - 1 - query_row, :] for w in windows
        ]
        rows_of.append(jnp.stack(per_col, axis=1))
    bias_block = jnp.stack(rows_of, axis=1).reshape(HEADS, local_count, key_count)
    query_heads = queries.reshape(local_count, HEADS, head_dim)
    key_heads = band_keyval[:, :channels].reshape(key_count, HEADS, head_dim)
    value_heads = band_keyval[:, channels:].reshape(key_count, HEADS, head_dim)
    scores = (
        jnp.einsum("qhd,khd->hqk", query_heads, key_heads, preferred_element_type=jnp.float32)
        / jnp.sqrt(jnp.float32(head_dim))
        + bias_block
    )
    attn = jax.nn.softmax(scores, axis=-1).astype(jnp.bfloat16)
    context = (
        jnp.einsum("hqk,khd->qhd", attn, value_heads, preferred_element_type=jnp.float32)
        .reshape(local_count, channels)
        .astype(jnp.bfloat16)
    )
    lifted = jnp.dot(context, w_out, preferred_element_type=jnp.float32).reshape(
        region_side, 1, region_side, 1, channels
    )
    spread = jnp.broadcast_to(lifted, (region_side, 8, region_side, 8, channels)).reshape(
        tile_rows, tile_cols, channels
    )
    return (block_out.astype(jnp.float32) + spread).astype(jnp.bfloat16)


def solution(mesh):
    return jax.shard_map(
        shards,
        mesh=mesh,
        in_specs=(
            P("row", "col", None),
            P(),
            P(),
            P(),
            P(),
            P(),
            P(),
            P(),
            P(),
            P(),
            P(),
            P(),
            P(),
            P(),
        ),
        out_specs=P("row", "col", None),
        check_vma=False,
    )
```

```python
import jax
import jax.numpy as jnp
from jax import lax
from jax.sharding import PartitionSpec as P
from jax.experimental import pallas as pl
from jax.experimental.pallas import tpu as pltpu

HEADS = 8


def shifted(piece, axis):
    devices = lax.axis_size(axis)
    up = [(i, i + 1) for i in range(devices - 1)]
    down = [(i + 1, i) for i in range(devices - 1)]
    return lax.ppermute(piece, axis, up), lax.ppermute(piece, axis, down)


def halo_pieces(features, width):
    rows, cols = features.shape[:2]
    top, _ = shifted(features[rows - width :], "row")
    _, bottom = shifted(features[:width], "row")
    last_cols = jnp.concatenate(
        [top[:, cols - width :], features[:, cols - width :], bottom[:, cols - width :]], axis=0
    )
    first_cols = jnp.concatenate([top[:, :width], features[:, :width], bottom[:, :width]], axis=0)
    left, _ = shifted(last_cols, "col")
    _, right = shifted(first_cols, "col")
    return top, bottom, left, right

TAPS = 7
ROW_BLOCK = 8


def conv_norm_kernel(x_ref, k_ref, db_ref, g_ref, nb_ref, o_ref, kf_ref, sh_ref):
    rows_p = x_ref.shape[0]
    tile_rows, tile_cols, channels = o_ref.shape
    for a in range(TAPS):
        kf_ref[a, pl.ds(0, TAPS), :] = k_ref[a].astype(jnp.float32)

    def widen(r, carry):
        row = x_ref[r].astype(jnp.float32)
        for b in range(TAPS):
            sh_ref[b, r] = row[b : b + tile_cols]
        return carry

    lax.fori_loop(0, rows_p, widen, 0)
    db = db_ref[...]
    g = g_ref[...]
    nb = nb_ref[...]
    lanes = 128
    halves = channels // lanes

    def body(i, carry):
        r0 = pl.multiple_of(i * ROW_BLOCK, ROW_BLOCK)
        for s0 in range(0, tile_cols, 8):
            parts = []
            for h in range(halves):
                lane = pl.ds(h * lanes, lanes)
                acc = jnp.zeros((ROW_BLOCK, 8, lanes), jnp.float32)
                for b in range(TAPS):
                    x = sh_ref[b, pl.ds(r0, ROW_BLOCK + TAPS - 1), pl.ds(s0, 8), lane]
                    for a in range(TAPS):
                        acc = acc + x[a : a + ROW_BLOCK] * kf_ref[a, pl.ds(b, 1), lane]
                parts.append(acc)
            acc = jnp.concatenate(parts, axis=-1) + db
            mean = jnp.mean(acc, axis=-1, keepdims=True)
            cen = acc - mean
            var = jnp.mean(cen * cen, axis=-1, keepdims=True)
            normed = cen * lax.rsqrt(var + 1e-06) * g + nb
            o_ref[pl.ds(r0, ROW_BLOCK), pl.ds(s0, 8), :] = normed.astype(o_ref.dtype)
        return carry

    lax.fori_loop(0, tile_rows // ROW_BLOCK, body, 0)

ERFC_COEFFS = (
    -1.26551223,
    1.00002368,
    0.37409196,
    0.09678418,
    -0.18628806,
    0.27886807,
    -1.13520398,
    1.48851587,
    -0.82215223,
    0.17087277,
)
PIXEL_BLOCK = 256
HIDDEN_BLOCK = 256


LOG2E = 1.4426950408889634


def gelu_exact(pre):
    t = 1.0 / (1.0 + jnp.abs(pre) * jnp.float32(0.5 * 0.7071067811865476))
    poly = jnp.float32(ERFC_COEFFS[-1] * LOG2E)
    for coeff in ERFC_COEFFS[-2:0:-1]:
        poly = poly * t + jnp.float32(coeff * LOG2E)
    poly = poly * t + jnp.float32(ERFC_COEFFS[0] * LOG2E - 1.0)
    half_tail = t * jnp.exp2(poly - (pre * pre) * jnp.float32(0.5 * LOG2E))
    return pre * jnp.where(pre >= 0, 1.0 - half_tail, half_tail)


def mlp_block(normed, features, we_ref, be_ref, wr_ref, br_ref, ls_ref, out_dtype):
    hidden_total = we_ref.shape[1]
    acc = jnp.zeros(features.shape, jnp.float32)
    for h0 in range(0, hidden_total, HIDDEN_BLOCK):
        pre = (
            jnp.dot(normed, we_ref[:, h0 : h0 + HIDDEN_BLOCK], preferred_element_type=jnp.float32)
            + be_ref[:, h0 : h0 + HIDDEN_BLOCK]
        )
        hidden = gelu_exact(pre).astype(jnp.bfloat16)
        acc = acc + jnp.dot(hidden, wr_ref[h0 : h0 + HIDDEN_BLOCK, :], preferred_element_type=jnp.float32)
    reduced = acc + br_ref[...]
    return (features.astype(jnp.float32) + ls_ref[...] * reduced).astype(out_dtype)


def region_tokens(out, wq_ref, copies):
    pixels, channels = out.shape
    tile_cols = pixels // 8
    per_row = tile_cols // 8
    column_sums = out.astype(jnp.float32).reshape(8, tile_cols, channels).sum(axis=0)
    region_sums = column_sums.reshape(per_row, 8, channels).sum(axis=1)
    pooled = (region_sums * jnp.float32(1.0 / 64.0)).astype(jnp.bfloat16)
    queries = jnp.dot(pooled, wq_ref[...], preferred_element_type=jnp.float32)
    queries = queries.astype(jnp.bfloat16).astype(jnp.float32)
    return queries, jnp.broadcast_to(pooled[None], (copies, per_row, channels))


def block_kernel(
    x_ref, k_ref, db_ref, g_ref, nb_ref, f_ref, we_hbm, be_ref, wr_hbm, br_ref, ls_ref, wq_hbm,
    o_ref, q_ref, s_ref, kf_ref, sh_ref, n_ref, we_ref, wr_ref, wq_ref, sem,
):
    loads = [
        pltpu.make_async_copy(source, target, sem.at[i])
        for i, (source, target) in enumerate(((we_hbm, we_ref), (wr_hbm, wr_ref), (wq_hbm, wq_ref)))
    ]
    for load in loads:
        load.start()
    conv_norm_kernel(x_ref, k_ref, db_ref, g_ref, nb_ref, n_ref, kf_ref, sh_ref)
    for load in loads:
        load.wait()
    tile_rows, tile_cols, channels = n_ref.shape
    per_row = tile_cols // 8
    block = 8 * tile_cols
    for step in range(tile_rows // 8):
        rows = pl.ds(step * block, block)
        normed = n_ref[pl.ds(step * 8, 8)].reshape(block, channels)
        out = mlp_block(normed, f_ref[rows], we_ref, be_ref, wr_ref, br_ref, ls_ref, o_ref.dtype)
        o_ref[rows] = out
        queries, copies = region_tokens(out, wq_ref, s_ref.shape[0])
        q_ref[pl.ds(step * per_row, per_row), :] = queries
        s_ref[:, pl.ds(step * per_row, per_row), :] = copies


def block_call(
    padded, features, dw_kernel, dw_bias, norm_gain, norm_bias, w_expand, b_expand, w_reduce,
    b_reduce, layer_scale, w_query, copies,
):
    rows_p, cols_p, channels = padded.shape
    tile_rows, tile_cols = features.shape[:2]
    pixels = tile_rows * tile_cols
    hidden_total = w_expand.shape[1]
    tokens = pixels // 64
    vmem = pl.BlockSpec(memory_space=pltpu.VMEM)
    anywhere = pl.BlockSpec(memory_space=pl.ANY)
    return pl.pallas_call(
        block_kernel,
        out_shape=(
            jax.ShapeDtypeStruct((pixels, channels), jnp.bfloat16),
            jax.ShapeDtypeStruct((tokens, channels), jnp.float32),
            jax.ShapeDtypeStruct((copies, tokens, channels), jnp.bfloat16),
        ),
        in_specs=[vmem] * 6 + [anywhere, vmem, anywhere, vmem, vmem, anywhere],
        out_specs=(vmem, vmem, vmem),
        scratch_shapes=[
            pltpu.VMEM((TAPS, 8, channels), jnp.float32),
            pltpu.VMEM((TAPS, rows_p, tile_cols, channels), jnp.float32),
            pltpu.VMEM((tile_rows, tile_cols, channels), jnp.bfloat16),
            pltpu.VMEM((channels, hidden_total), jnp.bfloat16),
            pltpu.VMEM((hidden_total, channels), jnp.bfloat16),
            pltpu.VMEM((channels, channels), jnp.bfloat16),
            pltpu.SemaphoreType.DMA((3,)),
        ],
        cost_estimate=pl.CostEstimate(
            flops=2 * TAPS * TAPS * pixels * channels + 4 * pixels * channels * hidden_total,
            bytes_accessed=2 * (rows_p * cols_p * channels + 2 * pixels * channels + 2 * channels * hidden_total),
            transcendentals=2 * pixels * hidden_total,
        ),
    )(
        padded,
        dw_kernel,
        dw_bias.reshape(1, channels),
        norm_gain.reshape(1, channels),
        norm_bias.reshape(1, channels),
        features.reshape(pixels, channels),
        w_expand,
        b_expand.reshape(1, hidden_total),
        w_reduce,
        b_reduce.reshape(1, channels),
        layer_scale.reshape(1, channels),
        w_query,
    )

def block_pass(
    pieces,
    features,
    dw_kernel,
    dw_bias,
    norm_gain,
    norm_bias,
    w_expand,
    b_expand,
    w_reduce,
    b_reduce,
    layer_scale,
    w_query,
    copies,
):
    tile_rows, tile_cols, channels = features.shape
    top, bottom, left, right = pieces
    extended = jnp.concatenate([top, features, bottom], axis=0)
    padded = jnp.concatenate(
        [left, extended, right], axis=1
    )
    summed, queries, sent = block_call(
        padded,
        features,
        dw_kernel,
        dw_bias,
        norm_gain,
        norm_bias,
        w_expand,
        b_expand,
        w_reduce,
        b_reduce,
        layer_scale,
        w_query,
        copies,
    )
    return summed.reshape(tile_rows, tile_cols, channels), queries, sent


def shards(
    features,
    dw_kernel,
    dw_bias,
    norm_gain,
    norm_bias,
    w_expand,
    b_expand,
    w_reduce,
    b_reduce,
    layer_scale,
    w_query,
    w_keyval,
    rel_bias,
    w_out,
):
    tile_rows, tile_cols, channels = features.shape
    head_dim = channels // HEADS
    pieces = halo_pieces(features, 3)
    columns = lax.axis_size("col")
    position = lax.axis_index("col")
    block_out, queries, sent = block_pass(
        pieces,
        features,
        dw_kernel,
        dw_bias,
        norm_gain,
        norm_bias,
        w_expand,
        b_expand,
        w_reduce,
        b_reduce,
        layer_scale,
        w_query,
        columns,
    )
    region_side = tile_rows // 8
    local_count = region_side * region_side
    queries = queries.astype(jnp.bfloat16)
    span_cols = region_side * columns
    key_count = local_count * columns
    band_pooled = lax.all_to_all(sent, "col", 0, 0)
    band_pooled = (
        band_pooled.reshape(columns, region_side, region_side, channels)
        .transpose(1, 0, 2, 3)
        .reshape(key_count, channels)
    )
    band_keyval = jnp.dot(band_pooled, w_keyval, preferred_element_type=jnp.float32).astype(
        jnp.bfloat16
    )
    windows = []
    for query_col in range(region_side):
        first = span_cols - 1 - (position * region_side + query_col)
        windows.append(lax.dynamic_slice_in_dim(rel_bias, first, span_cols, axis=2))
    rows_of = []
    for query_row in range(region_side):
        per_col = [
            w[:, region_side - 1 - query_row : 2 * region_side - 1 - query_row, :] for w in windows
        ]
        rows_of.append(jnp.stack(per_col, axis=1))
    bias_block = jnp.stack(rows_of, axis=1).reshape(HEADS, local_count, key_count)
    query_heads = queries.reshape(local_count, HEADS, head_dim)
    key_heads = band_keyval[:, :channels].reshape(key_count, HEADS, head_dim)
    value_heads = band_keyval[:, channels:].reshape(key_count, HEADS, head_dim)
    scores = (
        jnp.einsum("qhd,khd->hqk", query_heads, key_heads, preferred_element_type=jnp.float32)
        / jnp.sqrt(jnp.float32(head_dim))
        + bias_block
    )
    attn = jax.nn.softmax(scores, axis=-1).astype(jnp.bfloat16)
    context = (
        jnp.einsum("hqk,khd->qhd", attn, value_heads, preferred_element_type=jnp.float32)
        .reshape(local_count, channels)
        .astype(jnp.bfloat16)
    )
    lifted = jnp.dot(context, w_out, preferred_element_type=jnp.float32).reshape(
        region_side, 1, region_side, 1, channels
    )
    spread = jnp.broadcast_to(lifted, (region_side, 8, region_side, 8, channels)).reshape(
        tile_rows, tile_cols, channels
    )
    return (block_out.astype(jnp.float32) + spread).astype(jnp.bfloat16)


def solution(mesh):
    return jax.shard_map(
        shards,
        mesh=mesh,
        in_specs=(
            P("row", "col", None),
            P(),
            P(),
            P(),
            P(),
            P(),
            P(),
            P(),
            P(),
            P(),
            P(),
            P(),
            P(),
            P(),
        ),
        out_specs=P("row", "col", None),
        check_vma=False,
    )
```

```python
import jax
import jax.numpy as jnp
from jax import lax
from jax.sharding import PartitionSpec as P
from jax.experimental import pallas as pl
from jax.experimental.pallas import tpu as pltpu

HEADS = 8


def shifted(piece, axis):
    devices = lax.axis_size(axis)
    up = [(i, i + 1) for i in range(devices - 1)]
    down = [(i + 1, i) for i in range(devices - 1)]
    return lax.ppermute(piece, axis, up), lax.ppermute(piece, axis, down)


def halo_pieces(features, width):
    rows, cols = features.shape[:2]
    left, _ = shifted(features[:, cols - width :], "col")
    _, right = shifted(features[:, :width], "col")
    extended = jnp.concatenate([left, features, right], axis=1)
    top, _ = shifted(extended[rows - width :], "row")
    _, bottom = shifted(extended[:width], "row")
    return extended, top, bottom

TAPS = 7
ROW_BLOCK = 8


def conv_norm_kernel(x_ref, k_ref, db_ref, g_ref, nb_ref, o_ref, kf_ref, sh_ref):
    rows_p = x_ref.shape[0]
    tile_rows, tile_cols, channels = o_ref.shape
    for a in range(TAPS):
        kf_ref[a, pl.ds(0, TAPS), :] = k_ref[a].astype(jnp.float32)

    def widen(r, carry):
        row = x_ref[r].astype(jnp.float32)
        for b in range(TAPS):
            sh_ref[b, r] = row[b : b + tile_cols]
        return carry

    lax.fori_loop(0, rows_p, widen, 0)
    db = db_ref[...]
    g = g_ref[...]
    nb = nb_ref[...]
    lanes = 128
    halves = channels // lanes

    def body(i, carry):
        r0 = pl.multiple_of(i * ROW_BLOCK, ROW_BLOCK)
        for s0 in range(0, tile_cols, 8):
            parts = []
            for h in range(halves):
                lane = pl.ds(h * lanes, lanes)
                acc = jnp.zeros((ROW_BLOCK, 8, lanes), jnp.float32)
                for b in range(TAPS):
                    x = sh_ref[b, pl.ds(r0, ROW_BLOCK + TAPS - 1), pl.ds(s0, 8), lane]
                    for a in range(TAPS):
                        acc = acc + x[a : a + ROW_BLOCK] * kf_ref[a, pl.ds(b, 1), lane]
                parts.append(acc)
            acc = jnp.concatenate(parts, axis=-1) + db
            mean = jnp.mean(acc, axis=-1, keepdims=True)
            cen = acc - mean
            var = jnp.mean(cen * cen, axis=-1, keepdims=True)
            normed = cen * lax.rsqrt(var + 1e-06) * g + nb
            o_ref[pl.ds(r0, ROW_BLOCK), pl.ds(s0, 8), :] = normed.astype(o_ref.dtype)
        return carry

    lax.fori_loop(0, tile_rows // ROW_BLOCK, body, 0)

ERFC_COEFFS = (
    -1.26551223,
    1.00002368,
    0.37409196,
    0.09678418,
    -0.18628806,
    0.27886807,
    -1.13520398,
    1.48851587,
    -0.82215223,
    0.17087277,
)
PIXEL_BLOCK = 256
HIDDEN_BLOCK = 256


LOG2E = 1.4426950408889634


def gelu_exact(pre):
    t = 1.0 / (1.0 + jnp.abs(pre) * jnp.float32(0.5 * 0.7071067811865476))
    poly = jnp.float32(ERFC_COEFFS[-1] * LOG2E)
    for coeff in ERFC_COEFFS[-2:0:-1]:
        poly = poly * t + jnp.float32(coeff * LOG2E)
    poly = poly * t + jnp.float32(ERFC_COEFFS[0] * LOG2E - 1.0)
    half_tail = t * jnp.exp2(poly - (pre * pre) * jnp.float32(0.5 * LOG2E))
    return pre * jnp.where(pre >= 0, 1.0 - half_tail, half_tail)


def mlp_block(normed, features, we_ref, be_ref, wr_ref, br_ref, ls_ref, out_dtype):
    hidden_total = we_ref.shape[1]
    acc = jnp.zeros(features.shape, jnp.float32)
    for h0 in range(0, hidden_total, HIDDEN_BLOCK):
        pre = (
            jnp.dot(normed, we_ref[:, h0 : h0 + HIDDEN_BLOCK], preferred_element_type=jnp.float32)
            + be_ref[:, h0 : h0 + HIDDEN_BLOCK]
        )
        hidden = gelu_exact(pre).astype(jnp.bfloat16)
        acc = acc + jnp.dot(hidden, wr_ref[h0 : h0 + HIDDEN_BLOCK, :], preferred_element_type=jnp.float32)
    reduced = acc + br_ref[...]
    return (features.astype(jnp.float32) + ls_ref[...] * reduced).astype(out_dtype)


def region_tokens(out, wq_ref, copies):
    pixels, channels = out.shape
    tile_cols = pixels // 8
    per_row = tile_cols // 8
    column_sums = out.astype(jnp.float32).reshape(8, tile_cols, channels).sum(axis=0)
    region_sums = column_sums.reshape(per_row, 8, channels).sum(axis=1)
    pooled = (region_sums * jnp.float32(1.0 / 64.0)).astype(jnp.bfloat16)
    queries = jnp.dot(pooled, wq_ref[...], preferred_element_type=jnp.float32)
    queries = queries.astype(jnp.bfloat16).astype(jnp.float32)
    return queries, jnp.broadcast_to(pooled[None], (copies, per_row, channels))


def block_kernel(
    x_ref, k_ref, db_ref, g_ref, nb_ref, f_ref, we_hbm, be_ref, wr_hbm, br_ref, ls_ref, wq_hbm,
    o_ref, q_ref, s_ref, kf_ref, sh_ref, n_ref, we_ref, wr_ref, wq_ref, sem,
):
    loads = [
        pltpu.make_async_copy(source, target, sem.at[i])
        for i, (source, target) in enumerate(((we_hbm, we_ref), (wr_hbm, wr_ref), (wq_hbm, wq_ref)))
    ]
    for load in loads:
        load.start()
    conv_norm_kernel(x_ref, k_ref, db_ref, g_ref, nb_ref, n_ref, kf_ref, sh_ref)
    for load in loads:
        load.wait()
    tile_rows, tile_cols, channels = n_ref.shape
    per_row = tile_cols // 8
    block = 8 * tile_cols
    for step in range(tile_rows // 8):
        rows = pl.ds(step * block, block)
        normed = n_ref[pl.ds(step * 8, 8)].reshape(block, channels)
        out = mlp_block(normed, f_ref[rows], we_ref, be_ref, wr_ref, br_ref, ls_ref, o_ref.dtype)
        o_ref[rows] = out
        queries, copies = region_tokens(out, wq_ref, s_ref.shape[0])
        q_ref[pl.ds(step * per_row, per_row), :] = queries
        s_ref[:, pl.ds(step * per_row, per_row), :] = copies


def block_call(
    padded, features, dw_kernel, dw_bias, norm_gain, norm_bias, w_expand, b_expand, w_reduce,
    b_reduce, layer_scale, w_query, copies,
):
    rows_p, cols_p, channels = padded.shape
    tile_rows, tile_cols = features.shape[:2]
    pixels = tile_rows * tile_cols
    hidden_total = w_expand.shape[1]
    tokens = pixels // 64
    vmem = pl.BlockSpec(memory_space=pltpu.VMEM)
    anywhere = pl.BlockSpec(memory_space=pl.ANY)
    return pl.pallas_call(
        block_kernel,
        out_shape=(
            jax.ShapeDtypeStruct((pixels, channels), jnp.bfloat16),
            jax.ShapeDtypeStruct((tokens, channels), jnp.float32),
            jax.ShapeDtypeStruct((copies, tokens, channels), jnp.bfloat16),
        ),
        in_specs=[vmem] * 6 + [anywhere, vmem, anywhere, vmem, vmem, anywhere],
        out_specs=(vmem, vmem, vmem),
        scratch_shapes=[
            pltpu.VMEM((TAPS, 8, channels), jnp.float32),
            pltpu.VMEM((TAPS, rows_p, tile_cols, channels), jnp.float32),
            pltpu.VMEM((tile_rows, tile_cols, channels), jnp.bfloat16),
            pltpu.VMEM((channels, hidden_total), jnp.bfloat16),
            pltpu.VMEM((hidden_total, channels), jnp.bfloat16),
            pltpu.VMEM((channels, channels), jnp.bfloat16),
            pltpu.SemaphoreType.DMA((3,)),
        ],
        cost_estimate=pl.CostEstimate(
            flops=2 * TAPS * TAPS * pixels * channels + 4 * pixels * channels * hidden_total,
            bytes_accessed=2 * (rows_p * cols_p * channels + 2 * pixels * channels + 2 * channels * hidden_total),
            transcendentals=2 * pixels * hidden_total,
        ),
    )(
        padded,
        dw_kernel,
        dw_bias.reshape(1, channels),
        norm_gain.reshape(1, channels),
        norm_bias.reshape(1, channels),
        features.reshape(pixels, channels),
        w_expand,
        b_expand.reshape(1, hidden_total),
        w_reduce,
        b_reduce.reshape(1, channels),
        layer_scale.reshape(1, channels),
        w_query,
    )

def block_pass(
    pieces,
    features,
    dw_kernel,
    dw_bias,
    norm_gain,
    norm_bias,
    w_expand,
    b_expand,
    w_reduce,
    b_reduce,
    layer_scale,
    w_query,
    copies,
):
    tile_rows, tile_cols, channels = features.shape
    extended, top, bottom = pieces
    padded = jnp.concatenate([top, extended, bottom], axis=0)
    summed, queries, sent = block_call(
        padded,
        features,
        dw_kernel,
        dw_bias,
        norm_gain,
        norm_bias,
        w_expand,
        b_expand,
        w_reduce,
        b_reduce,
        layer_scale,
        w_query,
        copies,
    )
    return summed.reshape(tile_rows, tile_cols, channels), queries, sent


def shards(
    features,
    dw_kernel,
    dw_bias,
    norm_gain,
    norm_bias,
    w_expand,
    b_expand,
    w_reduce,
    b_reduce,
    layer_scale,
    w_query,
    w_keyval,
    rel_bias,
    w_out,
):
    tile_rows, tile_cols, channels = features.shape
    head_dim = channels // HEADS
    pieces = halo_pieces(features, 3)
    columns = lax.axis_size("col")
    position = lax.axis_index("col")
    block_out, queries, sent = block_pass(
        pieces,
        features,
        dw_kernel,
        dw_bias,
        norm_gain,
        norm_bias,
        w_expand,
        b_expand,
        w_reduce,
        b_reduce,
        layer_scale,
        w_query,
        columns,
    )
    region_side = tile_rows // 8
    local_count = region_side * region_side
    queries = queries.astype(jnp.bfloat16)
    span_cols = region_side * columns
    key_count = local_count * columns
    band_pooled = lax.all_to_all(sent, "col", 0, 0)
    band_pooled = (
        band_pooled.reshape(columns, region_side, region_side, channels)
        .transpose(1, 0, 2, 3)
        .reshape(key_count, channels)
    )
    band_keyval = jnp.dot(band_pooled, w_keyval, preferred_element_type=jnp.float32).astype(
        jnp.bfloat16
    )
    windows = []
    for query_col in range(region_side):
        first = span_cols - 1 - (position * region_side + query_col)
        windows.append(lax.dynamic_slice_in_dim(rel_bias, first, span_cols, axis=2))
    rows_of = []
    for query_row in range(region_side):
        per_col = [
            w[:, region_side - 1 - query_row : 2 * region_side - 1 - query_row, :] for w in windows
        ]
        rows_of.append(jnp.stack(per_col, axis=1))
    bias_block = jnp.stack(rows_of, axis=1).reshape(HEADS, local_count, key_count)
    query_heads = queries.reshape(local_count, HEADS, head_dim)
    key_heads = band_keyval[:, :channels].reshape(key_count, HEADS, head_dim)
    value_heads = band_keyval[:, channels:].reshape(key_count, HEADS, head_dim)
    scores = (
        jnp.einsum("qhd,khd->hqk", query_heads, key_heads, preferred_element_type=jnp.float32)
        / jnp.sqrt(jnp.float32(head_dim))
        + bias_block
    )
    attn = jax.nn.softmax(scores, axis=-1).astype(jnp.bfloat16)
    context = (
        jnp.einsum("hqk,khd->qhd", attn, value_heads, preferred_element_type=jnp.float32)
        .reshape(local_count, channels)
        .astype(jnp.bfloat16)
    )
    lifted = jnp.dot(context, w_out, preferred_element_type=jnp.float32).reshape(
        region_side, 1, region_side, 1, channels
    )
    spread = jnp.broadcast_to(lifted, (region_side, 8, region_side, 8, channels)).reshape(
        tile_rows, tile_cols, channels
    )
    return (block_out.astype(jnp.float32) + spread).astype(jnp.bfloat16)


def solution(mesh):
    return jax.shard_map(
        shards,
        mesh=mesh,
        in_specs=(
            P("row", "col", None),
            P(),
            P(),
            P(),
            P(),
            P(),
            P(),
            P(),
            P(),
            P(),
            P(),
            P(),
            P(),
            P(),
        ),
        out_specs=P("row", "col", None),
        check_vma=False,
    )
```

```python
import jax
import jax.numpy as jnp
from jax import lax
from jax.sharding import PartitionSpec as P
from jax.experimental import pallas as pl
from jax.experimental.pallas import tpu as pltpu

HEADS = 8


def shifted(piece, axis):
    devices = lax.axis_size(axis)
    up = [(i, i + 1) for i in range(devices - 1)]
    down = [(i + 1, i) for i in range(devices - 1)]
    return lax.ppermute(piece, axis, up), lax.ppermute(piece, axis, down)


def halo_pieces(features, width):
    rows, cols = features.shape[:2]
    top, _ = shifted(features[rows - width :], "row")
    _, bottom = shifted(features[:width], "row")
    last_cols = jnp.concatenate(
        [top[:, cols - width :], features[:, cols - width :], bottom[:, cols - width :]], axis=0
    )
    first_cols = jnp.concatenate([top[:, :width], features[:, :width], bottom[:, :width]], axis=0)
    left, _ = shifted(last_cols, "col")
    _, right = shifted(first_cols, "col")
    return top, bottom, left, right

TAPS = 7
ROW_BLOCK = 16


def conv_norm_kernel(x_ref, k_ref, db_ref, g_ref, nb_ref, o_ref, kf_ref, sh_ref):
    rows_p = x_ref.shape[0]
    tile_rows, tile_cols, channels = o_ref.shape
    for a in range(TAPS):
        kf_ref[a, pl.ds(0, TAPS), :] = k_ref[a].astype(jnp.float32)

    def widen(r, carry):
        row = x_ref[r].astype(jnp.float32)
        for b in range(TAPS):
            sh_ref[b, r] = row[b : b + tile_cols]
        return carry

    lax.fori_loop(0, rows_p, widen, 0)
    db = db_ref[...]
    g = g_ref[...]
    nb = nb_ref[...]
    lanes = 128
    halves = channels // lanes

    def body(i, carry):
        r0 = pl.multiple_of(i * ROW_BLOCK, ROW_BLOCK)
        for s0 in range(0, tile_cols, 8):
            parts = []
            for h in range(halves):
                lane = pl.ds(h * lanes, lanes)
                acc = jnp.zeros((ROW_BLOCK, 8, lanes), jnp.float32)
                for b in range(TAPS):
                    x = sh_ref[b, pl.ds(r0, ROW_BLOCK + TAPS - 1), pl.ds(s0, 8), lane]
                    for a in range(TAPS):
                        acc = acc + x[a : a + ROW_BLOCK] * kf_ref[a, pl.ds(b, 1), lane]
                parts.append(acc)
            acc = jnp.concatenate(parts, axis=-1) + db
            mean = jnp.mean(acc, axis=-1, keepdims=True)
            cen = acc - mean
            var = jnp.mean(cen * cen, axis=-1, keepdims=True)
            normed = cen * lax.rsqrt(var + 1e-06) * g + nb
            o_ref[pl.ds(r0, ROW_BLOCK), pl.ds(s0, 8), :] = normed.astype(o_ref.dtype)
        return carry

    lax.fori_loop(0, tile_rows // ROW_BLOCK, body, 0)

ERFC_COEFFS = (
    -1.26551223,
    1.00002368,
    0.37409196,
    0.09678418,
    -0.18628806,
    0.27886807,
    -1.13520398,
    1.48851587,
    -0.82215223,
    0.17087277,
)
PIXEL_BLOCK = 256
HIDDEN_BLOCK = 256


LOG2E = 1.4426950408889634


def gelu_exact(pre):
    t = 1.0 / (1.0 + jnp.abs(pre) * jnp.float32(0.5 * 0.7071067811865476))
    poly = jnp.float32(ERFC_COEFFS[-1] * LOG2E)
    for coeff in ERFC_COEFFS[-2:0:-1]:
        poly = poly * t + jnp.float32(coeff * LOG2E)
    poly = poly * t + jnp.float32(ERFC_COEFFS[0] * LOG2E - 1.0)
    half_tail = t * jnp.exp2(poly - (pre * pre) * jnp.float32(0.5 * LOG2E))
    return pre * jnp.where(pre >= 0, 1.0 - half_tail, half_tail)


def mlp_block(normed, features, we_ref, be_ref, wr_ref, br_ref, ls_ref, out_dtype):
    hidden_total = we_ref.shape[1]
    acc = jnp.zeros(features.shape, jnp.float32)
    for h0 in range(0, hidden_total, HIDDEN_BLOCK):
        pre = (
            jnp.dot(normed, we_ref[:, h0 : h0 + HIDDEN_BLOCK], preferred_element_type=jnp.float32)
            + be_ref[:, h0 : h0 + HIDDEN_BLOCK]
        )
        hidden = gelu_exact(pre).astype(jnp.bfloat16)
        acc = acc + jnp.dot(hidden, wr_ref[h0 : h0 + HIDDEN_BLOCK, :], preferred_element_type=jnp.float32)
    reduced = acc + br_ref[...]
    return (features.astype(jnp.float32) + ls_ref[...] * reduced).astype(out_dtype)


def region_tokens(out, wq_ref, copies):
    pixels, channels = out.shape
    tile_cols = pixels // 8
    per_row = tile_cols // 8
    column_sums = out.astype(jnp.float32).reshape(8, tile_cols, channels).sum(axis=0)
    region_sums = column_sums.reshape(per_row, 8, channels).sum(axis=1)
    pooled = (region_sums * jnp.float32(1.0 / 64.0)).astype(jnp.bfloat16)
    queries = jnp.dot(pooled, wq_ref[...], preferred_element_type=jnp.float32)
    queries = queries.astype(jnp.bfloat16).astype(jnp.float32)
    return queries, jnp.broadcast_to(pooled[None], (copies, per_row, channels))


def block_kernel(
    x_ref, k_ref, db_ref, g_ref, nb_ref, f_ref, we_hbm, be_ref, wr_hbm, br_ref, ls_ref, wq_hbm,
    o_ref, q_ref, s_ref, kf_ref, sh_ref, n_ref, we_ref, wr_ref, wq_ref, sem,
):
    loads = [
        pltpu.make_async_copy(source, target, sem.at[i])
        for i, (source, target) in enumerate(((we_hbm, we_ref), (wr_hbm, wr_ref), (wq_hbm, wq_ref)))
    ]
    for load in loads:
        load.start()
    conv_norm_kernel(x_ref, k_ref, db_ref, g_ref, nb_ref, n_ref, kf_ref, sh_ref)
    for load in loads:
        load.wait()
    tile_rows, tile_cols, channels = n_ref.shape
    per_row = tile_cols // 8
    block = 8 * tile_cols
    for step in range(tile_rows // 8):
        rows = pl.ds(step * block, block)
        normed = n_ref[pl.ds(step * 8, 8)].reshape(block, channels)
        out = mlp_block(normed, f_ref[rows], we_ref, be_ref, wr_ref, br_ref, ls_ref, o_ref.dtype)
        o_ref[rows] = out
        queries, copies = region_tokens(out, wq_ref, s_ref.shape[0])
        q_ref[pl.ds(step * per_row, per_row), :] = queries
        s_ref[:, pl.ds(step * per_row, per_row), :] = copies


def block_call(
    padded, features, dw_kernel, dw_bias, norm_gain, norm_bias, w_expand, b_expand, w_reduce,
    b_reduce, layer_scale, w_query, copies,
):
    rows_p, cols_p, channels = padded.shape
    tile_rows, tile_cols = features.shape[:2]
    pixels = tile_rows * tile_cols
    hidden_total = w_expand.shape[1]
    tokens = pixels // 64
    vmem = pl.BlockSpec(memory_space=pltpu.VMEM)
    anywhere = pl.BlockSpec(memory_space=pl.ANY)
    return pl.pallas_call(
        block_kernel,
        out_shape=(
            jax.ShapeDtypeStruct((pixels, channels), jnp.bfloat16),
            jax.ShapeDtypeStruct((tokens, channels), jnp.float32),
            jax.ShapeDtypeStruct((copies, tokens, channels), jnp.bfloat16),
        ),
        in_specs=[vmem] * 6 + [anywhere, vmem, anywhere, vmem, vmem, anywhere],
        out_specs=(vmem, vmem, vmem),
        scratch_shapes=[
            pltpu.VMEM((TAPS, 8, channels), jnp.float32),
            pltpu.VMEM((TAPS, rows_p, tile_cols, channels), jnp.float32),
            pltpu.VMEM((tile_rows, tile_cols, channels), jnp.bfloat16),
            pltpu.VMEM((channels, hidden_total), jnp.bfloat16),
            pltpu.VMEM((hidden_total, channels), jnp.bfloat16),
            pltpu.VMEM((channels, channels), jnp.bfloat16),
            pltpu.SemaphoreType.DMA((3,)),
        ],
        cost_estimate=pl.CostEstimate(
            flops=2 * TAPS * TAPS * pixels * channels + 4 * pixels * channels * hidden_total,
            bytes_accessed=2 * (rows_p * cols_p * channels + 2 * pixels * channels + 2 * channels * hidden_total),
            transcendentals=2 * pixels * hidden_total,
        ),
    )(
        padded,
        dw_kernel,
        dw_bias.reshape(1, channels),
        norm_gain.reshape(1, channels),
        norm_bias.reshape(1, channels),
        features.reshape(pixels, channels),
        w_expand,
        b_expand.reshape(1, hidden_total),
        w_reduce,
        b_reduce.reshape(1, channels),
        layer_scale.reshape(1, channels),
        w_query,
    )

def block_pass(
    pieces,
    features,
    dw_kernel,
    dw_bias,
    norm_gain,
    norm_bias,
    w_expand,
    b_expand,
    w_reduce,
    b_reduce,
    layer_scale,
    w_query,
    copies,
):
    tile_rows, tile_cols, channels = features.shape
    top, bottom, left, right = pieces
    extended = jnp.concatenate([top, features, bottom], axis=0)
    padded = jnp.concatenate(
        [left, extended, right], axis=1
    )
    summed, queries, sent = block_call(
        padded,
        features,
        dw_kernel,
        dw_bias,
        norm_gain,
        norm_bias,
        w_expand,
        b_expand,
        w_reduce,
        b_reduce,
        layer_scale,
        w_query,
        copies,
    )
    return summed.reshape(tile_rows, tile_cols, channels), queries, sent


def shards(
    features,
    dw_kernel,
    dw_bias,
    norm_gain,
    norm_bias,
    w_expand,
    b_expand,
    w_reduce,
    b_reduce,
    layer_scale,
    w_query,
    w_keyval,
    rel_bias,
    w_out,
):
    tile_rows, tile_cols, channels = features.shape
    head_dim = channels // HEADS
    pieces = halo_pieces(features, 3)
    columns = lax.axis_size("col")
    position = lax.axis_index("col")
    block_out, queries, sent = block_pass(
        pieces,
        features,
        dw_kernel,
        dw_bias,
        norm_gain,
        norm_bias,
        w_expand,
        b_expand,
        w_reduce,
        b_reduce,
        layer_scale,
        w_query,
        columns,
    )
    region_side = tile_rows // 8
    local_count = region_side * region_side
    queries = queries.astype(jnp.bfloat16)
    span_cols = region_side * columns
    key_count = local_count * columns
    band_pooled = lax.all_to_all(sent, "col", 0, 0)
    band_pooled = (
        band_pooled.reshape(columns, region_side, region_side, channels)
        .transpose(1, 0, 2, 3)
        .reshape(key_count, channels)
    )
    band_keyval = jnp.dot(band_pooled, w_keyval, preferred_element_type=jnp.float32).astype(
        jnp.bfloat16
    )
    windows = []
    for query_col in range(region_side):
        first = span_cols - 1 - (position * region_side + query_col)
        windows.append(lax.dynamic_slice_in_dim(rel_bias, first, span_cols, axis=2))
    rows_of = []
    for query_row in range(region_side):
        per_col = [
            w[:, region_side - 1 - query_row : 2 * region_side - 1 - query_row, :] for w in windows
        ]
        rows_of.append(jnp.stack(per_col, axis=1))
    bias_block = jnp.stack(rows_of, axis=1).reshape(HEADS, local_count, key_count)
    query_heads = queries.reshape(local_count, HEADS, head_dim)
    key_heads = band_keyval[:, :channels].reshape(key_count, HEADS, head_dim)
    value_heads = band_keyval[:, channels:].reshape(key_count, HEADS, head_dim)
    scores = (
        jnp.einsum("qhd,khd->hqk", query_heads, key_heads, preferred_element_type=jnp.float32)
        / jnp.sqrt(jnp.float32(head_dim))
        + bias_block
    )
    attn = jax.nn.softmax(scores, axis=-1).astype(jnp.bfloat16)
    context = (
        jnp.einsum("hqk,khd->qhd", attn, value_heads, preferred_element_type=jnp.float32)
        .reshape(local_count, channels)
        .astype(jnp.bfloat16)
    )
    lifted = jnp.dot(context, w_out, preferred_element_type=jnp.float32).reshape(
        region_side, 1, region_side, 1, channels
    )
    spread = jnp.broadcast_to(lifted, (region_side, 8, region_side, 8, channels)).reshape(
        tile_rows, tile_cols, channels
    )
    return (block_out.astype(jnp.float32) + spread).astype(jnp.bfloat16)


def solution(mesh):
    return jax.shard_map(
        shards,
        mesh=mesh,
        in_specs=(
            P("row", "col", None),
            P(),
            P(),
            P(),
            P(),
            P(),
            P(),
            P(),
            P(),
            P(),
            P(),
            P(),
            P(),
            P(),
        ),
        out_specs=P("row", "col", None),
        check_vma=False,
    )
```
